32 devices in a mesh: groups: 2 (over y), pairs: 4 (over z), mp: 4 (over x, core).
Axes of the slice: x: 2, y: 2, z: 4, core: 2. Of those that a mesh axis runs over, the one named last changes fastest.
Arguments:
- tokens: bfloat16 [512, 768], P(('groups', 'pairs'), 'mp'), parts along dimension 0, may hold values from -6 to 6
- pair_list: int32 [16, 2], P(('groups', 'pairs')), parts along dimension 0, may hold values from 0 to 7, as said below
- confidence: float32 [16, 64], P(('groups', 'pairs')), parts along dimension 0, may hold values from 0.1 to 10
- gain_self: float32 [768], replicated, may hold values from 0.1 to 1.9
- gain_query: float32 [768], replicated, may hold values from 0.1 to 1.9
- gain_context: float32 [768], replicated, may hold values from 0.1 to 1.9
- gain_mlp: float32 [768], replicated, may hold values from 0.1 to 1.9
- self_qkv: bfloat16 [3, 768, 768], P(None, None, 'mp'), may hold values from -1 to 1
- self_out: bfloat16 [768, 768], P('mp'), may hold values from -0.21875 to 0.21875
- cross_query: bfloat16 [768, 768], P(None, 'mp'), may hold values from -1 to 1
- cross_kv: bfloat16 [2, 768, 768], P(None, None, 'mp'), may hold values from -1 to 1
- cross_out: bfloat16 [768, 768], P('mp'), may hold values from -0.21875 to 0.21875
- mlp_up: bfloat16 [768, 3072], P(None, 'mp'), may hold values from -0.21875 to 0.21875
- mlp_down: bfloat16 [3072, 768], P('mp'), may hold values from -0.109375 to 0.109375
Outputs:
- image_features: bfloat16 [512, 768], P(('groups', 'pairs'), 'mp'), parts along dimension 0
The draws below stay inside these ranges and needn't reach their ends.
There are 2 independent parts, one for each index of `groups`. The reference program is written for one: setup_inputs(seed, part) draws one part's arguments, and reference() takes and returns one part's arrays. A program takes and returns all parts, laid end to end along the dimension named above; an argument that names none is the same for every part. Nothing has to cross between parts.
Inputs may be any that keep to these rules, and one draw needn't show every extreme that they name: `pair_list`: in each block of 2 consecutive pairs the 4 images named are distinct and have distinct owners, the owner of image i being i // 2; the images of each owner are named in exactly 4 blocks; some images are named by no pair.
All inputs are finite; a program needn't handle non-finite values.
Results may differ from the reference program's by a relative error of at most 0.012.
Values may be sent and summed in bfloat16 or wider, within the bound.
No kernel may reach another device: no remote copies, remote signals or barrier semaphores. Data moves between devices by JAX's collectives and lax.ppermute only.
A program may use at most 64 MiB of HBM per device.

```python
import math
import jax
import jax.numpy as jnp
from jax import lax

D = 768
HEAD = 64
FF = 3072
TOKS = 32
IMG_DEV = 2
PAIR_DEV = 2
IMAGES = 8
PAIRS = 8
N_MP = 4


def draw_pair_list(key, part):
    owners_n = PAIRS // PAIR_DEV
    views_n = 2 * PAIR_DEV
    subkeys = jax.random.split(key, 5)
    shifts = jax.random.permutation(subkeys[0], owners_n)[:views_n]
    ranking = jax.random.permutation(subkeys[1], owners_n)
    marked = ranking < owners_n // 2
    seldom = jax.random.randint(subkeys[2], (owners_n,), 0, IMG_DEV)
    seldom = seldom.at[0].set(IMG_DEV - 1).at[owners_n - 1].set(0)
    special = jax.random.randint(subkeys[3], (owners_n,), 0, views_n)
    first_free = jnp.where(special == 0, 1, 0)
    offsets = jax.random.randint(subkeys[4], (owners_n,), 0, IMG_DEV - 1)
    offsets = offsets.at[0].set((0 - first_free[0]) % (IMG_DEV - 1))
    offsets = offsets.at[owners_n - 1].set((IMG_DEV - 2 - first_free[owners_n - 1]) % (IMG_DEV - 1))
    block_index = jnp.arange(owners_n)[:, None]
    position = jnp.arange(views_n)[None, :]
    owner = (block_index + shifts[None, :]) % owners_n
    cycled = (position + offsets[owner]) % (IMG_DEV - 1)
    common = (seldom[owner] + 1 + cycled) % IMG_DEV
    use_seldom = (position == special[owner]) & marked[owner]
    local = jnp.where(use_seldom, seldom[owner], common)
    picked = owner * IMG_DEV + local
    return picked.reshape(PAIRS, 2).astype(jnp.int32)


def draw_tokens(key, part):
    total_rows = IMAGES * TOKS
    subkeys = jax.random.split(key, 1)
    values = jax.random.normal(subkeys[0], (total_rows, D), jnp.float32)
    return jnp.clip(values, -6.0, 6.0).astype(jnp.bfloat16)


def draw_self_qkv(key, part):
    noise_key = jax.random.fold_in(key, 101)
    values = jnp.clip(jax.random.normal(noise_key, (3, D, D), jnp.float32), -6.0, 6.0) * D ** (-0.5)
    return values.astype(jnp.bfloat16)


def draw_cross_query(key, part):
    noise_key = jax.random.fold_in(key, 102)
    values = jnp.clip(jax.random.normal(noise_key, (D, D), jnp.float32), -6.0, 6.0) * D ** (-0.5)
    return values.astype(jnp.bfloat16)


def draw_cross_kv(key, part):
    noise_key = jax.random.fold_in(key, 103)
    values = jnp.clip(jax.random.normal(noise_key, (2, D, D), jnp.float32), -6.0, 6.0) * D ** (-0.5)
    return values.astype(jnp.bfloat16)


def block_scale(rng, shape, shards, smallest, largest):
    loudness = 1.0
    for axis_at, blocks in shards:
        heights = jax.random.uniform(jax.random.fold_in(jax.random.fold_in(rng, 6), axis_at), (blocks,), jnp.float32, smallest / len(shards), largest / len(shards))
        loudness = loudness * jnp.repeat(jnp.exp(heights), shape[axis_at] // blocks).reshape((-1,) + (1,) * (len(shape) - 1 - axis_at))
    return loudness


def bell_draw(stream_key, extent, deviation, limit, pieces=(), dtype=jnp.bfloat16):
    level = block_scale(stream_key, extent, pieces, -0.22, 0.18) if pieces else 1.0
    array = jax.random.normal(stream_key, extent, jnp.float32) * deviation * level
    return jnp.minimum(jnp.maximum(array, -limit), limit).astype(dtype)


def setup_inputs(seed: int = 0, part: int = 0) -> dict:
    splits = jax.random.split(jax.random.key(seed), 15)
    part_splits = jax.random.split(jax.random.fold_in(splits[14], part), 15)
    tokens = draw_tokens(jax.random.fold_in(jax.random.fold_in(splits[14], part), 71), part)
    pair_list = draw_pair_list(jax.random.fold_in(jax.random.fold_in(splits[14], part), 71), part)
    confidence = jnp.clip(jnp.exp(math.log(10.0) - 4.6051702 * jax.random.uniform(part_splits[2], (PAIRS, 2 * TOKS), jnp.float32) ** block_scale(part_splits[2], (PAIRS, 2 * TOKS), ((0, 4),), -0.2, 0.2)), 0.1, 10.0)
    gain_self = jnp.clip(1.0 + 0.18 * jax.random.normal(splits[3], (D,), jnp.float32), 0.1, 1.9)
    gain_query = jnp.clip(1.0 + 0.18 * jax.random.normal(splits[4], (D,), jnp.float32), 0.1, 1.9)
    gain_context = jnp.clip(1.0 + 0.18 * jax.random.normal(splits[5], (D,), jnp.float32), 0.1, 1.9)
    gain_mlp = jnp.clip(1.0 + 0.18 * jax.random.normal(splits[6], (D,), jnp.float32), 0.1, 1.9)
    self_qkv = draw_self_qkv(jax.random.fold_in(splits[14], 71), part)
    self_out = bell_draw(splits[8], (D, D), D ** -0.5, 0.21875, ((0, 4),))
    cross_query = draw_cross_query(jax.random.fold_in(splits[14], 71), part)
    cross_kv = draw_cross_kv(jax.random.fold_in(splits[14], 71), part)
    cross_out = bell_draw(splits[11], (D, D), D ** -0.5, 0.21875, ((0, 4),))
    mlp_up = bell_draw(splits[12], (D, FF), D ** -0.5, 0.21875, ((1, 4),))
    mlp_down = bell_draw(splits[13], (FF, D), FF ** -0.5, 0.109375, ((0, 4),))
    return dict(tokens=tokens, pair_list=pair_list, confidence=confidence, gain_self=gain_self, gain_query=gain_query, gain_context=gain_context, gain_mlp=gain_mlp, self_qkv=self_qkv, self_out=self_out, cross_query=cross_query, cross_kv=cross_kv, cross_out=cross_out, mlp_up=mlp_up, mlp_down=mlp_down)


EPSILON = 1e-06

def layer_norm(values, gain):
    center = values - lax.optimization_barrier(jnp.mean(values, axis=-1, keepdims=True))
    spread = lax.optimization_barrier(jnp.mean(center * center, axis=-1, keepdims=True))
    return (center * lax.rsqrt(spread + EPSILON) * gain).astype(jnp.bfloat16)

def attend(query, keys, values):
    views_n, tokens_n, width = query.shape
    heads_n = width // HEAD
    qh = query.reshape(views_n, tokens_n, heads_n, HEAD).astype(jnp.float32)
    kh = keys.reshape(views_n, tokens_n, heads_n, HEAD).astype(jnp.float32)
    vh = values.reshape(views_n, tokens_n, heads_n, HEAD).astype(jnp.float32)
    scores = jnp.einsum('vqhc,vkhc->vhqk', qh, kh) * HEAD ** (-0.5)
    probs = jax.nn.softmax(scores, axis=-1).astype(jnp.bfloat16).astype(jnp.float32)
    mixed = jnp.einsum('vhqk,vkhc->vqhc', probs, vh)
    return mixed.astype(jnp.bfloat16).reshape(views_n * tokens_n, width)

def grouped_sum(mixed, weight):
    rows_n, inner = mixed.shape
    parts = jnp.einsum('rgc,gcd->rgd', mixed.reshape(rows_n, N_MP, inner // N_MP).astype(jnp.float32), weight.reshape(N_MP, inner // N_MP, weight.shape[1]).astype(jnp.float32))
    rounded = lax.optimization_barrier(parts.astype(jnp.bfloat16))
    return lax.optimization_barrier(jnp.sum(rounded.astype(jnp.float32), axis=1))

def partner(values):
    shape = values.shape
    paired = values.reshape((shape[0] // 2, 2) + shape[1:])
    return jnp.flip(paired, axis=1).reshape(shape)

def project(normed, weight):
    return jnp.dot(normed.astype(jnp.float32), weight.astype(jnp.float32)).astype(jnp.bfloat16)

def decode(start, gain_self, gain_query, gain_context, gain_mlp, self_qkv, self_out, cross_query, cross_kv, cross_out, mlp_up, mlp_down):
    views_n = start.shape[0]
    rows_n = views_n * TOKS
    resid = start.astype(jnp.float32).reshape(rows_n, D)
    context = layer_norm(partner(start.astype(jnp.float32)), gain_context).reshape(rows_n, D)
    normed = layer_norm(resid, gain_self)
    query = project(normed, self_qkv[0]).reshape(views_n, TOKS, D)
    keys = project(normed, self_qkv[1]).reshape(views_n, TOKS, D)
    values = project(normed, self_qkv[2]).reshape(views_n, TOKS, D)
    resid = resid + grouped_sum(attend(query, keys, values), self_out)
    normed = layer_norm(resid, gain_query)
    query = project(normed, cross_query).reshape(views_n, TOKS, D)
    keys = project(context, cross_kv[0]).reshape(views_n, TOKS, D)
    values = project(context, cross_kv[1]).reshape(views_n, TOKS, D)
    resid = resid + grouped_sum(attend(query, keys, values), cross_out)
    normed = layer_norm(resid, gain_mlp)
    hidden = jax.nn.gelu(jnp.dot(normed.astype(jnp.float32), mlp_up.astype(jnp.float32)), approximate=False)
    resid = resid + grouped_sum(hidden.astype(jnp.bfloat16), mlp_down)
    return resid.reshape(views_n, TOKS, D)

def reference(tokens, pair_list, confidence, gain_self, gain_query, gain_context, gain_mlp, self_qkv, self_out, cross_query, cross_kv, cross_out, mlp_up, mlp_down):
    images = tokens.reshape(-1, TOKS, D)
    images_n = images.shape[0]
    blocks = pair_list.reshape(-1, 2 * PAIR_DEV).astype(jnp.int32)
    conf_blocks = confidence.reshape(-1, 2 * PAIR_DEV, TOKS)

    def per_block(carry, item):
        num, den = carry
        ids, conf = item
        start = jnp.take(images, ids, axis=0)
        final = decode(start, gain_self, gain_query, gain_context, gain_mlp, self_qkv, self_out, cross_query, cross_kv, cross_out, mlp_up, mlp_down)
        weighted = final * conf[:, :, None]
        same = (ids[:, None] == ids[None, :]).astype(jnp.float32)
        grouped = jnp.einsum('uv,vtd->utd', same, weighted, precision=lax.Precision.HIGHEST).astype(jnp.bfloat16)
        grouped_w = jnp.dot(same, conf, precision=lax.Precision.HIGHEST).astype(jnp.bfloat16)
        first = (lax.optimization_barrier(jnp.sum(jnp.tril(same, -1), axis=1)) == 0).astype(jnp.float32)
        num = num.at[ids].add(grouped.astype(jnp.float32) * first[:, None, None])
        den = den.at[ids].add(grouped_w.astype(jnp.float32) * first[:, None])
        return ((num, den), None)
    init = (jnp.zeros((images_n, TOKS, D), jnp.float32), jnp.zeros((images_n, TOKS), jnp.float32))
    (num, den), _ = lax.scan(per_block, init, (blocks, conf_blocks))
    result = num / jnp.maximum(den, 1.0)[:, :, None]
    return result.astype(jnp.bfloat16).reshape(images_n * TOKS, D)
```

```python
import jax
import jax.numpy as jnp
from jax import lax
from jax.sharding import PartitionSpec as P

HEAD = 64
TOKS = 32


EPSILON = 1e-06


def layer_norm(values, gain):
    center = values - jnp.mean(values, axis=-1, keepdims=True)
    spread = jnp.mean(center * center, axis=-1, keepdims=True)
    return (center * lax.rsqrt(spread + EPSILON) * gain).astype(jnp.bfloat16)


def attend(query, keys, values, views_n):
    rows_n, width = query.shape
    heads_n = width // HEAD
    qh = query.reshape(views_n, TOKS, heads_n, HEAD)
    kh = keys.reshape(views_n, TOKS, heads_n, HEAD)
    vh = values.reshape(views_n, TOKS, heads_n, HEAD)
    scores = jnp.einsum("vqhc,vkhc->vhqk", qh, kh, preferred_element_type=jnp.float32) * HEAD ** (
        -0.5
    )
    probs = jax.nn.softmax(scores, axis=-1).astype(jnp.bfloat16)
    mixed = jnp.einsum("vhqk,vkhc->vqhc", probs, vh, preferred_element_type=jnp.float32)
    return mixed.astype(jnp.bfloat16).reshape(rows_n, width)


def swap(values, pairs):
    return lax.ppermute(values, "mp", pairs)


def mp_pairs(bit):
    n = 4
    return [(i, i ^ bit) for i in range(n)]


def mp_allreduce(term):
    if lax.axis_size("mp") != 4:
        return lax.psum(term.astype(jnp.float32), "mp")
    core = lax.axis_index("mp") % 2
    rows_n = term.shape[0]
    halves = term.reshape(2, rows_n // 2, term.shape[1])
    keep = jnp.where(core == 0, halves[0], halves[1])
    send = jnp.where(core == 0, halves[1], halves[0])
    got = swap(send, mp_pairs(1))
    chip_sum = (keep.astype(jnp.float32) + got.astype(jnp.float32)).astype(jnp.bfloat16)
    other = swap(chip_sum, mp_pairs(2))
    total = chip_sum.astype(jnp.float32) + other.astype(jnp.float32)
    rest = swap(total, mp_pairs(1))
    first = jnp.where(core == 0, total, rest)
    second = jnp.where(core == 0, rest, total)
    return jnp.concatenate([first, second], axis=0)


def mp_reduce_cols(term):
    if lax.axis_size("mp") != 4:
        full = lax.psum(term.astype(jnp.float32), "mp")
        quarter = term.shape[1] // lax.axis_size("mp")
        return lax.dynamic_slice_in_dim(full, lax.axis_index("mp") * quarter, quarter, 1)
    index = lax.axis_index("mp")
    core = index % 2
    chip = index // 2
    rows_n, width = term.shape
    parts = term.reshape(rows_n, 2, 2, width // 4)
    keep = jnp.where(core == 0, parts[:, :, 0], parts[:, :, 1])
    send = jnp.where(core == 0, parts[:, :, 1], parts[:, :, 0])
    got = swap(send, mp_pairs(1))
    both = keep.astype(jnp.float32) + got.astype(jnp.float32)
    mine = jnp.where(chip == 0, both[:, 0], both[:, 1])
    theirs = jnp.where(chip == 0, both[:, 1], both[:, 0])
    other = swap(theirs, mp_pairs(2))
    return mine + other


def mp_gather_cols(part):
    if lax.axis_size("mp") != 4:
        return lax.all_gather(part, "mp", axis=2, tiled=True)
    index = lax.axis_index("mp")
    core = index % 2
    chip = index // 2
    got = swap(part, mp_pairs(1))
    pair = jnp.where(
        core == 0, jnp.concatenate([part, got], axis=2), jnp.concatenate([got, part], axis=2)
    )
    other = swap(pair, mp_pairs(2))
    return jnp.where(
        chip == 0, jnp.concatenate([pair, other], axis=2), jnp.concatenate([other, pair], axis=2)
    )


def per_device(
    tokens,
    pair_list,
    confidence,
    gain_self,
    gain_query,
    gain_context,
    gain_mlp,
    self_qkv,
    self_out,
    cross_query,
    cross_kv,
    cross_out,
    mlp_up,
    mlp_down,
):
    quarter = tokens.shape[1]
    img_dev = tokens.shape[0] // TOKS
    pair_dev = pair_list.shape[0]
    views_n = 2 * pair_dev
    owners_n = lax.axis_size("pairs")
    every = lax.all_gather(tokens, "pairs", axis=0, tiled=True).reshape(
        owners_n * img_dev, TOKS, quarter
    )
    ids = pair_list.reshape(views_n)
    slices = jnp.take(every, ids, axis=0)
    start = mp_gather_cols(slices)
    width = start.shape[2]
    rows_n = views_n * TOKS
    flipped = start.reshape(pair_dev, 2, TOKS, width)
    flipped = jnp.concatenate([flipped[:, 1:], flipped[:, :1]], axis=1)
    begin = start.astype(jnp.float32).reshape(rows_n, width)
    context = layer_norm(flipped.astype(jnp.float32), gain_context).reshape(rows_n, width)
    normed = layer_norm(begin, gain_self)
    qkv = jnp.einsum("rd,kdc->krc", normed, self_qkv, preferred_element_type=jnp.float32).astype(
        jnp.bfloat16
    )
    term = jnp.dot(
        attend(qkv[0], qkv[1], qkv[2], views_n), self_out, preferred_element_type=jnp.float32
    )
    resid = begin + mp_allreduce(term.astype(jnp.bfloat16))
    normed = layer_norm(resid, gain_query)
    query = jnp.dot(normed, cross_query, preferred_element_type=jnp.float32).astype(jnp.bfloat16)
    keyval = jnp.einsum(
        "rd,kdc->krc", context, cross_kv, preferred_element_type=jnp.float32
    ).astype(jnp.bfloat16)
    term = jnp.dot(
        attend(query, keyval[0], keyval[1], views_n), cross_out, preferred_element_type=jnp.float32
    )
    resid = resid + mp_allreduce(term.astype(jnp.bfloat16))
    normed = layer_norm(resid, gain_mlp)
    hidden = jax.nn.gelu(
        jnp.dot(normed, mlp_up, preferred_element_type=jnp.float32), approximate=False
    )
    term = jnp.dot(hidden.astype(jnp.bfloat16), mlp_down, preferred_element_type=jnp.float32)
    offset = lax.axis_index("mp") * quarter
    final = lax.dynamic_slice_in_dim(resid, offset, quarter, 1) + mp_reduce_cols(
        term.astype(jnp.bfloat16)
    )
    conf = confidence.reshape(views_n, TOKS)
    weighted = (final.reshape(views_n, TOKS, quarter) * conf[:, :, None]).reshape(
        views_n, TOKS * quarter
    )
    source = ids // img_dev
    slot = (ids % img_dev + 1).astype(jnp.float32)
    route = (source[None, :] == jnp.arange(owners_n)[:, None]).astype(jnp.float32)
    back = jnp.dot(route, weighted, precision=lax.Precision.HIGHEST)
    back_weight = jnp.dot(route, conf, precision=lax.Precision.HIGHEST)
    back_slot = jnp.dot(route, slot[:, None], precision=lax.Precision.HIGHEST)
    pad = jnp.zeros((owners_n, 128 - TOKS - 1), jnp.float32)
    payload = jnp.concatenate([back, back_weight, back_slot, pad], axis=1).astype(jnp.bfloat16)
    got = lax.all_to_all(payload, "pairs", split_axis=0, concat_axis=0, tiled=True).astype(
        jnp.float32
    )
    feat = got[:, : TOKS * quarter].reshape(owners_n, TOKS, quarter)
    got_weight = got[:, TOKS * quarter : TOKS * quarter + TOKS]
    got_slot = got[:, TOKS * quarter + TOKS]
    owner_match = (got_slot[None, :] == (jnp.arange(img_dev) + 1)[:, None].astype(jnp.float32)).astype(
        jnp.float32
    )
    numer = jnp.einsum("ij,jtc->itc", owner_match, feat, precision=lax.Precision.HIGHEST)
    denom = jnp.dot(owner_match, got_weight, precision=lax.Precision.HIGHEST)
    result = numer / jnp.maximum(denom, 1.0)[:, :, None]
    return result.astype(jnp.bfloat16).reshape(img_dev * TOKS, quarter)


def solution(mesh):
    return jax.shard_map(
        per_device,
        mesh=mesh,
        in_specs=(
            P(("groups", "pairs"), "mp"),
            P(("groups", "pairs"), None),
            P(("groups", "pairs"), None),
            P(),
            P(),
            P(),
            P(),
            P(None, None, "mp"),
            P("mp", None),
            P(None, "mp"),
            P(None, None, "mp"),
            P("mp", None),
            P(None, "mp"),
            P("mp", None),
        ),
        out_specs=P(("groups", "pairs"), "mp"),
        check_vma=False,
    )
```

```python
import jax
import jax.numpy as jnp
from jax import lax
from jax.sharding import PartitionSpec as P

HEAD = 64
TOKS = 32


EPSILON = 1e-06


def layer_norm(values, gain):
    center = values - jnp.mean(values, axis=-1, keepdims=True)
    spread = jnp.mean(center * center, axis=-1, keepdims=True)
    return (center * lax.rsqrt(spread + EPSILON) * gain).astype(jnp.bfloat16)


def attend(query, keys, values, views_n):
    rows_n, width = query.shape
    heads_n = width // HEAD
    qh = query.reshape(views_n, TOKS, heads_n, HEAD)
    kh = keys.reshape(views_n, TOKS, heads_n, HEAD)
    vh = values.reshape(views_n, TOKS, heads_n, HEAD)
    scores = jnp.einsum("vqhc,vkhc->vhqk", qh, kh, preferred_element_type=jnp.float32) * HEAD ** (
        -0.5
    )
    probs = jax.nn.softmax(scores, axis=-1).astype(jnp.bfloat16)
    mixed = jnp.einsum("vhqk,vkhc->vqhc", probs, vh, preferred_element_type=jnp.float32)
    return mixed.astype(jnp.bfloat16).reshape(rows_n, width)


SHIFTS_MAX = 8


def pairs_shift(values, step, owners_n):
    return lax.ppermute(values, "pairs", [(i, (i + step) % owners_n) for i in range(owners_n)])


def swap(values, pairs):
    return lax.ppermute(values, "mp", pairs)


def mp_pairs(bit):
    n = 4
    return [(i, i ^ bit) for i in range(n)]


def mp_allreduce(term):
    if lax.axis_size("mp") != 4:
        return lax.psum(term.astype(jnp.float32), "mp")
    core = lax.axis_index("mp") % 2
    rows_n = term.shape[0]
    halves = term.reshape(2, rows_n // 2, term.shape[1])
    keep = jnp.where(core == 0, halves[0], halves[1])
    send = jnp.where(core == 0, halves[1], halves[0])
    got = swap(send, mp_pairs(1))
    chip_sum = (keep.astype(jnp.float32) + got.astype(jnp.float32)).astype(jnp.bfloat16)
    other = swap(chip_sum, mp_pairs(2))
    total = chip_sum.astype(jnp.float32) + other.astype(jnp.float32)
    rest = swap(total, mp_pairs(1))
    first = jnp.where(core == 0, total, rest)
    second = jnp.where(core == 0, rest, total)
    return jnp.concatenate([first, second], axis=0)


def mp_reduce_cols(term):
    if lax.axis_size("mp") != 4:
        full = lax.psum(term.astype(jnp.float32), "mp")
        quarter = term.shape[1] // lax.axis_size("mp")
        return lax.dynamic_slice_in_dim(full, lax.axis_index("mp") * quarter, quarter, 1)
    index = lax.axis_index("mp")
    core = index % 2
    chip = index // 2
    rows_n, width = term.shape
    parts = term.reshape(rows_n, 2, 2, width // 4)
    keep = jnp.where(core == 0, parts[:, :, 0], parts[:, :, 1])
    send = jnp.where(core == 0, parts[:, :, 1], parts[:, :, 0])
    got = swap(send, mp_pairs(1))
    both = keep.astype(jnp.float32) + got.astype(jnp.float32)
    mine = jnp.where(chip == 0, both[:, 0], both[:, 1])
    theirs = jnp.where(chip == 0, both[:, 1], both[:, 0])
    other = swap(theirs, mp_pairs(2))
    return mine + other


def mp_gather_cols(part):
    if lax.axis_size("mp") != 4:
        return lax.all_gather(part, "mp", axis=2, tiled=True)
    index = lax.axis_index("mp")
    core = index % 2
    chip = index // 2
    got = swap(part, mp_pairs(1))
    pair = jnp.where(
        core == 0, jnp.concatenate([part, got], axis=2), jnp.concatenate([got, part], axis=2)
    )
    other = swap(pair, mp_pairs(2))
    return jnp.where(
        chip == 0, jnp.concatenate([pair, other], axis=2), jnp.concatenate([other, pair], axis=2)
    )


def per_device(
    tokens,
    pair_list,
    confidence,
    gain_self,
    gain_query,
    gain_context,
    gain_mlp,
    self_qkv,
    self_out,
    cross_query,
    cross_kv,
    cross_out,
    mlp_up,
    mlp_down,
):
    quarter = tokens.shape[1]
    img_dev = tokens.shape[0] // TOKS
    pair_dev = pair_list.shape[0]
    views_n = 2 * pair_dev
    owners_n = lax.axis_size("pairs")
    own = lax.axis_index("pairs")
    ids = pair_list.reshape(views_n)
    source = ids // img_dev
    if owners_n <= SHIFTS_MAX:
        every = jnp.concatenate(
            [tokens] + [pairs_shift(tokens, step, owners_n) for step in range(1, owners_n)], axis=0
        )
        at = ((own - source) % owners_n) * img_dev + ids % img_dev
        targets = (own + jnp.arange(owners_n)) % owners_n
    else:
        every = lax.all_gather(tokens, "pairs", axis=0, tiled=True)
        at = ids
        targets = jnp.arange(owners_n)
    every = every.reshape(owners_n * img_dev, TOKS, quarter)
    slices = jnp.take(every, at, axis=0)
    start = mp_gather_cols(slices)
    width = start.shape[2]
    rows_n = views_n * TOKS
    flipped = start.reshape(pair_dev, 2, TOKS, width)
    flipped = jnp.concatenate([flipped[:, 1:], flipped[:, :1]], axis=1)
    begin = start.astype(jnp.float32).reshape(rows_n, width)
    context = layer_norm(flipped.astype(jnp.float32), gain_context).reshape(rows_n, width)
    normed = layer_norm(begin, gain_self)
    qkv = jnp.einsum("rd,kdc->krc", normed, self_qkv, preferred_element_type=jnp.float32).astype(
        jnp.bfloat16
    )
    term = jnp.dot(
        attend(qkv[0], qkv[1], qkv[2], views_n), self_out, preferred_element_type=jnp.float32
    )
    resid = begin + mp_allreduce(term.astype(jnp.bfloat16))
    normed = layer_norm(resid, gain_query)
    query = jnp.dot(normed, cross_query, preferred_element_type=jnp.float32).astype(jnp.bfloat16)
    keyval = jnp.einsum(
        "rd,kdc->krc", context, cross_kv, preferred_element_type=jnp.float32
    ).astype(jnp.bfloat16)
    term = jnp.dot(
        attend(query, keyval[0], keyval[1], views_n), cross_out, preferred_element_type=jnp.float32
    )
    resid = resid + mp_allreduce(term.astype(jnp.bfloat16))
    normed = layer_norm(resid, gain_mlp)
    hidden = jax.nn.gelu(
        jnp.dot(normed, mlp_up, preferred_element_type=jnp.float32), approximate=False
    )
    term = jnp.dot(hidden.astype(jnp.bfloat16), mlp_down, preferred_element_type=jnp.float32)
    offset = lax.axis_index("mp") * quarter
    final = lax.dynamic_slice_in_dim(resid, offset, quarter, 1) + mp_reduce_cols(
        term.astype(jnp.bfloat16)
    )
    conf = confidence.reshape(views_n, TOKS)
    weighted = (final.reshape(views_n, TOKS, quarter) * conf[:, :, None]).reshape(
        views_n, TOKS * quarter
    )
    slot = (ids % img_dev + 1).astype(jnp.float32)
    route = (source[None, :] == targets[:, None]).astype(jnp.float32)
    back = jnp.dot(route, weighted, precision=lax.Precision.HIGHEST)
    back_weight = jnp.dot(route, conf, precision=lax.Precision.HIGHEST)
    back_slot = jnp.dot(route, slot[:, None], precision=lax.Precision.HIGHEST)
    pad = jnp.zeros((owners_n, 128 - TOKS - 1), jnp.float32)
    payload = jnp.concatenate([back, back_weight, back_slot, pad], axis=1).astype(jnp.bfloat16)
    if owners_n <= SHIFTS_MAX:
        got = jnp.stack(
            [payload[0]]
            + [pairs_shift(payload[step], step, owners_n) for step in range(1, owners_n)]
        )
    else:
        got = lax.all_to_all(payload, "pairs", split_axis=0, concat_axis=0, tiled=True)
    got = got.astype(jnp.float32)
    feat = got[:, : TOKS * quarter].reshape(owners_n, TOKS, quarter)
    got_weight = got[:, TOKS * quarter : TOKS * quarter + TOKS]
    got_slot = got[:, TOKS * quarter + TOKS]
    owner_match = (got_slot[None, :] == (jnp.arange(img_dev) + 1)[:, None].astype(jnp.float32)).astype(
        jnp.float32
    )
    numer = jnp.einsum("ij,jtc->itc", owner_match, feat, precision=lax.Precision.HIGHEST)
    denom = jnp.dot(owner_match, got_weight, precision=lax.Precision.HIGHEST)
    result = numer / jnp.maximum(denom, 1.0)[:, :, None]
    return result.astype(jnp.bfloat16).reshape(img_dev * TOKS, quarter)


def solution(mesh):
    return jax.shard_map(
        per_device,
        mesh=mesh,
        in_specs=(
            P(("groups", "pairs"), "mp"),
            P(("groups", "pairs"), None),
            P(("groups", "pairs"), None),
            P(),
            P(),
            P(),
            P(),
            P(None, None, "mp"),
            P("mp", None),
            P(None, "mp"),
            P(None, None, "mp"),
            P("mp", None),
            P(None, "mp"),
            P("mp", None),
        ),
        out_specs=P(("groups", "pairs"), "mp"),
        check_vma=False,
    )
```

```python
import jax
import jax.numpy as jnp
from jax import lax
from jax.sharding import PartitionSpec as P

HEAD = 64
TOKS = 32


EPSILON = 1e-06


def layer_norm(values, gain):
    center = values - jnp.mean(values, axis=-1, keepdims=True)
    spread = jnp.mean(center * center, axis=-1, keepdims=True)
    return (center * lax.rsqrt(spread + EPSILON) * gain).astype(jnp.bfloat16)


def attend(query, keys, values, views_n):
    rows_n, width = query.shape
    heads_n = width // HEAD
    qh = query.reshape(views_n, TOKS, heads_n, HEAD)
    kh = keys.reshape(views_n, TOKS, heads_n, HEAD)
    vh = values.reshape(views_n, TOKS, heads_n, HEAD)
    scores = jnp.einsum("vqhc,vkhc->vhqk", qh, kh, preferred_element_type=jnp.float32) * HEAD ** (
        -0.5
    )
    probs = jax.nn.softmax(scores, axis=-1).astype(jnp.bfloat16)
    mixed = jnp.einsum("vhqk,vkhc->vqhc", probs, vh, preferred_element_type=jnp.float32)
    return mixed.astype(jnp.bfloat16).reshape(rows_n, width)


SHIFTS_MAX = 8


def pairs_shift(values, step, owners_n):
    return lax.ppermute(values, "pairs", [(i, (i + step) % owners_n) for i in range(owners_n)])


def swap(values, pairs):
    return lax.ppermute(values, "mp", pairs)


def mp_pairs(bit):
    n = 4
    return [(i, i ^ bit) for i in range(n)]


def mp_allreduce(term):
    if lax.axis_size("mp") != 4:
        return lax.psum(term.astype(jnp.float32), "mp")
    core = lax.axis_index("mp") % 2
    rows_n = term.shape[0]
    halves = term.reshape(2, rows_n // 2, term.shape[1])
    keep = jnp.where(core == 0, halves[0], halves[1])
    send = jnp.where(core == 0, halves[1], halves[0])
    got = swap(send, mp_pairs(1))
    chip_sum = (keep.astype(jnp.float32) + got.astype(jnp.float32)).astype(jnp.bfloat16)
    other = swap(chip_sum, mp_pairs(2))
    total = chip_sum.astype(jnp.float32) + other.astype(jnp.float32)
    rest = swap(total, mp_pairs(1))
    first = jnp.where(core == 0, total, rest)
    second = jnp.where(core == 0, rest, total)
    return jnp.concatenate([first, second], axis=0)


def mp_reduce_cols(term):
    if lax.axis_size("mp") != 4:
        full = lax.psum(term.astype(jnp.float32), "mp")
        quarter = term.shape[1] // lax.axis_size("mp")
        return lax.dynamic_slice_in_dim(full, lax.axis_index("mp") * quarter, quarter, 1)
    index = lax.axis_index("mp")
    rows_n, width = term.shape
    parts = term.reshape(rows_n, 4, width // 4)
    total = jnp.take(parts, index, axis=1).astype(jnp.float32)
    for bit in (1, 2, 3):
        total = total + swap(jnp.take(parts, index ^ bit, axis=1), mp_pairs(bit)).astype(jnp.float32)
    return total


def gather_tokens(tokens, owners_n):
    index = lax.axis_index("mp")
    core = index % 2
    chip = index // 2
    got = swap(tokens, mp_pairs(1))
    half = jnp.where(
        core == 0, jnp.concatenate([tokens, got], axis=1), jnp.concatenate([got, tokens], axis=1)
    )
    owners = []
    for step in range(owners_n):
        moved = []
        for cross in (0, 2):
            if step == 0 and cross == 0:
                moved.append(half)
                continue
            perm = [
                (p * 4 + m, ((p + step) % owners_n) * 4 + (m ^ cross))
                for p in range(owners_n)
                for m in range(4)
            ]
            moved.append(lax.ppermute(half, ("pairs", "mp"), perm))
        mine, other = moved
        owners.append(
            jnp.where(
                chip == 0,
                jnp.concatenate([mine, other], axis=1),
                jnp.concatenate([other, mine], axis=1),
            )
        )
    return jnp.stack(owners)


def mp_gather_cols(part):
    if lax.axis_size("mp") != 4:
        return lax.all_gather(part, "mp", axis=2, tiled=True)
    index = lax.axis_index("mp")
    core = index % 2
    chip = index // 2
    got = swap(part, mp_pairs(1))
    pair = jnp.where(
        core == 0, jnp.concatenate([part, got], axis=2), jnp.concatenate([got, part], axis=2)
    )
    other = swap(pair, mp_pairs(2))
    return jnp.where(
        chip == 0, jnp.concatenate([pair, other], axis=2), jnp.concatenate([other, pair], axis=2)
    )


def per_device(
    tokens,
    pair_list,
    confidence,
    gain_self,
    gain_query,
    gain_context,
    gain_mlp,
    self_qkv,
    self_out,
    cross_query,
    cross_kv,
    cross_out,
    mlp_up,
    mlp_down,
):
    quarter = tokens.shape[1]
    img_dev = tokens.shape[0] // TOKS
    pair_dev = pair_list.shape[0]
    views_n = 2 * pair_dev
    owners_n = lax.axis_size("pairs")
    own = lax.axis_index("pairs")
    ids = pair_list.reshape(views_n)
    source = ids // img_dev
    if owners_n <= SHIFTS_MAX and lax.axis_size("mp") == 4:
        every = gather_tokens(tokens, owners_n)
        at = ((own - source) % owners_n) * img_dev + ids % img_dev
        targets = (own + jnp.arange(owners_n)) % owners_n
    else:
        every = lax.all_gather(tokens, "pairs", axis=0, tiled=True)
        every = lax.all_gather(every, "mp", axis=1, tiled=True)
        at = ids
        targets = jnp.arange(owners_n)
    every = every.reshape(owners_n * img_dev, TOKS * 4 * quarter)
    pick = (at[:, None] == jnp.arange(owners_n * img_dev)[None, :]).astype(jnp.bfloat16)
    start = (
        jnp.dot(pick, every, preferred_element_type=jnp.float32)
        .astype(jnp.bfloat16)
        .reshape(views_n, TOKS, 4 * quarter)
    )
    width = start.shape[2]
    rows_n = views_n * TOKS
    flipped = start.reshape(pair_dev, 2, TOKS, width)
    flipped = jnp.concatenate([flipped[:, 1:], flipped[:, :1]], axis=1)
    begin = start.astype(jnp.float32).reshape(rows_n, width)
    context = layer_norm(flipped.astype(jnp.float32), gain_context).reshape(rows_n, width)
    normed = layer_norm(begin, gain_self)
    qkv = jnp.einsum("rd,kdc->krc", normed, self_qkv, preferred_element_type=jnp.float32).astype(
        jnp.bfloat16
    )
    term = jnp.dot(
        attend(qkv[0], qkv[1], qkv[2], views_n), self_out, preferred_element_type=jnp.float32
    )
    resid = begin + mp_allreduce(term.astype(jnp.bfloat16))
    normed = layer_norm(resid, gain_query)
    query = jnp.dot(normed, cross_query, preferred_element_type=jnp.float32).astype(jnp.bfloat16)
    keyval = jnp.einsum(
        "rd,kdc->krc", context, cross_kv, preferred_element_type=jnp.float32
    ).astype(jnp.bfloat16)
    term = jnp.dot(
        attend(query, keyval[0], keyval[1], views_n), cross_out, preferred_element_type=jnp.float32
    )
    resid = resid + mp_allreduce(term.astype(jnp.bfloat16))
    normed = layer_norm(resid, gain_mlp)
    hidden = jax.nn.gelu(
        jnp.dot(normed, mlp_up, preferred_element_type=jnp.float32), approximate=False
    )
    term = jnp.dot(hidden.astype(jnp.bfloat16), mlp_down, preferred_element_type=jnp.float32)
    offset = lax.axis_index("mp") * quarter
    final = lax.dynamic_slice_in_dim(resid, offset, quarter, 1) + mp_reduce_cols(
        term.astype(jnp.bfloat16)
    )
    conf = confidence.reshape(views_n, TOKS)
    weighted = (final.reshape(views_n, TOKS, quarter) * conf[:, :, None]).reshape(
        views_n, TOKS * quarter
    )
    slot = (ids % img_dev + 1).astype(jnp.float32)
    route = (source[None, :] == targets[:, None]).astype(jnp.float32)
    back = jnp.dot(route, weighted, precision=lax.Precision.HIGHEST)
    back_weight = jnp.dot(route, conf, precision=lax.Precision.HIGHEST)
    back_slot = jnp.dot(route, slot[:, None], precision=lax.Precision.HIGHEST)
    pad = jnp.zeros((owners_n, 128 - TOKS - 1), jnp.float32)
    payload = jnp.concatenate([back, back_weight, back_slot, pad], axis=1).astype(jnp.bfloat16)
    if owners_n <= SHIFTS_MAX and lax.axis_size("mp") == 4:
        got = jnp.stack(
            [payload[0]]
            + [pairs_shift(payload[step], step, owners_n) for step in range(1, owners_n)]
        )
    else:
        got = lax.all_to_all(payload, "pairs", split_axis=0, concat_axis=0, tiled=True)
    got = got.astype(jnp.float32)
    feat = got[:, : TOKS * quarter].reshape(owners_n, TOKS, quarter)
    got_weight = got[:, TOKS * quarter : TOKS * quarter + TOKS]
    got_slot = got[:, TOKS * quarter + TOKS]
    owner_match = (got_slot[None, :] == (jnp.arange(img_dev) + 1)[:, None].astype(jnp.float32)).astype(
        jnp.float32
    )
    numer = jnp.einsum("ij,jtc->itc", owner_match, feat, precision=lax.Precision.HIGHEST)
    denom = jnp.dot(owner_match, got_weight, precision=lax.Precision.HIGHEST)
    result = numer / jnp.maximum(denom, 1.0)[:, :, None]
    return result.astype(jnp.bfloat16).reshape(img_dev * TOKS, quarter)


def solution(mesh):
    return jax.shard_map(
        per_device,
        mesh=mesh,
        in_specs=(
            P(("groups", "pairs"), "mp"),
            P(("groups", "pairs"), None),
            P(("groups", "pairs"), None),
            P(),
            P(),
            P(),
            P(),
            P(None, None, "mp"),
            P("mp", None),
            P(None, "mp"),
            P(None, None, "mp"),
            P("mp", None),
            P(None, "mp"),
            P("mp", None),
        ),
        out_specs=P(("groups", "pairs"), "mp"),
        check_vma=False,
    )
```

```python
import jax
import jax.numpy as jnp
from jax import lax
from jax.sharding import PartitionSpec as P

HEAD = 64
TOKS = 32


EPSILON = 1e-06


def layer_norm(values, gain):
    center = values - jnp.mean(values, axis=-1, keepdims=True)
    spread = jnp.mean(center * center, axis=-1, keepdims=True)
    return (center * lax.rsqrt(spread + EPSILON) * gain).astype(jnp.bfloat16)


def attend(query, keys, values, views_n):
    rows_n, width = query.shape
    heads_n = width // HEAD
    qh = query.reshape(views_n, TOKS, heads_n, HEAD)
    kh = keys.reshape(views_n, TOKS, heads_n, HEAD)
    vh = values.reshape(views_n, TOKS, heads_n, HEAD)
    scores = jnp.einsum("vqhc,vkhc->vhqk", qh, kh, preferred_element_type=jnp.float32) * HEAD ** (
        -0.5
    )
    probs = jax.nn.softmax(scores, axis=-1).astype(jnp.bfloat16)
    mixed = jnp.einsum("vhqk,vkhc->vqhc", probs, vh, preferred_element_type=jnp.float32)
    return mixed.astype(jnp.bfloat16).reshape(rows_n, width)


SHIFTS_MAX = 8


def pairs_shift(values, step, owners_n):
    return lax.ppermute(values, "pairs", [(i, (i + step) % owners_n) for i in range(owners_n)])


def swap(values, pairs):
    return lax.ppermute(values, "mp", pairs)


def mp_pairs(bit):
    n = 4
    return [(i, i ^ bit) for i in range(n)]


def mp_allreduce(term):
    if lax.axis_size("mp") != 4:
        return lax.psum(term.astype(jnp.float32), "mp")
    core = lax.axis_index("mp") % 2
    rows_n = term.shape[0]
    halves = term.reshape(2, rows_n // 2, term.shape[1])
    keep = jnp.where(core == 0, halves[0], halves[1])
    send = jnp.where(core == 0, halves[1], halves[0])
    got = swap(send, mp_pairs(1))
    chip_sum = (keep.astype(jnp.float32) + got.astype(jnp.float32)).astype(jnp.bfloat16)
    other = swap(chip_sum, mp_pairs(2))
    total = chip_sum.astype(jnp.float32) + other.astype(jnp.float32)
    rest = swap(total, mp_pairs(1))
    first = jnp.where(core == 0, total, rest)
    second = jnp.where(core == 0, rest, total)
    return jnp.concatenate([first, second], axis=0)


def mp_reduce_cols(term):
    if lax.axis_size("mp") != 4:
        full = lax.psum(term.astype(jnp.float32), "mp")
        quarter = term.shape[1] // lax.axis_size("mp")
        return lax.dynamic_slice_in_dim(full, lax.axis_index("mp") * quarter, quarter, 1)
    index = lax.axis_index("mp")
    rows_n, width = term.shape
    parts = term.reshape(rows_n, 4, width // 4)
    total = jnp.take(parts, index, axis=1).astype(jnp.float32)
    for bit in (1, 2, 3):
        total = total + swap(jnp.take(parts, index ^ bit, axis=1), mp_pairs(bit)).astype(jnp.float32)
    return total


def mp_gather_cols(part):
    if lax.axis_size("mp") != 4:
        return lax.all_gather(part, "mp", axis=2, tiled=True)
    index = lax.axis_index("mp")
    core = index % 2
    chip = index // 2
    got = swap(part, mp_pairs(1))
    pair = jnp.where(
        core == 0, jnp.concatenate([part, got], axis=2), jnp.concatenate([got, part], axis=2)
    )
    other = swap(pair, mp_pairs(2))
    return jnp.where(
        chip == 0, jnp.concatenate([pair, other], axis=2), jnp.concatenate([other, pair], axis=2)
    )


def per_device(
    tokens,
    pair_list,
    confidence,
    gain_self,
    gain_query,
    gain_context,
    gain_mlp,
    self_qkv,
    self_out,
    cross_query,
    cross_kv,
    cross_out,
    mlp_up,
    mlp_down,
):
    quarter = tokens.shape[1]
    img_dev = tokens.shape[0] // TOKS
    pair_dev = pair_list.shape[0]
    views_n = 2 * pair_dev
    owners_n = lax.axis_size("pairs")
    own = lax.axis_index("pairs")
    ids = pair_list.reshape(views_n)
    source = ids // img_dev
    if owners_n <= SHIFTS_MAX:
        every = jnp.concatenate(
            [tokens] + [pairs_shift(tokens, step, owners_n) for step in range(1, owners_n)], axis=0
        )
        at = ((own - source) % owners_n) * img_dev + ids % img_dev
        targets = (own + jnp.arange(owners_n)) % owners_n
    else:
        every = lax.all_gather(tokens, "pairs", axis=0, tiled=True)
        at = ids
        targets = jnp.arange(owners_n)
    every = every.reshape(owners_n * img_dev, TOKS * quarter)
    pick = (at[:, None] == jnp.arange(owners_n * img_dev)[None, :]).astype(jnp.bfloat16)
    slices = (
        jnp.dot(pick, every, preferred_element_type=jnp.float32)
        .astype(jnp.bfloat16)
        .reshape(views_n, TOKS, quarter)
    )
    start = mp_gather_cols(slices)
    width = start.shape[2]
    rows_n = views_n * TOKS
    flipped = start.reshape(pair_dev, 2, TOKS, width)
    flipped = jnp.concatenate([flipped[:, 1:], flipped[:, :1]], axis=1)
    begin = start.astype(jnp.float32).reshape(rows_n, width)
    context = layer_norm(flipped.astype(jnp.float32), gain_context).reshape(rows_n, width)
    normed = layer_norm(begin, gain_self)
    qkv = jnp.einsum("rd,kdc->krc", normed, self_qkv, preferred_element_type=jnp.float32).astype(
        jnp.bfloat16
    )
    term = jnp.dot(
        attend(qkv[0], qkv[1], qkv[2], views_n), self_out, preferred_element_type=jnp.float32
    )
    resid = begin + mp_allreduce(term.astype(jnp.bfloat16))
    normed = layer_norm(resid, gain_query)
    query = jnp.dot(normed, cross_query, preferred_element_type=jnp.float32).astype(jnp.bfloat16)
    keyval = jnp.einsum(
        "rd,kdc->krc", context, cross_kv, preferred_element_type=jnp.float32
    ).astype(jnp.bfloat16)
    term = jnp.dot(
        attend(query, keyval[0], keyval[1], views_n), cross_out, preferred_element_type=jnp.float32
    )
    resid = resid + mp_allreduce(term.astype(jnp.bfloat16))
    normed = layer_norm(resid, gain_mlp)
    hidden = jax.nn.gelu(
        jnp.dot(normed, mlp_up, preferred_element_type=jnp.float32), approximate=False
    )
    term = jnp.dot(hidden.astype(jnp.bfloat16), mlp_down, preferred_element_type=jnp.float32)
    offset = lax.axis_index("mp") * quarter
    final = lax.dynamic_slice_in_dim(resid, offset, quarter, 1) + mp_reduce_cols(
        term.astype(jnp.bfloat16)
    )
    conf = confidence.reshape(views_n, TOKS)
    weighted = (final.reshape(views_n, TOKS, quarter) * conf[:, :, None]).reshape(
        views_n, TOKS * quarter
    )
    slot = (ids % img_dev + 1).astype(jnp.float32)
    route = (source[None, :] == targets[:, None]).astype(jnp.float32)
    back = jnp.dot(route, weighted, precision=lax.Precision.HIGHEST)
    back_weight = jnp.dot(route, conf, precision=lax.Precision.HIGHEST)
    back_slot = jnp.dot(route, slot[:, None], precision=lax.Precision.HIGHEST)
    pad = jnp.zeros((owners_n, 128 - TOKS - 1), jnp.float32)
    payload = jnp.concatenate([back, back_weight, back_slot, pad], axis=1).astype(jnp.bfloat16)
    if owners_n <= SHIFTS_MAX:
        got = jnp.stack(
            [payload[0]]
            + [pairs_shift(payload[step], step, owners_n) for step in range(1, owners_n)]
        )
    else:
        got = lax.all_to_all(payload, "pairs", split_axis=0, concat_axis=0, tiled=True)
    got = got.astype(jnp.float32)
    feat = got[:, : TOKS * quarter].reshape(owners_n, TOKS, quarter)
    got_weight = got[:, TOKS * quarter : TOKS * quarter + TOKS]
    got_slot = got[:, TOKS * quarter + TOKS]
    owner_match = (got_slot[None, :] == (jnp.arange(img_dev) + 1)[:, None].astype(jnp.float32)).astype(
        jnp.float32
    )
    numer = jnp.einsum("ij,jtc->itc", owner_match, feat, precision=lax.Precision.HIGHEST)
    denom = jnp.dot(owner_match, got_weight, precision=lax.Precision.HIGHEST)
    result = numer / jnp.maximum(denom, 1.0)[:, :, None]
    return result.astype(jnp.bfloat16).reshape(img_dev * TOKS, quarter)


def solution(mesh):
    return jax.shard_map(
        per_device,
        mesh=mesh,
        in_specs=(
            P(("groups", "pairs"), "mp"),
            P(("groups", "pairs"), None),
            P(("groups", "pairs"), None),
            P(),
            P(),
            P(),
            P(),
            P(None, None, "mp"),
            P("mp", None),
            P(None, "mp"),
            P(None, None, "mp"),
            P("mp", None),
            P(None, "mp"),
            P("mp", None),
        ),
        out_specs=P(("groups", "pairs"), "mp"),
        check_vma=False,
    )
```

```python
import jax
import jax.numpy as jnp
from jax import lax
from jax.sharding import PartitionSpec as P

HEAD = 64
TOKS = 32


EPSILON = 1e-06


def layer_norm(values, gain):
    center = values - jnp.mean(values, axis=-1, keepdims=True)
    spread = jnp.mean(center * center, axis=-1, keepdims=True)
    return (center * lax.rsqrt(spread + EPSILON) * gain).astype(jnp.bfloat16)


def attend(query, keys, values, views_n):
    rows_n, width = query.shape
    heads_n = width // HEAD
    qh = query.reshape(views_n, TOKS, heads_n, HEAD)
    kh = keys.reshape(views_n, TOKS, heads_n, HEAD)
    vh = values.reshape(views_n, TOKS, heads_n, HEAD)
    scores = jnp.einsum("vqhc,vkhc->vhqk", qh, kh, preferred_element_type=jnp.float32) * HEAD ** (
        -0.5
    )
    probs = jax.nn.softmax(scores, axis=-1).astype(jnp.bfloat16)
    mixed = jnp.einsum("vhqk,vkhc->vqhc", probs, vh, preferred_element_type=jnp.float32)
    return mixed.astype(jnp.bfloat16).reshape(rows_n, width)


SHIFTS_MAX = 8


def pairs_shift(values, step, owners_n):
    return lax.ppermute(values, "pairs", [(i, (i + step) % owners_n) for i in range(owners_n)])


def swap(values, pairs):
    return lax.ppermute(values, "mp", pairs)


def mp_pairs(bit):
    n = 4
    return [(i, i ^ bit) for i in range(n)]


def mp_allreduce(term):
    if lax.axis_size("mp") != 4:
        return lax.psum(term.astype(jnp.float32), "mp")
    core = lax.axis_index("mp") % 2
    rows_n = term.shape[0]
    halves = term.reshape(2, rows_n // 2, term.shape[1])
    keep = jnp.where(core == 0, halves[0], halves[1])
    send = jnp.where(core == 0, halves[1], halves[0])
    got = swap(send, mp_pairs(1))
    chip_sum = (keep.astype(jnp.float32) + got.astype(jnp.float32)).astype(jnp.bfloat16)
    other = swap(chip_sum, mp_pairs(2))
    total = chip_sum.astype(jnp.float32) + other.astype(jnp.float32)
    rest = swap(total, mp_pairs(1))
    first = jnp.where(core == 0, total, rest)
    second = jnp.where(core == 0, rest, total)
    return jnp.concatenate([first, second], axis=0)


def mp_reduce_cols(term):
    if lax.axis_size("mp") != 4:
        full = lax.psum(term.astype(jnp.float32), "mp")
        quarter = term.shape[1] // lax.axis_size("mp")
        return lax.dynamic_slice_in_dim(full, lax.axis_index("mp") * quarter, quarter, 1)
    index = lax.axis_index("mp")
    rows_n, width = term.shape
    parts = term.reshape(rows_n, 4, width // 4)
    total = jnp.take(parts, index, axis=1).astype(jnp.float32)
    for bit in (1, 2, 3):
        total = total + swap(jnp.take(parts, index ^ bit, axis=1), mp_pairs(bit)).astype(jnp.float32)
    return total


def mp_gather_cols(part):
    if lax.axis_size("mp") != 4:
        return lax.all_gather(part, "mp", axis=2, tiled=True)
    index = lax.axis_index("mp")
    core = index % 2
    chip = index // 2
    got = swap(part, mp_pairs(1))
    pair = jnp.where(
        core == 0, jnp.concatenate([part, got], axis=2), jnp.concatenate([got, part], axis=2)
    )
    other = swap(pair, mp_pairs(2))
    return jnp.where(
        chip == 0, jnp.concatenate([pair, other], axis=2), jnp.concatenate([other, pair], axis=2)
    )


def pairs_gather(payload, owners_n):
    if owners_n <= SHIFTS_MAX:
        return jnp.stack(
            [payload] + [pairs_shift(payload, step, owners_n) for step in range(1, owners_n)]
        )
    own = lax.axis_index("pairs")
    every = lax.all_gather(payload, "pairs", axis=0)
    return jnp.roll(every[::-1], own + 1, axis=0)


def pick_rows(onehot, values):
    shape = values.shape
    flat = values.reshape(shape[0], -1)
    picked = jnp.dot(onehot.astype(values.dtype), flat, preferred_element_type=jnp.float32)
    return picked.astype(values.dtype).reshape((onehot.shape[0],) + shape[1:])


def per_device(
    tokens,
    pair_list,
    confidence,
    gain_self,
    gain_query,
    gain_context,
    gain_mlp,
    self_qkv,
    self_out,
    cross_query,
    cross_kv,
    cross_out,
    mlp_up,
    mlp_down,
):
    quarter = tokens.shape[1]
    img_dev = tokens.shape[0] // TOKS
    pair_dev = pair_list.shape[0]
    views_n = 2 * pair_dev
    owners_n = lax.axis_size("pairs")
    own = lax.axis_index("pairs")

    payload = jnp.concatenate(
        [
            tokens.astype(jnp.float32).reshape(-1),
            pair_list.astype(jnp.float32).reshape(-1),
            confidence.reshape(-1),
        ]
    )
    table = pairs_gather(payload, owners_n)
    cut_tok = img_dev * TOKS * quarter
    cut_ids = cut_tok + views_n
    all_tok = table[:, :cut_tok].astype(jnp.bfloat16).reshape(owners_n * img_dev, TOKS * quarter)
    all_ids = table[:, cut_tok:cut_ids].astype(jnp.int32)
    all_conf = table[:, cut_ids:].reshape(owners_n * views_n, TOKS)
    partner_ids = all_ids.reshape(owners_n, pair_dev, 2)[:, :, ::-1].reshape(-1)
    all_ids = all_ids.reshape(-1)

    mine = (all_ids // img_dev == own).astype(jnp.int32)
    rank = jnp.cumsum(mine) - 1
    choose = (mine[None, :] == 1) & (rank[None, :] == jnp.arange(views_n)[:, None])
    image = jnp.sum(jnp.where(choose, all_ids[None, :], 0), axis=1)
    other = jnp.sum(jnp.where(choose, partner_ids[None, :], 0), axis=1)
    conf = jnp.dot(choose.astype(jnp.float32), all_conf, precision=lax.Precision.HIGHEST)
    local = image % img_dev
    at = ((own - other // img_dev) % owners_n) * img_dev + other % img_dev
    far = (at[:, None] == jnp.arange(owners_n * img_dev)[None, :]).astype(jnp.bfloat16)
    context_q = pick_rows(far, all_tok).reshape(views_n, TOKS, quarter)

    own_tok = mp_gather_cols(tokens.reshape(img_dev, TOKS, quarter))
    width = own_tok.shape[2]
    img_rows = img_dev * TOKS
    begin = own_tok.astype(jnp.float32).reshape(img_rows, width)
    normed = layer_norm(begin, gain_self)
    qkv = jnp.einsum("rd,kdc->krc", normed, self_qkv, preferred_element_type=jnp.float32).astype(
        jnp.bfloat16
    )
    term = jnp.dot(
        attend(qkv[0], qkv[1], qkv[2], img_dev), self_out, preferred_element_type=jnp.float32
    )
    resid_img = begin + mp_allreduce(term.astype(jnp.bfloat16))
    normed = layer_norm(resid_img, gain_query)
    query_img = jnp.dot(normed, cross_query, preferred_element_type=jnp.float32).astype(
        jnp.bfloat16
    )

    rows_n = views_n * TOKS
    context = layer_norm(mp_gather_cols(context_q).astype(jnp.float32), gain_context).reshape(
        rows_n, width
    )
    keyval = jnp.einsum(
        "rd,kdc->krc", context, cross_kv, preferred_element_type=jnp.float32
    ).astype(jnp.bfloat16)
    near = (local[:, None] == jnp.arange(img_dev)[None, :]).astype(jnp.bfloat16)
    query = pick_rows(near, query_img.reshape(img_dev, TOKS, -1)).reshape(rows_n, -1)
    resid = jnp.take(resid_img.reshape(img_dev, TOKS, width), local, axis=0).reshape(
        rows_n, width
    )
    term = jnp.dot(
        attend(query, keyval[0], keyval[1], views_n), cross_out, preferred_element_type=jnp.float32
    )
    resid = resid + mp_allreduce(term.astype(jnp.bfloat16))
    normed = layer_norm(resid, gain_mlp)
    hidden = jax.nn.gelu(
        jnp.dot(normed, mlp_up, preferred_element_type=jnp.float32), approximate=False
    )
    term = jnp.dot(hidden.astype(jnp.bfloat16), mlp_down, preferred_element_type=jnp.float32)
    offset = lax.axis_index("mp") * quarter
    final = lax.dynamic_slice_in_dim(resid, offset, quarter, 1) + mp_reduce_cols(
        term.astype(jnp.bfloat16)
    )
    part = (final.reshape(views_n, TOKS, quarter) * conf[:, :, None]).astype(jnp.bfloat16)
    weight = conf.astype(jnp.bfloat16)
    owner_match = near.astype(jnp.float32).T
    numer = jnp.einsum(
        "iv,vtc->itc", owner_match, part.astype(jnp.float32), precision=lax.Precision.HIGHEST
    )
    denom = jnp.dot(owner_match, weight.astype(jnp.float32), precision=lax.Precision.HIGHEST)
    result = numer / jnp.maximum(denom, 1.0)[:, :, None]
    return result.astype(jnp.bfloat16).reshape(img_dev * TOKS, quarter)


def solution(mesh):
    return jax.shard_map(
        per_device,
        mesh=mesh,
        in_specs=(
            P(("groups", "pairs"), "mp"),
            P(("groups", "pairs"), None),
            P(("groups", "pairs"), None),
            P(),
            P(),
            P(),
            P(),
            P(None, None, "mp"),
            P("mp", None),
            P(None, "mp"),
            P(None, None, "mp"),
            P("mp", None),
            P(None, "mp"),
            P("mp", None),
        ),
        out_specs=P(("groups", "pairs"), "mp"),
        check_vma=False,
    )
```

```python
import jax
import jax.numpy as jnp
from jax import lax
from jax.sharding import PartitionSpec as P

HEAD = 64
TOKS = 32


EPSILON = 1e-06


def layer_norm(values, gain):
    center = values - jnp.mean(values, axis=-1, keepdims=True)
    spread = jnp.mean(center * center, axis=-1, keepdims=True)
    return (center * lax.rsqrt(spread + EPSILON) * gain).astype(jnp.bfloat16)


def attend(query, keys, values, views_n):
    rows_n, width = query.shape
    heads_n = width // HEAD
    qh = query.reshape(views_n, TOKS, heads_n, HEAD)
    kh = keys.reshape(views_n, TOKS, heads_n, HEAD)
    vh = values.reshape(views_n, TOKS, heads_n, HEAD)
    scores = jnp.einsum("vqhc,vkhc->vhqk", qh, kh, preferred_element_type=jnp.float32) * HEAD ** (
        -0.5
    )
    probs = jax.nn.softmax(scores, axis=-1).astype(jnp.bfloat16)
    mixed = jnp.einsum("vhqk,vkhc->vqhc", probs, vh, preferred_element_type=jnp.float32)
    return mixed.astype(jnp.bfloat16).reshape(rows_n, width)


SHIFTS_MAX = 8


def pairs_shift(values, step, owners_n):
    return lax.ppermute(values, "pairs", [(i, (i + step) % owners_n) for i in range(owners_n)])


def swap(values, pairs):
    return lax.ppermute(values, "mp", pairs)


def mp_pairs(bit):
    n = 4
    return [(i, i ^ bit) for i in range(n)]


def mp_allreduce(term):
    if lax.axis_size("mp") != 4:
        return lax.psum(term.astype(jnp.float32), "mp")
    core = lax.axis_index("mp") % 2
    rows_n = term.shape[0]
    halves = term.reshape(2, rows_n // 2, term.shape[1])
    keep = jnp.where(core == 0, halves[0], halves[1])
    send = jnp.where(core == 0, halves[1], halves[0])
    got = swap(send, mp_pairs(1))
    chip_sum = (keep.astype(jnp.float32) + got.astype(jnp.float32)).astype(jnp.bfloat16)
    other = swap(chip_sum, mp_pairs(2))
    total = chip_sum.astype(jnp.float32) + other.astype(jnp.float32)
    rest = swap(total, mp_pairs(1))
    first = jnp.where(core == 0, total, rest)
    second = jnp.where(core == 0, rest, total)
    return jnp.concatenate([first, second], axis=0)


def mp_reduce_cols(term):
    if lax.axis_size("mp") != 4:
        full = lax.psum(term.astype(jnp.float32), "mp")
        quarter = term.shape[1] // lax.axis_size("mp")
        return lax.dynamic_slice_in_dim(full, lax.axis_index("mp") * quarter, quarter, 1)
    index = lax.axis_index("mp")
    rows_n, width = term.shape
    parts = term.reshape(rows_n, 4, width // 4)
    total = jnp.take(parts, index, axis=1).astype(jnp.float32)
    for bit in (1, 2, 3):
        total = total + swap(jnp.take(parts, index ^ bit, axis=1), mp_pairs(bit)).astype(jnp.float32)
    return total


def mp_gather_cols(part):
    if lax.axis_size("mp") != 4:
        return lax.all_gather(part, "mp", axis=2, tiled=True)
    index = lax.axis_index("mp")
    core = index % 2
    chip = index // 2
    got = swap(part, mp_pairs(1))
    pair = jnp.concatenate(
        [jnp.where(core == 0, part, got), jnp.where(core == 0, got, part)], axis=2
    )
    other = swap(pair, mp_pairs(2))
    return jnp.concatenate(
        [jnp.where(chip == 0, pair, other), jnp.where(chip == 0, other, pair)], axis=2
    )


def pairs_gather(payload, owners_n):
    if owners_n <= SHIFTS_MAX:
        return jnp.stack(
            [payload] + [pairs_shift(payload, step, owners_n) for step in range(1, owners_n)]
        )
    own = lax.axis_index("pairs")
    every = lax.all_gather(payload, "pairs", axis=0)
    return jnp.roll(every[::-1], own + 1, axis=0)


def pick_rows(onehot, values):
    shape = values.shape
    flat = values.reshape(shape[0], -1)
    picked = jnp.dot(onehot.astype(values.dtype), flat, preferred_element_type=jnp.float32)
    return picked.astype(values.dtype).reshape((onehot.shape[0],) + shape[1:])


def per_device(
    tokens,
    pair_list,
    confidence,
    gain_self,
    gain_query,
    gain_context,
    gain_mlp,
    self_qkv,
    self_out,
    cross_query,
    cross_kv,
    cross_out,
    mlp_up,
    mlp_down,
):
    quarter = tokens.shape[1]
    img_dev = tokens.shape[0] // TOKS
    pair_dev = pair_list.shape[0]
    views_n = 2 * pair_dev
    owners_n = lax.axis_size("pairs")
    own = lax.axis_index("pairs")

    extra_n = -(-(pair_dev + 1) // 8) * 8
    extra = jnp.concatenate(
        [
            jnp.pad(confidence, ((0, 0), (0, quarter - confidence.shape[1]))),
            jnp.pad(pair_list.reshape(1, views_n).astype(jnp.float32), ((0, 0), (0, quarter - views_n))),
            jnp.zeros((extra_n - pair_dev - 1, quarter), jnp.float32),
        ]
    )
    payload = jnp.concatenate([tokens.astype(jnp.float32), extra])
    table = pairs_gather(payload, owners_n)
    tok_rows = img_dev * TOKS
    all_tok = table[:, :tok_rows].astype(jnp.bfloat16).reshape(owners_n * img_dev, TOKS * quarter)
    all_conf = table[:, tok_rows : tok_rows + pair_dev, : 2 * TOKS].reshape(owners_n * views_n, TOKS)
    all_ids = table[:, tok_rows + pair_dev, :views_n].astype(jnp.int32)
    partner_ids = all_ids.reshape(owners_n, pair_dev, 2)[:, :, ::-1].reshape(-1)
    all_ids = all_ids.reshape(-1)

    mine = (all_ids // img_dev == own).astype(jnp.int32)
    rank = jnp.cumsum(mine) - 1
    choose = (mine[None, :] == 1) & (rank[None, :] == jnp.arange(views_n)[:, None])
    image = jnp.sum(jnp.where(choose, all_ids[None, :], 0), axis=1)
    other = jnp.sum(jnp.where(choose, partner_ids[None, :], 0), axis=1)
    conf = jnp.dot(choose.astype(jnp.float32), all_conf, precision=lax.Precision.HIGHEST)
    local = image % img_dev
    at = ((own - other // img_dev) % owners_n) * img_dev + other % img_dev
    far = (at[:, None] == jnp.arange(owners_n * img_dev)[None, :]).astype(jnp.bfloat16)
    context_q = pick_rows(far, all_tok).reshape(views_n, TOKS, quarter)

    own_tok = mp_gather_cols(tokens.reshape(img_dev, TOKS, quarter))
    width = own_tok.shape[2]
    img_rows = img_dev * TOKS
    begin = own_tok.astype(jnp.float32).reshape(img_rows, width)
    normed = layer_norm(begin, gain_self)
    qkv = jnp.einsum("rd,kdc->krc", normed, self_qkv, preferred_element_type=jnp.float32).astype(
        jnp.bfloat16
    )
    term = jnp.dot(
        attend(qkv[0], qkv[1], qkv[2], img_dev), self_out, preferred_element_type=jnp.float32
    )
    resid_img = begin + mp_allreduce(term.astype(jnp.bfloat16))
    normed = layer_norm(resid_img, gain_query)
    query_img = jnp.dot(normed, cross_query, preferred_element_type=jnp.float32).astype(
        jnp.bfloat16
    )

    rows_n = views_n * TOKS
    context = layer_norm(mp_gather_cols(context_q).astype(jnp.float32), gain_context).reshape(
        rows_n, width
    )
    keyval = jnp.einsum(
        "rd,kdc->krc", context, cross_kv, preferred_element_type=jnp.float32
    ).astype(jnp.bfloat16)
    near = (local[:, None] == jnp.arange(img_dev)[None, :]).astype(jnp.bfloat16)
    query = pick_rows(near, query_img.reshape(img_dev, TOKS, -1)).reshape(rows_n, -1)
    resid = jnp.take(resid_img.reshape(img_dev, TOKS, width), local, axis=0).reshape(
        rows_n, width
    )
    term = jnp.dot(
        attend(query, keyval[0], keyval[1], views_n), cross_out, preferred_element_type=jnp.float32
    )
    resid = resid + mp_allreduce(term.astype(jnp.bfloat16))
    normed = layer_norm(resid, gain_mlp)
    hidden = jax.nn.gelu(
        jnp.dot(normed, mlp_up, preferred_element_type=jnp.float32), approximate=False
    )
    term = jnp.dot(hidden.astype(jnp.bfloat16), mlp_down, preferred_element_type=jnp.float32)
    offset = lax.axis_index("mp") * quarter
    final = lax.dynamic_slice_in_dim(resid, offset, quarter, 1) + mp_reduce_cols(
        term.astype(jnp.bfloat16)
    )
    part = (final.reshape(views_n, TOKS, quarter) * conf[:, :, None]).astype(jnp.bfloat16)
    weight = conf.astype(jnp.bfloat16)
    owner_match = near.astype(jnp.float32).T
    numer = jnp.einsum(
        "iv,vtc->itc", owner_match, part.astype(jnp.float32), precision=lax.Precision.HIGHEST
    )
    denom = jnp.dot(owner_match, weight.astype(jnp.float32), precision=lax.Precision.HIGHEST)
    result = numer / jnp.maximum(denom, 1.0)[:, :, None]
    return result.astype(jnp.bfloat16).reshape(img_dev * TOKS, quarter)


def solution(mesh):
    return jax.shard_map(
        per_device,
        mesh=mesh,
        in_specs=(
            P(("groups", "pairs"), "mp"),
            P(("groups", "pairs"), None),
            P(("groups", "pairs"), None),
            P(),
            P(),
            P(),
            P(),
            P(None, None, "mp"),
            P("mp", None),
            P(None, "mp"),
            P(None, None, "mp"),
            P("mp", None),
            P(None, "mp"),
            P("mp", None),
        ),
        out_specs=P(("groups", "pairs"), "mp"),
        check_vma=False,
    )
```

```python
import jax
import jax.numpy as jnp
from jax import lax
from jax.sharding import PartitionSpec as P

HEAD = 64
TOKS = 32


EPSILON = 1e-06


def layer_norm(values, gain):
    center = values - jnp.mean(values, axis=-1, keepdims=True)
    spread = jnp.mean(center * center, axis=-1, keepdims=True)
    return (center * lax.rsqrt(spread + EPSILON) * gain).astype(jnp.bfloat16)


def attend(query, keys, values, views_n):
    rows_n, width = query.shape
    heads_n = width // HEAD
    qh = query.reshape(views_n, TOKS, heads_n, HEAD)
    kh = keys.reshape(views_n, TOKS, heads_n, HEAD)
    vh = values.reshape(views_n, TOKS, heads_n, HEAD)
    scores = jnp.einsum("vqhc,vkhc->vhqk", qh, kh, preferred_element_type=jnp.float32) * HEAD ** (
        -0.5
    )
    probs = jax.nn.softmax(scores, axis=-1).astype(jnp.bfloat16)
    mixed = jnp.einsum("vhqk,vkhc->vqhc", probs, vh, preferred_element_type=jnp.float32)
    return mixed.astype(jnp.bfloat16).reshape(rows_n, width)


SHIFTS_MAX = 8


def pairs_shift(values, step, owners_n):
    return lax.ppermute(values, "pairs", [(i, (i + step) % owners_n) for i in range(owners_n)])


def swap(values, pairs):
    return lax.ppermute(values, "mp", pairs)


def mp_pairs(bit):
    n = 4
    return [(i, i ^ bit) for i in range(n)]


def mp_allreduce(term):
    if lax.axis_size("mp") != 4:
        return lax.psum(term.astype(jnp.float32), "mp")
    core = lax.axis_index("mp") % 2
    rows_n = term.shape[0]
    halves = term.reshape(2, rows_n // 2, term.shape[1])
    keep = jnp.where(core == 0, halves[0], halves[1])
    send = jnp.where(core == 0, halves[1], halves[0])
    got = swap(send, mp_pairs(1))
    chip_sum = (keep.astype(jnp.float32) + got.astype(jnp.float32)).astype(jnp.bfloat16)
    other = swap(chip_sum, mp_pairs(2))
    total = chip_sum.astype(jnp.float32) + other.astype(jnp.float32)
    rest = swap(total, mp_pairs(1))
    first = jnp.where(core == 0, total, rest)
    second = jnp.where(core == 0, rest, total)
    return jnp.concatenate([first, second], axis=0)


def mp_reduce_cols(term):
    if lax.axis_size("mp") != 4:
        full = lax.psum(term.astype(jnp.float32), "mp")
        quarter = term.shape[1] // lax.axis_size("mp")
        return lax.dynamic_slice_in_dim(full, lax.axis_index("mp") * quarter, quarter, 1)
    index = lax.axis_index("mp")
    rows_n, width = term.shape
    parts = term.reshape(rows_n, 4, width // 4)
    total = jnp.take(parts, index, axis=1).astype(jnp.float32)
    for bit in (1, 2, 3):
        total = total + swap(jnp.take(parts, index ^ bit, axis=1), mp_pairs(bit)).astype(jnp.float32)
    return total


def mp_gather_cols(part):
    if lax.axis_size("mp") != 4:
        return lax.all_gather(part, "mp", axis=2, tiled=True)
    index = lax.axis_index("mp")
    core = index % 2
    chip = index // 2
    got = swap(part, mp_pairs(1))
    pair = jnp.where(
        core == 0, jnp.concatenate([part, got], axis=2), jnp.concatenate([got, part], axis=2)
    )
    other = swap(pair, mp_pairs(2))
    return jnp.where(
        chip == 0, jnp.concatenate([pair, other], axis=2), jnp.concatenate([other, pair], axis=2)
    )


def pairs_gather(payload, owners_n):
    if owners_n <= SHIFTS_MAX:
        return jnp.stack(
            [payload] + [pairs_shift(payload, step, owners_n) for step in range(1, owners_n)]
        )
    own = lax.axis_index("pairs")
    every = lax.all_gather(payload, "pairs", axis=0)
    return jnp.roll(every[::-1], own + 1, axis=0)


def pick_rows(onehot, values):
    shape = values.shape
    flat = values.reshape(shape[0], -1)
    picked = jnp.dot(onehot.astype(values.dtype), flat, preferred_element_type=jnp.float32)
    return picked.astype(values.dtype).reshape((onehot.shape[0],) + shape[1:])


def per_device(
    tokens,
    pair_list,
    confidence,
    gain_self,
    gain_query,
    gain_context,
    gain_mlp,
    self_qkv,
    self_out,
    cross_query,
    cross_kv,
    cross_out,
    mlp_up,
    mlp_down,
):
    quarter = tokens.shape[1]
    img_dev = tokens.shape[0] // TOKS
    pair_dev = pair_list.shape[0]
    views_n = 2 * pair_dev
    owners_n = lax.axis_size("pairs")
    own = lax.axis_index("pairs")

    own_tok = mp_gather_cols(tokens.reshape(img_dev, TOKS, quarter))
    width = own_tok.shape[2]
    img_rows = img_dev * TOKS

    high = confidence.astype(jnp.bfloat16)
    rest = confidence - high.astype(jnp.float32)
    mid = rest.astype(jnp.bfloat16)
    low = (rest - mid.astype(jnp.float32)).astype(jnp.bfloat16)
    extra_n = -(-(3 * pair_dev + 1) // 8) * 8
    conf_w = confidence.shape[1]
    extra = jnp.concatenate(
        [
            jnp.concatenate([high, mid, low], axis=0),
            pair_list.reshape(1, views_n).astype(jnp.bfloat16)
            if views_n == conf_w
            else jnp.pad(pair_list.reshape(1, views_n).astype(jnp.bfloat16), ((0, 0), (0, conf_w - views_n))),
            jnp.zeros((extra_n - 3 * pair_dev - 1, conf_w), jnp.bfloat16),
        ]
    )
    extra = jnp.pad(extra, ((0, 0), (0, width - conf_w)))
    payload = jnp.concatenate([own_tok.reshape(img_rows, width), extra])
    table = pairs_gather(payload, owners_n)
    all_tok = table[:, :img_rows].reshape(owners_n * img_dev, TOKS * width)
    pieces = table[:, img_rows : img_rows + 3 * pair_dev, :conf_w].astype(jnp.float32)
    pieces = pieces.reshape(owners_n, 3, pair_dev, conf_w)
    all_conf = (pieces[:, 0] + pieces[:, 1] + pieces[:, 2]).reshape(owners_n * views_n, TOKS)
    all_ids = table[:, img_rows + 3 * pair_dev, :views_n].astype(jnp.int32)
    partner_ids = all_ids.reshape(owners_n, pair_dev, 2)[:, :, ::-1].reshape(-1)
    all_ids = all_ids.reshape(-1)

    mine = (all_ids // img_dev == own).astype(jnp.int32)
    rank = jnp.cumsum(mine) - 1
    choose = (mine[None, :] == 1) & (rank[None, :] == jnp.arange(views_n)[:, None])
    image = jnp.sum(jnp.where(choose, all_ids[None, :], 0), axis=1)
    other = jnp.sum(jnp.where(choose, partner_ids[None, :], 0), axis=1)
    conf = jnp.dot(choose.astype(jnp.float32), all_conf, precision=lax.Precision.HIGHEST)
    local = image % img_dev
    at = ((own - other // img_dev) % owners_n) * img_dev + other % img_dev
    far = (at[:, None] == jnp.arange(owners_n * img_dev)[None, :]).astype(jnp.bfloat16)
    context_tok = pick_rows(far, all_tok).reshape(views_n, TOKS, width)

    begin = own_tok.astype(jnp.float32).reshape(img_rows, width)
    normed = layer_norm(begin, gain_self)
    qkv = jnp.einsum("rd,kdc->krc", normed, self_qkv, preferred_element_type=jnp.float32).astype(
        jnp.bfloat16
    )
    term = jnp.dot(
        attend(qkv[0], qkv[1], qkv[2], img_dev), self_out, preferred_element_type=jnp.float32
    )
    resid_img = begin + mp_allreduce(term.astype(jnp.bfloat16))
    normed = layer_norm(resid_img, gain_query)
    query_img = jnp.dot(normed, cross_query, preferred_element_type=jnp.float32).astype(
        jnp.bfloat16
    )

    rows_n = views_n * TOKS
    context = layer_norm(context_tok.astype(jnp.float32), gain_context).reshape(rows_n, width)
    keyval = jnp.einsum(
        "rd,kdc->krc", context, cross_kv, preferred_element_type=jnp.float32
    ).astype(jnp.bfloat16)
    near = (local[:, None] == jnp.arange(img_dev)[None, :]).astype(jnp.bfloat16)
    query = pick_rows(near, query_img.reshape(img_dev, TOKS, -1)).reshape(rows_n, -1)
    resid = jnp.take(resid_img.reshape(img_dev, TOKS, width), local, axis=0).reshape(
        rows_n, width
    )
    term = jnp.dot(
        attend(query, keyval[0], keyval[1], views_n), cross_out, preferred_element_type=jnp.float32
    )
    resid = resid + mp_allreduce(term.astype(jnp.bfloat16))
    normed = layer_norm(resid, gain_mlp)
    hidden = jax.nn.gelu(
        jnp.dot(normed, mlp_up, preferred_element_type=jnp.float32), approximate=False
    )
    term = jnp.dot(hidden.astype(jnp.bfloat16), mlp_down, preferred_element_type=jnp.float32)
    offset = lax.axis_index("mp") * quarter
    final = lax.dynamic_slice_in_dim(resid, offset, quarter, 1) + mp_reduce_cols(
        term.astype(jnp.bfloat16)
    )
    part = (final.reshape(views_n, TOKS, quarter) * conf[:, :, None]).astype(jnp.bfloat16)
    weight = conf.astype(jnp.bfloat16)
    owner_match = near.astype(jnp.float32).T
    numer = jnp.einsum(
        "iv,vtc->itc", owner_match, part.astype(jnp.float32), precision=lax.Precision.HIGHEST
    )
    denom = jnp.dot(owner_match, weight.astype(jnp.float32), precision=lax.Precision.HIGHEST)
    result = numer / jnp.maximum(denom, 1.0)[:, :, None]
    return result.astype(jnp.bfloat16).reshape(img_dev * TOKS, quarter)


def solution(mesh):
    return jax.shard_map(
        per_device,
        mesh=mesh,
        in_specs=(
            P(("groups", "pairs"), "mp"),
            P(("groups", "pairs"), None),
            P(("groups", "pairs"), None),
            P(),
            P(),
            P(),
            P(),
            P(None, None, "mp"),
            P("mp", None),
            P(None, "mp"),
            P(None, None, "mp"),
            P("mp", None),
            P(None, "mp"),
            P("mp", None),
        ),
        out_specs=P(("groups", "pairs"), "mp"),
        check_vma=False,
    )
```

```python
import jax
import jax.numpy as jnp
from jax import lax
from jax.sharding import PartitionSpec as P

HEAD = 64
TOKS = 32


EPSILON = 1e-06


def layer_norm(values, gain):
    center = values - jnp.mean(values, axis=-1, keepdims=True)
    spread = jnp.mean(center * center, axis=-1, keepdims=True)
    return (center * lax.rsqrt(spread + EPSILON) * gain).astype(jnp.bfloat16)


def attend(query, keys, values, views_n):
    rows_n, width = query.shape
    heads_n = width // HEAD
    qh = query.reshape(views_n, TOKS, heads_n, HEAD)
    kh = keys.reshape(views_n, TOKS, heads_n, HEAD)
    vh = values.reshape(views_n, TOKS, heads_n, HEAD)
    scores = jnp.einsum("vqhc,vkhc->vhqk", qh, kh, preferred_element_type=jnp.float32) * HEAD ** (
        -0.5
    )
    probs = jax.nn.softmax(scores, axis=-1).astype(jnp.bfloat16)
    mixed = jnp.einsum("vhqk,vkhc->vqhc", probs, vh, preferred_element_type=jnp.float32)
    return mixed.astype(jnp.bfloat16).reshape(rows_n, width)


SHIFTS_MAX = 8


def pairs_shift(values, step, owners_n):
    return lax.ppermute(values, "pairs", [(i, (i + step) % owners_n) for i in range(owners_n)])


def layer_norm_quarters(values, gain):
    center = values - jnp.mean(values, axis=(0, 2), keepdims=True)
    spread = jnp.mean(center * center, axis=(0, 2), keepdims=True)
    gain = gain.reshape(values.shape[0], 1, values.shape[2])
    return (center * lax.rsqrt(spread + EPSILON) * gain).astype(jnp.bfloat16)


def mp_gather_major(part):
    if lax.axis_size("mp") != 4:
        return lax.all_gather(part, "mp", axis=0)
    index = lax.axis_index("mp")
    core = index % 2
    chip = index // 2
    got = swap(part, mp_pairs(1))
    pair = jnp.stack([jnp.where(core == 0, part, got), jnp.where(core == 0, got, part)])
    other = swap(pair, mp_pairs(2))
    return jnp.concatenate([jnp.where(chip == 0, pair, other), jnp.where(chip == 0, other, pair)])


def swap(values, pairs):
    return lax.ppermute(values, "mp", pairs)


def mp_pairs(bit):
    n = 4
    return [(i, i ^ bit) for i in range(n)]


def mp_allreduce(term):
    if lax.axis_size("mp") != 4:
        return lax.psum(term.astype(jnp.float32), "mp")
    core = lax.axis_index("mp") % 2
    rows_n = term.shape[0]
    halves = term.reshape(2, rows_n // 2, term.shape[1])
    keep = jnp.where(core == 0, halves[0], halves[1])
    send = jnp.where(core == 0, halves[1], halves[0])
    got = swap(send, mp_pairs(1))
    chip_sum = (keep.astype(jnp.float32) + got.astype(jnp.float32)).astype(jnp.bfloat16)
    other = swap(chip_sum, mp_pairs(2))
    total = chip_sum.astype(jnp.float32) + other.astype(jnp.float32)
    rest = swap(total, mp_pairs(1))
    first = jnp.where(core == 0, total, rest)
    second = jnp.where(core == 0, rest, total)
    return jnp.concatenate([first, second], axis=0)


def mp_reduce_cols(term):
    if lax.axis_size("mp") != 4:
        full = lax.psum(term.astype(jnp.float32), "mp")
        quarter = term.shape[1] // lax.axis_size("mp")
        return lax.dynamic_slice_in_dim(full, lax.axis_index("mp") * quarter, quarter, 1)
    index = lax.axis_index("mp")
    rows_n, width = term.shape
    parts = term.reshape(rows_n, 4, width // 4)
    total = jnp.take(parts, index, axis=1).astype(jnp.float32)
    for bit in (1, 2, 3):
        total = total + swap(jnp.take(parts, index ^ bit, axis=1), mp_pairs(bit)).astype(jnp.float32)
    return total


def mp_gather_cols(part):
    if lax.axis_size("mp") != 4:
        return lax.all_gather(part, "mp", axis=2, tiled=True)
    index = lax.axis_index("mp")
    core = index % 2
    chip = index // 2
    got = swap(part, mp_pairs(1))
    pair = jnp.where(
        core == 0, jnp.concatenate([part, got], axis=2), jnp.concatenate([got, part], axis=2)
    )
    other = swap(pair, mp_pairs(2))
    return jnp.where(
        chip == 0, jnp.concatenate([pair, other], axis=2), jnp.concatenate([other, pair], axis=2)
    )


def pairs_gather(payload, owners_n):
    if owners_n <= SHIFTS_MAX:
        return jnp.stack(
            [payload] + [pairs_shift(payload, step, owners_n) for step in range(1, owners_n)]
        )
    own = lax.axis_index("pairs")
    every = lax.all_gather(payload, "pairs", axis=0)
    return jnp.roll(every[::-1], own + 1, axis=0)


def pick_rows(onehot, values):
    shape = values.shape
    flat = values.reshape(shape[0], -1)
    picked = jnp.dot(onehot.astype(values.dtype), flat, preferred_element_type=jnp.float32)
    return picked.astype(values.dtype).reshape((onehot.shape[0],) + shape[1:])


def per_device(
    tokens,
    pair_list,
    confidence,
    gain_self,
    gain_query,
    gain_context,
    gain_mlp,
    self_qkv,
    self_out,
    cross_query,
    cross_kv,
    cross_out,
    mlp_up,
    mlp_down,
):
    quarter = tokens.shape[1]
    img_dev = tokens.shape[0] // TOKS
    pair_dev = pair_list.shape[0]
    views_n = 2 * pair_dev
    owners_n = lax.axis_size("pairs")
    own = lax.axis_index("pairs")

    img_rows = img_dev * TOKS
    own_tok = mp_gather_major(tokens)
    parts_n = own_tok.shape[0]
    width = parts_n * quarter

    payload = jnp.concatenate(
        [
            tokens.astype(jnp.float32).reshape(-1),
            pair_list.astype(jnp.float32).reshape(-1),
            confidence.reshape(-1),
        ]
    )
    payload, own_tok = lax.optimization_barrier((payload, own_tok))
    table = pairs_gather(payload, owners_n)
    cut_tok = img_dev * TOKS * quarter
    cut_ids = cut_tok + views_n
    all_tok = table[:, :cut_tok].astype(jnp.bfloat16).reshape(owners_n * img_dev, TOKS * quarter)
    all_ids = table[:, cut_tok:cut_ids].astype(jnp.int32)
    all_conf = table[:, cut_ids:].reshape(owners_n * views_n, TOKS)
    partner_ids = all_ids.reshape(owners_n, pair_dev, 2)[:, :, ::-1].reshape(-1)
    all_ids = all_ids.reshape(-1)

    mine = (all_ids // img_dev == own).astype(jnp.int32)
    rank = jnp.cumsum(mine) - 1
    choose = (mine[None, :] == 1) & (rank[None, :] == jnp.arange(views_n)[:, None])
    image = jnp.sum(jnp.where(choose, all_ids[None, :], 0), axis=1)
    other = jnp.sum(jnp.where(choose, partner_ids[None, :], 0), axis=1)
    conf = jnp.dot(choose.astype(jnp.float32), all_conf, precision=lax.Precision.HIGHEST)
    local = image % img_dev
    at = ((own - other // img_dev) % owners_n) * img_dev + other % img_dev
    far = (at[:, None] == jnp.arange(owners_n * img_dev)[None, :]).astype(jnp.bfloat16)
    context_q = pick_rows(far, all_tok).reshape(views_n * TOKS, quarter)

    begin = jnp.transpose(own_tok, (1, 0, 2)).reshape(img_rows, width).astype(jnp.float32)
    normed = layer_norm_quarters(own_tok.astype(jnp.float32), gain_self)
    qkv = jnp.einsum(
        "qrd,kqdc->krc",
        normed,
        self_qkv.reshape(3, parts_n, quarter, -1),
        preferred_element_type=jnp.float32,
    ).astype(jnp.bfloat16)
    term = jnp.dot(
        attend(qkv[0], qkv[1], qkv[2], img_dev), self_out, preferred_element_type=jnp.float32
    )
    resid_img = begin + mp_allreduce(term.astype(jnp.bfloat16))
    normed = layer_norm(resid_img, gain_query)
    query_img = jnp.dot(normed, cross_query, preferred_element_type=jnp.float32).astype(
        jnp.bfloat16
    )

    rows_n = views_n * TOKS
    context = layer_norm_quarters(mp_gather_major(context_q).astype(jnp.float32), gain_context)
    keyval = jnp.einsum(
        "qrd,kqdc->krc",
        context,
        cross_kv.reshape(2, parts_n, quarter, -1),
        preferred_element_type=jnp.float32,
    ).astype(jnp.bfloat16)
    near = (local[:, None] == jnp.arange(img_dev)[None, :]).astype(jnp.bfloat16)
    query = pick_rows(near, query_img.reshape(img_dev, TOKS, -1)).reshape(rows_n, -1)
    resid = jnp.take(resid_img.reshape(img_dev, TOKS, width), local, axis=0).reshape(
        rows_n, width
    )
    term = jnp.dot(
        attend(query, keyval[0], keyval[1], views_n), cross_out, preferred_element_type=jnp.float32
    )
    resid = resid + mp_allreduce(term.astype(jnp.bfloat16))
    normed = layer_norm(resid, gain_mlp)
    hidden = jax.nn.gelu(
        jnp.dot(normed, mlp_up, preferred_element_type=jnp.float32), approximate=False
    )
    term = jnp.dot(hidden.astype(jnp.bfloat16), mlp_down, preferred_element_type=jnp.float32)
    offset = lax.axis_index("mp") * quarter
    final = lax.dynamic_slice_in_dim(resid, offset, quarter, 1) + mp_reduce_cols(
        term.astype(jnp.bfloat16)
    )
    part = (final.reshape(views_n, TOKS, quarter) * conf[:, :, None]).astype(jnp.bfloat16)
    weight = conf.astype(jnp.bfloat16)
    owner_match = near.astype(jnp.float32).T
    numer = jnp.einsum(
        "iv,vtc->itc", owner_match, part.astype(jnp.float32), precision=lax.Precision.HIGHEST
    )
    denom = jnp.dot(owner_match, weight.astype(jnp.float32), precision=lax.Precision.HIGHEST)
    result = numer / jnp.maximum(denom, 1.0)[:, :, None]
    return result.astype(jnp.bfloat16).reshape(img_dev * TOKS, quarter)


def solution(mesh):
    return jax.shard_map(
        per_device,
        mesh=mesh,
        in_specs=(
            P(("groups", "pairs"), "mp"),
            P(("groups", "pairs"), None),
            P(("groups", "pairs"), None),
            P(),
            P(),
            P(),
            P(),
            P(None, None, "mp"),
            P("mp", None),
            P(None, "mp"),
            P(None, None, "mp"),
            P("mp", None),
            P(None, "mp"),
            P("mp", None),
        ),
        out_specs=P(("groups", "pairs"), "mp"),
        check_vma=False,
    )
```

```python
import jax
import jax.numpy as jnp
from jax import lax
from jax.sharding import PartitionSpec as P

HEAD = 64
TOKS = 32


EPSILON = 1e-06


def layer_norm(values, gain):
    center = values - jnp.mean(values, axis=-1, keepdims=True)
    spread = jnp.mean(center * center, axis=-1, keepdims=True)
    return (center * lax.rsqrt(spread + EPSILON) * gain).astype(jnp.bfloat16)


def attend(query, keys, values, views_n):
    rows_n, width = query.shape
    heads_n = width // HEAD
    qh = query.reshape(views_n, TOKS, heads_n, HEAD)
    kh = keys.reshape(views_n, TOKS, heads_n, HEAD)
    vh = values.reshape(views_n, TOKS, heads_n, HEAD)
    scores = jnp.einsum("vqhc,vkhc->vhqk", qh, kh, preferred_element_type=jnp.float32) * HEAD ** (
        -0.5
    )
    probs = jax.nn.softmax(scores, axis=-1).astype(jnp.bfloat16)
    mixed = jnp.einsum("vhqk,vkhc->vqhc", probs, vh, preferred_element_type=jnp.float32)
    return mixed.astype(jnp.bfloat16).reshape(rows_n, width)


SHIFTS_MAX = 8


def pairs_shift(values, step, owners_n):
    return lax.ppermute(values, "pairs", [(i, (i + step) % owners_n) for i in range(owners_n)])


def swap(values, pairs):
    return lax.ppermute(values, "mp", pairs)


def mp_pairs(bit):
    n = 4
    return [(i, i ^ bit) for i in range(n)]


def mp_allreduce(term):
    if lax.axis_size("mp") != 4:
        return lax.psum(term.astype(jnp.float32), "mp")
    core = lax.axis_index("mp") % 2
    rows_n = term.shape[0]
    halves = term.reshape(2, rows_n // 2, term.shape[1])
    keep = jnp.where(core == 0, halves[0], halves[1])
    send = jnp.where(core == 0, halves[1], halves[0])
    got = swap(send, mp_pairs(1))
    chip_sum = (keep.astype(jnp.float32) + got.astype(jnp.float32)).astype(jnp.bfloat16)
    other = swap(chip_sum, mp_pairs(2))
    total = chip_sum.astype(jnp.float32) + other.astype(jnp.float32)
    rest = swap(total, mp_pairs(1))
    first = jnp.where(core == 0, total, rest)
    second = jnp.where(core == 0, rest, total)
    return jnp.concatenate([first, second], axis=0)


def mp_reduce_cols(term):
    if lax.axis_size("mp") != 4:
        full = lax.psum(term.astype(jnp.float32), "mp")
        quarter = term.shape[1] // lax.axis_size("mp")
        return lax.dynamic_slice_in_dim(full, lax.axis_index("mp") * quarter, quarter, 1)
    index = lax.axis_index("mp")
    rows_n, width = term.shape
    parts = term.reshape(rows_n, 4, width // 4)
    total = jnp.take(parts, index, axis=1).astype(jnp.float32)
    for bit in (1, 2, 3):
        total = total + swap(jnp.take(parts, index ^ bit, axis=1), mp_pairs(bit)).astype(jnp.float32)
    return total


def mp_gather_cols(part):
    if lax.axis_size("mp") != 4:
        return lax.all_gather(part, "mp", axis=2, tiled=True)
    index = lax.axis_index("mp")
    core = index % 2
    chip = index // 2
    got = swap(part, mp_pairs(1))
    pair = jnp.where(
        core == 0, jnp.concatenate([part, got], axis=2), jnp.concatenate([got, part], axis=2)
    )
    other = swap(pair, mp_pairs(2))
    return jnp.where(
        chip == 0, jnp.concatenate([pair, other], axis=2), jnp.concatenate([other, pair], axis=2)
    )


def pairs_gather(payload, owners_n):
    if owners_n <= SHIFTS_MAX:
        return jnp.stack(
            [payload] + [pairs_shift(payload, step, owners_n) for step in range(1, owners_n)]
        )
    own = lax.axis_index("pairs")
    every = lax.all_gather(payload, "pairs", axis=0)
    return jnp.roll(every[::-1], own + 1, axis=0)


def pick_rows(onehot, values):
    shape = values.shape
    flat = values.reshape(shape[0], -1)
    picked = jnp.dot(onehot.astype(values.dtype), flat, preferred_element_type=jnp.float32)
    return picked.astype(values.dtype).reshape((onehot.shape[0],) + shape[1:])


def per_device(
    tokens,
    pair_list,
    confidence,
    gain_self,
    gain_query,
    gain_context,
    gain_mlp,
    self_qkv,
    self_out,
    cross_query,
    cross_kv,
    cross_out,
    mlp_up,
    mlp_down,
):
    quarter = tokens.shape[1]
    img_dev = tokens.shape[0] // TOKS
    pair_dev = pair_list.shape[0]
    views_n = 2 * pair_dev
    owners_n = lax.axis_size("pairs")
    own = lax.axis_index("pairs")

    payload = jnp.concatenate(
        [
            tokens.astype(jnp.float32).reshape(-1),
            pair_list.astype(jnp.float32).reshape(-1),
            confidence.reshape(-1),
        ]
    )
    own_tok = mp_gather_cols(tokens.reshape(img_dev, TOKS, quarter))
    payload, own_tok = lax.optimization_barrier((payload, own_tok))
    table = pairs_gather(payload, owners_n)
    cut_tok = img_dev * TOKS * quarter
    cut_ids = cut_tok + views_n
    all_tok = table[:, :cut_tok].astype(jnp.bfloat16).reshape(owners_n * img_dev, TOKS * quarter)
    all_ids = table[:, cut_tok:cut_ids].astype(jnp.int32)
    all_conf = table[:, cut_ids:].reshape(owners_n * views_n, TOKS)
    partner_ids = all_ids.reshape(owners_n, pair_dev, 2)[:, :, ::-1].reshape(-1)
    all_ids = all_ids.reshape(-1)

    mine = (all_ids // img_dev == own).astype(jnp.int32)
    rank = jnp.cumsum(mine) - 1
    choose = (mine[None, :] == 1) & (rank[None, :] == jnp.arange(views_n)[:, None])
    image = jnp.sum(jnp.where(choose, all_ids[None, :], 0), axis=1)
    other = jnp.sum(jnp.where(choose, partner_ids[None, :], 0), axis=1)
    conf = jnp.dot(choose.astype(jnp.float32), all_conf, precision=lax.Precision.HIGHEST)
    local = image % img_dev
    at = ((own - other // img_dev) % owners_n) * img_dev + other % img_dev
    far = (at[:, None] == jnp.arange(owners_n * img_dev)[None, :]).astype(jnp.bfloat16)
    context_q = pick_rows(far, all_tok).reshape(views_n, TOKS, quarter)

    width = own_tok.shape[2]
    img_rows = img_dev * TOKS
    begin = own_tok.astype(jnp.float32).reshape(img_rows, width)
    normed = layer_norm(begin, gain_self)
    qkv = jnp.einsum("rd,kdc->krc", normed, self_qkv, preferred_element_type=jnp.float32).astype(
        jnp.bfloat16
    )
    term = jnp.dot(
        attend(qkv[0], qkv[1], qkv[2], img_dev), self_out, preferred_element_type=jnp.float32
    )
    resid_img = begin + mp_allreduce(term.astype(jnp.bfloat16))
    normed = layer_norm(resid_img, gain_query)
    query_img = jnp.dot(normed, cross_query, preferred_element_type=jnp.float32).astype(
        jnp.bfloat16
    )

    rows_n = views_n * TOKS
    context = layer_norm(mp_gather_cols(context_q).astype(jnp.float32), gain_context).reshape(
        rows_n, width
    )
    keyval = jnp.einsum(
        "rd,kdc->krc", context, cross_kv, preferred_element_type=jnp.float32
    ).astype(jnp.bfloat16)
    near = (local[:, None] == jnp.arange(img_dev)[None, :]).astype(jnp.bfloat16)
    query = pick_rows(near, query_img.reshape(img_dev, TOKS, -1)).reshape(rows_n, -1)
    resid = jnp.take(resid_img.reshape(img_dev, TOKS, width), local, axis=0).reshape(
        rows_n, width
    )
    term = jnp.dot(
        attend(query, keyval[0], keyval[1], views_n), cross_out, preferred_element_type=jnp.float32
    )
    resid = resid + mp_allreduce(term.astype(jnp.bfloat16))
    normed = layer_norm(resid, gain_mlp)
    hidden = jax.nn.gelu(
        jnp.dot(normed, mlp_up, preferred_element_type=jnp.float32), approximate=False
    )
    term = jnp.dot(hidden.astype(jnp.bfloat16), mlp_down, preferred_element_type=jnp.float32)
    offset = lax.axis_index("mp") * quarter
    final = lax.dynamic_slice_in_dim(resid, offset, quarter, 1) + mp_reduce_cols(
        term.astype(jnp.bfloat16)
    )
    part = (final.reshape(views_n, TOKS, quarter) * conf[:, :, None]).astype(jnp.bfloat16)
    weight = conf.astype(jnp.bfloat16)
    owner_match = near.astype(jnp.float32).T
    numer = jnp.einsum(
        "iv,vtc->itc", owner_match, part.astype(jnp.float32), precision=lax.Precision.HIGHEST
    )
    denom = jnp.dot(owner_match, weight.astype(jnp.float32), precision=lax.Precision.HIGHEST)
    result = numer / jnp.maximum(denom, 1.0)[:, :, None]
    return result.astype(jnp.bfloat16).reshape(img_dev * TOKS, quarter)


def solution(mesh):
    return jax.shard_map(
        per_device,
        mesh=mesh,
        in_specs=(
            P(("groups", "pairs"), "mp"),
            P(("groups", "pairs"), None),
            P(("groups", "pairs"), None),
            P(),
            P(),
            P(),
            P(),
            P(None, None, "mp"),
            P("mp", None),
            P(None, "mp"),
            P(None, None, "mp"),
            P("mp", None),
            P(None, "mp"),
            P("mp", None),
        ),
        out_specs=P(("groups", "pairs"), "mp"),
        check_vma=False,
    )
```

```python
import jax
import jax.numpy as jnp
from jax import lax
from jax.sharding import PartitionSpec as P

HEAD = 64
TOKS = 32


EPSILON = 1e-06


def layer_norm(values, gain):
    center = values - jnp.mean(values, axis=-1, keepdims=True)
    spread = jnp.mean(center * center, axis=-1, keepdims=True)
    return (center * lax.rsqrt(spread + EPSILON) * gain).astype(jnp.bfloat16)


def attend(query, keys, values, views_n):
    rows_n, width = query.shape
    heads_n = width // HEAD
    qh = query.reshape(views_n, TOKS, heads_n, HEAD)
    kh = keys.reshape(views_n, TOKS, heads_n, HEAD)
    vh = values.reshape(views_n, TOKS, heads_n, HEAD)
    scores = jnp.einsum("vqhc,vkhc->vhqk", qh, kh, preferred_element_type=jnp.float32) * HEAD ** (
        -0.5
    )
    probs = jax.nn.softmax(scores, axis=-1).astype(jnp.bfloat16)
    mixed = jnp.einsum("vhqk,vkhc->vqhc", probs, vh, preferred_element_type=jnp.float32)
    return mixed.astype(jnp.bfloat16).reshape(rows_n, width)


SHIFTS_MAX = 8


def pairs_shift(values, step, owners_n):
    return lax.ppermute(values, "pairs", [(i, (i + step) % owners_n) for i in range(owners_n)])


def swap(values, pairs):
    return lax.ppermute(values, "mp", pairs)


def mp_pairs(bit):
    n = 4
    return [(i, i ^ bit) for i in range(n)]


def mp_allreduce(term):
    if lax.axis_size("mp") != 4:
        return lax.psum(term.astype(jnp.float32), "mp")
    core = lax.axis_index("mp") % 2
    rows_n = term.shape[0]
    halves = term.reshape(2, rows_n // 2, term.shape[1])
    keep = jnp.where(core == 0, halves[0], halves[1])
    send = jnp.where(core == 0, halves[1], halves[0])
    got = swap(send, mp_pairs(1))
    chip_sum = (keep.astype(jnp.float32) + got.astype(jnp.float32)).astype(jnp.bfloat16)
    other = swap(chip_sum, mp_pairs(2))
    total = chip_sum.astype(jnp.float32) + other.astype(jnp.float32)
    rest = swap(total, mp_pairs(1))
    first = jnp.where(core == 0, total, rest)
    second = jnp.where(core == 0, rest, total)
    return jnp.concatenate([first, second], axis=0)


def mp_reduce_cols(term):
    if lax.axis_size("mp") != 4:
        full = lax.psum(term.astype(jnp.float32), "mp")
        quarter = term.shape[1] // lax.axis_size("mp")
        return lax.dynamic_slice_in_dim(full, lax.axis_index("mp") * quarter, quarter, 1)
    index = lax.axis_index("mp")
    rows_n, width = term.shape
    parts = term.reshape(rows_n, 4, width // 4)
    total = jnp.take(parts, index, axis=1).astype(jnp.float32)
    for bit in (1, 2, 3):
        total = total + swap(jnp.take(parts, index ^ bit, axis=1), mp_pairs(bit)).astype(jnp.float32)
    return total


def mp_gather_cols(part):
    if lax.axis_size("mp") != 4:
        return lax.all_gather(part, "mp", axis=2, tiled=True)
    index = lax.axis_index("mp")
    moved = [part] + [swap(part, mp_pairs(bit)) for bit in (1, 2, 3)]
    placed = []
    for q in range(4):
        rel = index ^ q
        piece = jnp.where(rel == 0, moved[0], moved[1])
        piece = jnp.where(rel == 2, moved[2], piece)
        placed.append(jnp.where(rel == 3, moved[3], piece))
    return jnp.concatenate(placed, axis=2)


def pairs_gather(payload, owners_n):
    if owners_n <= SHIFTS_MAX:
        return jnp.stack(
            [payload] + [pairs_shift(payload, step, owners_n) for step in range(1, owners_n)]
        )
    own = lax.axis_index("pairs")
    every = lax.all_gather(payload, "pairs", axis=0)
    return jnp.roll(every[::-1], own + 1, axis=0)


def pick_rows(onehot, values):
    shape = values.shape
    flat = values.reshape(shape[0], -1)
    picked = jnp.dot(onehot.astype(values.dtype), flat, preferred_element_type=jnp.float32)
    return picked.astype(values.dtype).reshape((onehot.shape[0],) + shape[1:])


def per_device(
    tokens,
    pair_list,
    confidence,
    gain_self,
    gain_query,
    gain_context,
    gain_mlp,
    self_qkv,
    self_out,
    cross_query,
    cross_kv,
    cross_out,
    mlp_up,
    mlp_down,
):
    quarter = tokens.shape[1]
    img_dev = tokens.shape[0] // TOKS
    pair_dev = pair_list.shape[0]
    views_n = 2 * pair_dev
    owners_n = lax.axis_size("pairs")
    own = lax.axis_index("pairs")

    payload = jnp.concatenate(
        [
            tokens.astype(jnp.float32).reshape(-1),
            pair_list.astype(jnp.float32).reshape(-1),
            confidence.reshape(-1),
        ]
    )
    table = pairs_gather(payload, owners_n)
    cut_tok = img_dev * TOKS * quarter
    cut_ids = cut_tok + views_n
    all_tok = table[:, :cut_tok].astype(jnp.bfloat16).reshape(owners_n * img_dev, TOKS * quarter)
    all_ids = table[:, cut_tok:cut_ids].astype(jnp.int32)
    all_conf = table[:, cut_ids:].reshape(owners_n * views_n, TOKS)
    partner_ids = all_ids.reshape(owners_n, pair_dev, 2)[:, :, ::-1].reshape(-1)
    all_ids = all_ids.reshape(-1)

    mine = (all_ids // img_dev == own).astype(jnp.int32)
    rank = jnp.cumsum(mine) - 1
    choose = (mine[None, :] == 1) & (rank[None, :] == jnp.arange(views_n)[:, None])
    image = jnp.sum(jnp.where(choose, all_ids[None, :], 0), axis=1)
    other = jnp.sum(jnp.where(choose, partner_ids[None, :], 0), axis=1)
    conf = jnp.dot(choose.astype(jnp.float32), all_conf, precision=lax.Precision.HIGHEST)
    local = image % img_dev
    at = ((own - other // img_dev) % owners_n) * img_dev + other % img_dev
    far = (at[:, None] == jnp.arange(owners_n * img_dev)[None, :]).astype(jnp.bfloat16)
    context_q = pick_rows(far, all_tok).reshape(views_n, TOKS, quarter)

    own_tok = mp_gather_cols(tokens.reshape(img_dev, TOKS, quarter))
    width = own_tok.shape[2]
    img_rows = img_dev * TOKS
    begin = own_tok.astype(jnp.float32).reshape(img_rows, width)
    normed = layer_norm(begin, gain_self)
    qkv = jnp.einsum("rd,kdc->krc", normed, self_qkv, preferred_element_type=jnp.float32).astype(
        jnp.bfloat16
    )
    term = jnp.dot(
        attend(qkv[0], qkv[1], qkv[2], img_dev), self_out, preferred_element_type=jnp.float32
    )
    resid_img = begin + mp_allreduce(term.astype(jnp.bfloat16))
    normed = layer_norm(resid_img, gain_query)
    query_img = jnp.dot(normed, cross_query, preferred_element_type=jnp.float32).astype(
        jnp.bfloat16
    )

    rows_n = views_n * TOKS
    context = layer_norm(mp_gather_cols(context_q).astype(jnp.float32), gain_context).reshape(
        rows_n, width
    )
    keyval = jnp.einsum(
        "rd,kdc->krc", context, cross_kv, preferred_element_type=jnp.float32
    ).astype(jnp.bfloat16)
    near = (local[:, None] == jnp.arange(img_dev)[None, :]).astype(jnp.bfloat16)
    query = pick_rows(near, query_img.reshape(img_dev, TOKS, -1)).reshape(rows_n, -1)
    resid = jnp.take(resid_img.reshape(img_dev, TOKS, width), local, axis=0).reshape(
        rows_n, width
    )
    term = jnp.dot(
        attend(query, keyval[0], keyval[1], views_n), cross_out, preferred_element_type=jnp.float32
    )
    resid = resid + mp_allreduce(term.astype(jnp.bfloat16))
    normed = layer_norm(resid, gain_mlp)
    hidden = jax.nn.gelu(
        jnp.dot(normed, mlp_up, preferred_element_type=jnp.float32), approximate=False
    )
    term = jnp.dot(hidden.astype(jnp.bfloat16), mlp_down, preferred_element_type=jnp.float32)
    offset = lax.axis_index("mp") * quarter
    final = lax.dynamic_slice_in_dim(resid, offset, quarter, 1) + mp_reduce_cols(
        term.astype(jnp.bfloat16)
    )
    part = (final.reshape(views_n, TOKS, quarter) * conf[:, :, None]).astype(jnp.bfloat16)
    weight = conf.astype(jnp.bfloat16)
    owner_match = near.astype(jnp.float32).T
    numer = jnp.einsum(
        "iv,vtc->itc", owner_match, part.astype(jnp.float32), precision=lax.Precision.HIGHEST
    )
    denom = jnp.dot(owner_match, weight.astype(jnp.float32), precision=lax.Precision.HIGHEST)
    result = numer / jnp.maximum(denom, 1.0)[:, :, None]
    return result.astype(jnp.bfloat16).reshape(img_dev * TOKS, quarter)


def solution(mesh):
    return jax.shard_map(
        per_device,
        mesh=mesh,
        in_specs=(
            P(("groups", "pairs"), "mp"),
            P(("groups", "pairs"), None),
            P(("groups", "pairs"), None),
            P(),
            P(),
            P(),
            P(),
            P(None, None, "mp"),
            P("mp", None),
            P(None, "mp"),
            P(None, None, "mp"),
            P("mp", None),
            P(None, "mp"),
            P("mp", None),
        ),
        out_specs=P(("groups", "pairs"), "mp"),
        check_vma=False,
    )
```

```python
import jax
import jax.numpy as jnp
from jax import lax
from jax.sharding import PartitionSpec as P

HEAD = 64
TOKS = 32


EPSILON = 1e-06


def layer_norm(values, gain):
    center = values - jnp.mean(values, axis=-1, keepdims=True)
    spread = jnp.mean(center * center, axis=-1, keepdims=True)
    return (center * lax.rsqrt(spread + EPSILON) * gain).astype(jnp.bfloat16)


def attend(query, keys, values, views_n):
    rows_n, width = query.shape
    heads_n = width // HEAD
    qh = query.reshape(views_n, TOKS, heads_n, HEAD)
    kh = keys.reshape(views_n, TOKS, heads_n, HEAD)
    vh = values.reshape(views_n, TOKS, heads_n, HEAD)
    scores = jnp.einsum("vqhc,vkhc->vhqk", qh, kh, preferred_element_type=jnp.float32) * HEAD ** (
        -0.5
    )
    probs = jax.nn.softmax(scores, axis=-1).astype(jnp.bfloat16)
    mixed = jnp.einsum("vhqk,vkhc->vqhc", probs, vh, preferred_element_type=jnp.float32)
    return mixed.astype(jnp.bfloat16).reshape(rows_n, width)


SHIFTS_MAX = 8


def pairs_shift(values, step, owners_n):
    return lax.ppermute(values, "pairs", [(i, (i + step) % owners_n) for i in range(owners_n)])


def swap(values, pairs):
    return lax.ppermute(values, "mp", pairs)


def mp_pairs(bit):
    n = 4
    return [(i, i ^ bit) for i in range(n)]


def mp_allreduce(term):
    if lax.axis_size("mp") != 4:
        return lax.psum(term.astype(jnp.float32), "mp")
    core = lax.axis_index("mp") % 2
    rows_n = term.shape[0]
    halves = term.reshape(2, rows_n // 2, term.shape[1])
    keep = jnp.where(core == 0, halves[0], halves[1])
    send = jnp.where(core == 0, halves[1], halves[0])
    got = swap(send, mp_pairs(1))
    chip_sum = (keep.astype(jnp.float32) + got.astype(jnp.float32)).astype(jnp.bfloat16)
    other = swap(chip_sum, mp_pairs(2))
    total = chip_sum.astype(jnp.float32) + other.astype(jnp.float32)
    rest = swap(total, mp_pairs(1))
    first = jnp.where(core == 0, total, rest)
    second = jnp.where(core == 0, rest, total)
    return jnp.concatenate([first, second], axis=0)


def mp_reduce_cols(term):
    if lax.axis_size("mp") != 4:
        full = lax.psum(term.astype(jnp.float32), "mp")
        quarter = term.shape[1] // lax.axis_size("mp")
        return lax.dynamic_slice_in_dim(full, lax.axis_index("mp") * quarter, quarter, 1)
    index = lax.axis_index("mp")
    rows_n, width = term.shape
    parts = term.reshape(rows_n, 4, width // 4)
    total = jnp.take(parts, index, axis=1).astype(jnp.float32)
    for bit in (1, 2, 3):
        total = total + swap(jnp.take(parts, index ^ bit, axis=1), mp_pairs(bit)).astype(jnp.float32)
    return total


def mp_gather_cols(part):
    if lax.axis_size("mp") != 4:
        return lax.all_gather(part, "mp", axis=2, tiled=True)
    index = lax.axis_index("mp")
    moved = [part] + [swap(part, mp_pairs(bit)) for bit in (1, 2, 3)]
    placed = []
    for q in range(4):
        rel = index ^ q
        piece = jnp.where(rel == 0, moved[0], moved[1])
        piece = jnp.where(rel == 2, moved[2], piece)
        placed.append(jnp.where(rel == 3, moved[3], piece))
    return jnp.concatenate(placed, axis=2)


def mp_gather_steps(part):
    if lax.axis_size("mp") != 4:
        return lax.all_gather(part, "mp", axis=2, tiled=True)
    index = lax.axis_index("mp")
    core = index % 2
    chip = index // 2
    got = swap(part, mp_pairs(1))
    pair = jnp.where(
        core == 0, jnp.concatenate([part, got], axis=2), jnp.concatenate([got, part], axis=2)
    )
    other = swap(pair, mp_pairs(2))
    return jnp.where(
        chip == 0, jnp.concatenate([pair, other], axis=2), jnp.concatenate([other, pair], axis=2)
    )


def pairs_gather(payload, owners_n):
    if owners_n <= SHIFTS_MAX:
        return jnp.stack(
            [payload] + [pairs_shift(payload, step, owners_n) for step in range(1, owners_n)]
        )
    own = lax.axis_index("pairs")
    every = lax.all_gather(payload, "pairs", axis=0)
    return jnp.roll(every[::-1], own + 1, axis=0)


def pick_rows(onehot, values):
    shape = values.shape
    flat = values.reshape(shape[0], -1)
    picked = jnp.dot(onehot.astype(values.dtype), flat, preferred_element_type=jnp.float32)
    return picked.astype(values.dtype).reshape((onehot.shape[0],) + shape[1:])


def per_device(
    tokens,
    pair_list,
    confidence,
    gain_self,
    gain_query,
    gain_context,
    gain_mlp,
    self_qkv,
    self_out,
    cross_query,
    cross_kv,
    cross_out,
    mlp_up,
    mlp_down,
):
    quarter = tokens.shape[1]
    img_dev = tokens.shape[0] // TOKS
    pair_dev = pair_list.shape[0]
    views_n = 2 * pair_dev
    owners_n = lax.axis_size("pairs")
    own = lax.axis_index("pairs")

    payload = jnp.concatenate(
        [
            tokens.astype(jnp.float32).reshape(-1),
            pair_list.astype(jnp.float32).reshape(-1),
            confidence.reshape(-1),
        ]
    )
    table = pairs_gather(payload, owners_n)
    cut_tok = img_dev * TOKS * quarter
    cut_ids = cut_tok + views_n
    all_tok = table[:, :cut_tok].astype(jnp.bfloat16).reshape(owners_n * img_dev, TOKS * quarter)
    all_ids = table[:, cut_tok:cut_ids].astype(jnp.int32)
    all_conf = table[:, cut_ids:].reshape(owners_n * views_n, TOKS)
    partner_ids = all_ids.reshape(owners_n, pair_dev, 2)[:, :, ::-1].reshape(-1)
    all_ids = all_ids.reshape(-1)

    mine = (all_ids // img_dev == own).astype(jnp.int32)
    rank = jnp.cumsum(mine) - 1
    choose = (mine[None, :] == 1) & (rank[None, :] == jnp.arange(views_n)[:, None])
    image = jnp.sum(jnp.where(choose, all_ids[None, :], 0), axis=1)
    other = jnp.sum(jnp.where(choose, partner_ids[None, :], 0), axis=1)
    conf = jnp.dot(choose.astype(jnp.float32), all_conf, precision=lax.Precision.HIGHEST)
    local = image % img_dev
    at = ((own - other // img_dev) % owners_n) * img_dev + other % img_dev
    far = (at[:, None] == jnp.arange(owners_n * img_dev)[None, :]).astype(jnp.bfloat16)
    context_q = pick_rows(far, all_tok).reshape(views_n, TOKS, quarter)

    own_tok = mp_gather_cols(tokens.reshape(img_dev, TOKS, quarter))
    width = own_tok.shape[2]
    img_rows = img_dev * TOKS
    begin = own_tok.astype(jnp.float32).reshape(img_rows, width)
    normed = layer_norm(begin, gain_self)
    qkv = jnp.einsum("rd,kdc->krc", normed, self_qkv, preferred_element_type=jnp.float32).astype(
        jnp.bfloat16
    )
    term = jnp.dot(
        attend(qkv[0], qkv[1], qkv[2], img_dev), self_out, preferred_element_type=jnp.float32
    )
    resid_img = begin + mp_allreduce(term.astype(jnp.bfloat16))
    normed = layer_norm(resid_img, gain_query)
    query_img = jnp.dot(normed, cross_query, preferred_element_type=jnp.float32).astype(
        jnp.bfloat16
    )

    rows_n = views_n * TOKS
    context = layer_norm(mp_gather_steps(context_q).astype(jnp.float32), gain_context).reshape(
        rows_n, width
    )
    keyval = jnp.einsum(
        "rd,kdc->krc", context, cross_kv, preferred_element_type=jnp.float32
    ).astype(jnp.bfloat16)
    near = (local[:, None] == jnp.arange(img_dev)[None, :]).astype(jnp.bfloat16)
    query = pick_rows(near, query_img.reshape(img_dev, TOKS, -1)).reshape(rows_n, -1)
    resid = jnp.take(resid_img.reshape(img_dev, TOKS, width), local, axis=0).reshape(
        rows_n, width
    )
    term = jnp.dot(
        attend(query, keyval[0], keyval[1], views_n), cross_out, preferred_element_type=jnp.float32
    )
    resid = resid + mp_allreduce(term.astype(jnp.bfloat16))
    normed = layer_norm(resid, gain_mlp)
    hidden = jax.nn.gelu(
        jnp.dot(normed, mlp_up, preferred_element_type=jnp.float32), approximate=False
    )
    term = jnp.dot(hidden.astype(jnp.bfloat16), mlp_down, preferred_element_type=jnp.float32)
    offset = lax.axis_index("mp") * quarter
    final = lax.dynamic_slice_in_dim(resid, offset, quarter, 1) + mp_reduce_cols(
        term.astype(jnp.bfloat16)
    )
    part = (final.reshape(views_n, TOKS, quarter) * conf[:, :, None]).astype(jnp.bfloat16)
    weight = conf.astype(jnp.bfloat16)
    owner_match = near.astype(jnp.float32).T
    numer = jnp.einsum(
        "iv,vtc->itc", owner_match, part.astype(jnp.float32), precision=lax.Precision.HIGHEST
    )
    denom = jnp.dot(owner_match, weight.astype(jnp.float32), precision=lax.Precision.HIGHEST)
    result = numer / jnp.maximum(denom, 1.0)[:, :, None]
    return result.astype(jnp.bfloat16).reshape(img_dev * TOKS, quarter)


def solution(mesh):
    return jax.shard_map(
        per_device,
        mesh=mesh,
        in_specs=(
            P(("groups", "pairs"), "mp"),
            P(("groups", "pairs"), None),
            P(("groups", "pairs"), None),
            P(),
            P(),
            P(),
            P(),
            P(None, None, "mp"),
            P("mp", None),
            P(None, "mp"),
            P(None, None, "mp"),
            P("mp", None),
            P(None, "mp"),
            P("mp", None),
        ),
        out_specs=P(("groups", "pairs"), "mp"),
        check_vma=False,
    )
```

```python
import jax
import jax.numpy as jnp
from jax import lax
from jax.sharding import PartitionSpec as P

HEAD = 64
TOKS = 32


EPSILON = 1e-06


def layer_norm(values, gain):
    center = values - jnp.mean(values, axis=-1, keepdims=True)
    spread = jnp.mean(center * center, axis=-1, keepdims=True)
    return (center * lax.rsqrt(spread + EPSILON) * gain).astype(jnp.bfloat16)


def attend(query, keys, values, views_n):
    rows_n, width = query.shape
    heads_n = width // HEAD
    qh = query.reshape(views_n, TOKS, heads_n, HEAD)
    kh = keys.reshape(views_n, TOKS, heads_n, HEAD)
    vh = values.reshape(views_n, TOKS, heads_n, HEAD)
    scores = jnp.einsum("vqhc,vkhc->vhqk", qh, kh, preferred_element_type=jnp.float32) * HEAD ** (
        -0.5
    )
    probs = jax.nn.softmax(scores, axis=-1).astype(jnp.bfloat16)
    mixed = jnp.einsum("vhqk,vkhc->vqhc", probs, vh, preferred_element_type=jnp.float32)
    return mixed.astype(jnp.bfloat16).reshape(rows_n, width)


SHIFTS_MAX = 8


def pairs_shift(values, step, owners_n):
    return lax.ppermute(values, "pairs", [(i, (i + step) % owners_n) for i in range(owners_n)])


def swap(values, pairs):
    return lax.ppermute(values, "mp", pairs)


def mp_pairs(bit):
    n = 4
    return [(i, i ^ bit) for i in range(n)]


def mp_allreduce(term):
    if lax.axis_size("mp") != 4:
        return lax.psum(term.astype(jnp.float32), "mp")
    core = lax.axis_index("mp") % 2
    rows_n = term.shape[0]
    halves = term.reshape(2, rows_n // 2, term.shape[1])
    keep = jnp.where(core == 0, halves[0], halves[1])
    send = jnp.where(core == 0, halves[1], halves[0])
    got = swap(send, mp_pairs(1))
    chip_sum = (keep.astype(jnp.float32) + got.astype(jnp.float32)).astype(jnp.bfloat16)
    other = swap(chip_sum, mp_pairs(2))
    total = chip_sum.astype(jnp.float32) + other.astype(jnp.float32)
    rest = swap(total, mp_pairs(1))
    first = jnp.where(core == 0, total, rest)
    second = jnp.where(core == 0, rest, total)
    return jnp.concatenate([first, second], axis=0)


def mp_reduce_cols(term):
    if lax.axis_size("mp") != 4:
        full = lax.psum(term.astype(jnp.float32), "mp")
        quarter = term.shape[1] // lax.axis_size("mp")
        return lax.dynamic_slice_in_dim(full, lax.axis_index("mp") * quarter, quarter, 1)
    index = lax.axis_index("mp")
    rows_n, width = term.shape
    parts = term.reshape(rows_n, 4, width // 4)
    total = jnp.take(parts, index, axis=1).astype(jnp.float32)
    for bit in (1, 2, 3):
        total = total + swap(jnp.take(parts, index ^ bit, axis=1), mp_pairs(bit)).astype(jnp.float32)
    return total


def mp_gather_cols(part):
    if lax.axis_size("mp") != 4:
        return lax.all_gather(part, "mp", axis=2, tiled=True)
    index = lax.axis_index("mp")
    moved = [part] + [swap(part, mp_pairs(bit)) for bit in (1, 2, 3)]
    placed = []
    for q in range(4):
        rel = index ^ q
        piece = jnp.where(rel == 0, moved[0], moved[1])
        piece = jnp.where(rel == 2, moved[2], piece)
        placed.append(jnp.where(rel == 3, moved[3], piece))
    return jnp.concatenate(placed, axis=2)


def mp_gather_steps(part):
    if lax.axis_size("mp") != 4:
        return lax.all_gather(part, "mp", axis=2, tiled=True)
    index = lax.axis_index("mp")
    core = index % 2
    chip = index // 2
    got = swap(part, mp_pairs(1))
    pair = jnp.where(
        core == 0, jnp.concatenate([part, got], axis=2), jnp.concatenate([got, part], axis=2)
    )
    other = swap(pair, mp_pairs(2))
    return jnp.where(
        chip == 0, jnp.concatenate([pair, other], axis=2), jnp.concatenate([other, pair], axis=2)
    )


def pairs_gather(payload, owners_n):
    if owners_n <= SHIFTS_MAX:
        return jnp.stack(
            [payload] + [pairs_shift(payload, step, owners_n) for step in range(1, owners_n)]
        )
    own = lax.axis_index("pairs")
    every = lax.all_gather(payload, "pairs", axis=0)
    return jnp.roll(every[::-1], own + 1, axis=0)


def pick_rows(onehot, values):
    shape = values.shape
    flat = values.reshape(shape[0], -1)
    picked = jnp.dot(onehot.astype(values.dtype), flat, preferred_element_type=jnp.float32)
    return picked.astype(values.dtype).reshape((onehot.shape[0],) + shape[1:])


def per_device(
    tokens,
    pair_list,
    confidence,
    gain_self,
    gain_query,
    gain_context,
    gain_mlp,
    self_qkv,
    self_out,
    cross_query,
    cross_kv,
    cross_out,
    mlp_up,
    mlp_down,
):
    quarter = tokens.shape[1]
    img_dev = tokens.shape[0] // TOKS
    pair_dev = pair_list.shape[0]
    views_n = 2 * pair_dev
    owners_n = lax.axis_size("pairs")
    own = lax.axis_index("pairs")

    small = jnp.concatenate(
        [pair_list.astype(jnp.float32).reshape(-1), confidence.reshape(-1)]
    )
    table = pairs_gather(small, owners_n)
    all_ids = table[:, :views_n].astype(jnp.int32)
    all_conf = table[:, views_n:].reshape(owners_n * views_n, TOKS)
    partner_ids = all_ids.reshape(owners_n, pair_dev, 2)[:, :, ::-1].reshape(-1)
    all_ids = all_ids.reshape(-1)

    mine = (all_ids // img_dev == own).astype(jnp.int32)
    rank = jnp.cumsum(mine) - 1
    choose = (mine[None, :] == 1) & (rank[None, :] == jnp.arange(views_n)[:, None])
    image = jnp.sum(jnp.where(choose, all_ids[None, :], 0), axis=1)
    other = jnp.sum(jnp.where(choose, partner_ids[None, :], 0), axis=1)
    conf = jnp.dot(choose.astype(jnp.float32), all_conf, precision=lax.Precision.HIGHEST)
    local = image % img_dev
    at = ((own - other // img_dev) % owners_n) * img_dev + other % img_dev
    far = (at[:, None] == jnp.arange(owners_n * img_dev)[None, :]).astype(jnp.bfloat16)

    own_tok = mp_gather_cols(tokens.reshape(img_dev, TOKS, quarter))
    width = own_tok.shape[2]
    img_rows = img_dev * TOKS
    all_tok = pairs_gather(own_tok.reshape(img_rows, width), owners_n).reshape(
        owners_n * img_dev, TOKS * width
    )
    context_tok = pick_rows(far, all_tok).reshape(views_n * TOKS, width)

    begin = own_tok.astype(jnp.float32).reshape(img_rows, width)
    normed = layer_norm(begin, gain_self)
    qkv = jnp.einsum("rd,kdc->krc", normed, self_qkv, preferred_element_type=jnp.float32).astype(
        jnp.bfloat16
    )
    term = jnp.dot(
        attend(qkv[0], qkv[1], qkv[2], img_dev), self_out, preferred_element_type=jnp.float32
    )
    resid_img = begin + mp_allreduce(term.astype(jnp.bfloat16))
    normed = layer_norm(resid_img, gain_query)
    query_img = jnp.dot(normed, cross_query, preferred_element_type=jnp.float32).astype(
        jnp.bfloat16
    )

    rows_n = views_n * TOKS
    context = layer_norm(context_tok.astype(jnp.float32), gain_context)
    keyval = jnp.einsum(
        "rd,kdc->krc", context, cross_kv, preferred_element_type=jnp.float32
    ).astype(jnp.bfloat16)
    near = (local[:, None] == jnp.arange(img_dev)[None, :]).astype(jnp.bfloat16)
    query = pick_rows(near, query_img.reshape(img_dev, TOKS, -1)).reshape(rows_n, -1)
    resid = jnp.take(resid_img.reshape(img_dev, TOKS, width), local, axis=0).reshape(
        rows_n, width
    )
    term = jnp.dot(
        attend(query, keyval[0], keyval[1], views_n), cross_out, preferred_element_type=jnp.float32
    )
    resid = resid + mp_allreduce(term.astype(jnp.bfloat16))
    normed = layer_norm(resid, gain_mlp)
    hidden = jax.nn.gelu(
        jnp.dot(normed, mlp_up, preferred_element_type=jnp.float32), approximate=False
    )
    term = jnp.dot(hidden.astype(jnp.bfloat16), mlp_down, preferred_element_type=jnp.float32)
    offset = lax.axis_index("mp") * quarter
    final = lax.dynamic_slice_in_dim(resid, offset, quarter, 1) + mp_reduce_cols(
        term.astype(jnp.bfloat16)
    )
    part = (final.reshape(views_n, TOKS, quarter) * conf[:, :, None]).astype(jnp.bfloat16)
    weight = conf.astype(jnp.bfloat16)
    owner_match = near.astype(jnp.float32).T
    numer = jnp.einsum(
        "iv,vtc->itc", owner_match, part.astype(jnp.float32), precision=lax.Precision.HIGHEST
    )
    denom = jnp.dot(owner_match, weight.astype(jnp.float32), precision=lax.Precision.HIGHEST)
    result = numer / jnp.maximum(denom, 1.0)[:, :, None]
    return result.astype(jnp.bfloat16).reshape(img_dev * TOKS, quarter)


def solution(mesh):
    return jax.shard_map(
        per_device,
        mesh=mesh,
        in_specs=(
            P(("groups", "pairs"), "mp"),
            P(("groups", "pairs"), None),
            P(("groups", "pairs"), None),
            P(),
            P(),
            P(),
            P(),
            P(None, None, "mp"),
            P("mp", None),
            P(None, "mp"),
            P(None, None, "mp"),
            P("mp", None),
            P(None, "mp"),
            P("mp", None),
        ),
        out_specs=P(("groups", "pairs"), "mp"),
        check_vma=False,
    )
```

```python
import jax
import jax.numpy as jnp
from jax import lax
from jax.sharding import PartitionSpec as P

HEAD = 64
TOKS = 32


EPSILON = 1e-06


def layer_norm(values, gain):
    center = values - jnp.mean(values, axis=-1, keepdims=True)
    spread = jnp.mean(center * center, axis=-1, keepdims=True)
    return (center * lax.rsqrt(spread + EPSILON) * gain).astype(jnp.bfloat16)


def attend(query, keys, values, views_n):
    rows_n, width = query.shape
    heads_n = width // HEAD
    qh = query.reshape(views_n, TOKS, heads_n, HEAD)
    kh = keys.reshape(views_n, TOKS, heads_n, HEAD)
    vh = values.reshape(views_n, TOKS, heads_n, HEAD)
    scores = jnp.einsum("vqhc,vkhc->vhqk", qh, kh, preferred_element_type=jnp.float32) * HEAD ** (
        -0.5
    )
    probs = jax.nn.softmax(scores, axis=-1).astype(jnp.bfloat16)
    mixed = jnp.einsum("vhqk,vkhc->vqhc", probs, vh, preferred_element_type=jnp.float32)
    return mixed.astype(jnp.bfloat16).reshape(rows_n, width)


SHIFTS_MAX = 8


def pairs_shift(values, step, owners_n):
    return lax.ppermute(values, "pairs", [(i, (i + step) % owners_n) for i in range(owners_n)])


def swap(values, pairs):
    return lax.ppermute(values, "mp", pairs)


def mp_pairs(bit):
    n = 4
    return [(i, i ^ bit) for i in range(n)]


def mp_allreduce(term):
    if lax.axis_size("mp") != 4:
        return lax.psum(term.astype(jnp.float32), "mp")
    core = lax.axis_index("mp") % 2
    rows_n = term.shape[0]
    halves = term.reshape(2, rows_n // 2, term.shape[1])
    keep = jnp.where(core == 0, halves[0], halves[1])
    send = jnp.where(core == 0, halves[1], halves[0])
    got = swap(send, mp_pairs(1))
    chip_sum = (keep.astype(jnp.float32) + got.astype(jnp.float32)).astype(jnp.bfloat16)
    other = swap(chip_sum, mp_pairs(2))
    total = chip_sum.astype(jnp.float32) + other.astype(jnp.float32)
    rest = swap(total, mp_pairs(1))
    first = jnp.where(core == 0, total, rest)
    second = jnp.where(core == 0, rest, total)
    return jnp.concatenate([first, second], axis=0)


def mp_reduce_cols(term):
    if lax.axis_size("mp") != 4:
        full = lax.psum(term.astype(jnp.float32), "mp")
        quarter = term.shape[1] // lax.axis_size("mp")
        return lax.dynamic_slice_in_dim(full, lax.axis_index("mp") * quarter, quarter, 1)
    index = lax.axis_index("mp")
    rows_n, width = term.shape
    parts = term.reshape(rows_n, 4, width // 4)
    total = jnp.take(parts, index, axis=1).astype(jnp.float32)
    for bit in (1, 2, 3):
        total = total + swap(jnp.take(parts, index ^ bit, axis=1), mp_pairs(bit)).astype(jnp.float32)
    return total


def mp_gather_cols(part):
    if lax.axis_size("mp") != 4:
        return lax.all_gather(part, "mp", axis=2, tiled=True)
    index = lax.axis_index("mp")
    moved = [part] + [swap(part, mp_pairs(bit)) for bit in (1, 2, 3)]
    placed = []
    for q in range(4):
        rel = index ^ q
        piece = jnp.where(rel == 0, moved[0], moved[1])
        piece = jnp.where(rel == 2, moved[2], piece)
        placed.append(jnp.where(rel == 3, moved[3], piece))
    return jnp.concatenate(placed, axis=2)


def mp_gather_steps(part):
    if lax.axis_size("mp") != 4:
        return lax.all_gather(part, "mp", axis=2, tiled=True)
    index = lax.axis_index("mp")
    core = index % 2
    chip = index // 2
    got = swap(part, mp_pairs(1))
    pair = jnp.where(
        core == 0, jnp.concatenate([part, got], axis=2), jnp.concatenate([got, part], axis=2)
    )
    other = swap(pair, mp_pairs(2))
    return jnp.where(
        chip == 0, jnp.concatenate([pair, other], axis=2), jnp.concatenate([other, pair], axis=2)
    )


def pairs_gather(payload, owners_n):
    if owners_n <= SHIFTS_MAX:
        return jnp.stack(
            [payload] + [pairs_shift(payload, step, owners_n) for step in range(1, owners_n)]
        )
    own = lax.axis_index("pairs")
    every = lax.all_gather(payload, "pairs", axis=0)
    return jnp.roll(every[::-1], own + 1, axis=0)


def pick_rows(onehot, values):
    shape = values.shape
    flat = values.reshape(shape[0], -1)
    picked = jnp.dot(onehot.astype(values.dtype), flat, preferred_element_type=jnp.float32)
    return picked.astype(values.dtype).reshape((onehot.shape[0],) + shape[1:])


def per_device(
    tokens,
    pair_list,
    confidence,
    gain_self,
    gain_query,
    gain_context,
    gain_mlp,
    self_qkv,
    self_out,
    cross_query,
    cross_kv,
    cross_out,
    mlp_up,
    mlp_down,
):
    quarter = tokens.shape[1]
    img_dev = tokens.shape[0] // TOKS
    pair_dev = pair_list.shape[0]
    views_n = 2 * pair_dev
    owners_n = lax.axis_size("pairs")
    own = lax.axis_index("pairs")

    all_tok = pairs_gather(tokens, owners_n).reshape(owners_n * img_dev, TOKS * quarter)
    small = jnp.concatenate([confidence, pair_list.astype(jnp.float32)], axis=1)
    table = pairs_gather(small, owners_n)
    conf_w = confidence.shape[1]
    all_conf = table[:, :, :conf_w].reshape(owners_n * views_n, TOKS)
    all_ids = table[:, :, conf_w:].reshape(owners_n, views_n).astype(jnp.int32)
    partner_ids = all_ids.reshape(owners_n, pair_dev, 2)[:, :, ::-1].reshape(-1)
    all_ids = all_ids.reshape(-1)

    mine = (all_ids // img_dev == own).astype(jnp.int32)
    rank = jnp.cumsum(mine) - 1
    choose = (mine[None, :] == 1) & (rank[None, :] == jnp.arange(views_n)[:, None])
    image = jnp.sum(jnp.where(choose, all_ids[None, :], 0), axis=1)
    other = jnp.sum(jnp.where(choose, partner_ids[None, :], 0), axis=1)
    conf = jnp.dot(choose.astype(jnp.float32), all_conf, precision=lax.Precision.HIGHEST)
    local = image % img_dev
    at = ((own - other // img_dev) % owners_n) * img_dev + other % img_dev
    far = (at[:, None] == jnp.arange(owners_n * img_dev)[None, :]).astype(jnp.bfloat16)
    context_q = pick_rows(far, all_tok).reshape(views_n, TOKS, quarter)

    own_tok = mp_gather_cols(tokens.reshape(img_dev, TOKS, quarter))
    width = own_tok.shape[2]
    img_rows = img_dev * TOKS
    begin = own_tok.astype(jnp.float32).reshape(img_rows, width)
    normed = layer_norm(begin, gain_self)
    qkv = jnp.einsum("rd,kdc->krc", normed, self_qkv, preferred_element_type=jnp.float32).astype(
        jnp.bfloat16
    )
    term = jnp.dot(
        attend(qkv[0], qkv[1], qkv[2], img_dev), self_out, preferred_element_type=jnp.float32
    )
    resid_img = begin + mp_allreduce(term.astype(jnp.bfloat16))
    normed = layer_norm(resid_img, gain_query)
    query_img = jnp.dot(normed, cross_query, preferred_element_type=jnp.float32).astype(
        jnp.bfloat16
    )

    rows_n = views_n * TOKS
    context = layer_norm(mp_gather_steps(context_q).astype(jnp.float32), gain_context).reshape(
        rows_n, width
    )
    keyval = jnp.einsum(
        "rd,kdc->krc", context, cross_kv, preferred_element_type=jnp.float32
    ).astype(jnp.bfloat16)
    near = (local[:, None] == jnp.arange(img_dev)[None, :]).astype(jnp.bfloat16)
    query = pick_rows(near, query_img.reshape(img_dev, TOKS, -1)).reshape(rows_n, -1)
    resid = jnp.take(resid_img.reshape(img_dev, TOKS, width), local, axis=0).reshape(
        rows_n, width
    )
    term = jnp.dot(
        attend(query, keyval[0], keyval[1], views_n), cross_out, preferred_element_type=jnp.float32
    )
    resid = resid + mp_allreduce(term.astype(jnp.bfloat16))
    normed = layer_norm(resid, gain_mlp)
    hidden = jax.nn.gelu(
        jnp.dot(normed, mlp_up, preferred_element_type=jnp.float32), approximate=False
    )
    term = jnp.dot(hidden.astype(jnp.bfloat16), mlp_down, preferred_element_type=jnp.float32)
    offset = lax.axis_index("mp") * quarter
    final = lax.dynamic_slice_in_dim(resid, offset, quarter, 1) + mp_reduce_cols(
        term.astype(jnp.bfloat16)
    )
    part = (final.reshape(views_n, TOKS, quarter) * conf[:, :, None]).astype(jnp.bfloat16)
    weight = conf.astype(jnp.bfloat16)
    owner_match = near.astype(jnp.float32).T
    numer = jnp.einsum(
        "iv,vtc->itc", owner_match, part.astype(jnp.float32), precision=lax.Precision.HIGHEST
    )
    denom = jnp.dot(owner_match, weight.astype(jnp.float32), precision=lax.Precision.HIGHEST)
    result = numer / jnp.maximum(denom, 1.0)[:, :, None]
    return result.astype(jnp.bfloat16).reshape(img_dev * TOKS, quarter)


def solution(mesh):
    return jax.shard_map(
        per_device,
        mesh=mesh,
        in_specs=(
            P(("groups", "pairs"), "mp"),
            P(("groups", "pairs"), None),
            P(("groups", "pairs"), None),
            P(),
            P(),
            P(),
            P(),
            P(None, None, "mp"),
            P("mp", None),
            P(None, "mp"),
            P(None, None, "mp"),
            P("mp", None),
            P(None, "mp"),
            P("mp", None),
        ),
        out_specs=P(("groups", "pairs"), "mp"),
        check_vma=False,
    )
```

```python
import jax
import jax.numpy as jnp
from jax import lax
from jax.sharding import PartitionSpec as P

HEAD = 64
TOKS = 32


EPSILON = 1e-06


def layer_norm(values, gain):
    center = values - jnp.mean(values, axis=-1, keepdims=True)
    spread = jnp.mean(center * center, axis=-1, keepdims=True)
    return (center * lax.rsqrt(spread + EPSILON) * gain).astype(jnp.bfloat16)


def attend(query, keys, values, views_n):
    rows_n, width = query.shape
    heads_n = width // HEAD
    qh = query.reshape(views_n, TOKS, heads_n, HEAD)
    kh = keys.reshape(views_n, TOKS, heads_n, HEAD)
    vh = values.reshape(views_n, TOKS, heads_n, HEAD)
    scores = jnp.einsum("vqhc,vkhc->vhqk", qh, kh, preferred_element_type=jnp.float32) * HEAD ** (
        -0.5
    )
    probs = jax.nn.softmax(scores, axis=-1).astype(jnp.bfloat16)
    mixed = jnp.einsum("vhqk,vkhc->vqhc", probs, vh, preferred_element_type=jnp.float32)
    return mixed.astype(jnp.bfloat16).reshape(rows_n, width)


SHIFTS_MAX = 8


def pairs_shift(values, step, owners_n):
    return lax.ppermute(values, "pairs", [(i, (i + step) % owners_n) for i in range(owners_n)])


def swap(values, pairs):
    return lax.ppermute(values, "mp", pairs)


def mp_pairs(bit):
    n = 4
    return [(i, i ^ bit) for i in range(n)]


def mp_allreduce(term):
    if lax.axis_size("mp") != 4:
        return lax.psum(term.astype(jnp.float32), "mp")
    core = lax.axis_index("mp") % 2
    rows_n = term.shape[0]
    halves = term.reshape(2, rows_n // 2, term.shape[1])
    keep = jnp.where(core == 0, halves[0], halves[1])
    send = jnp.where(core == 0, halves[1], halves[0])
    got = swap(send, mp_pairs(1))
    chip_sum = (keep.astype(jnp.float32) + got.astype(jnp.float32)).astype(jnp.bfloat16)
    other = swap(chip_sum, mp_pairs(2))
    total = chip_sum.astype(jnp.float32) + other.astype(jnp.float32)
    rest = swap(total, mp_pairs(1))
    first = jnp.where(core == 0, total, rest)
    second = jnp.where(core == 0, rest, total)
    return jnp.concatenate([first, second], axis=0)


def mp_reduce_cols(term):
    if lax.axis_size("mp") != 4:
        full = lax.psum(term.astype(jnp.float32), "mp")
        quarter = term.shape[1] // lax.axis_size("mp")
        return lax.dynamic_slice_in_dim(full, lax.axis_index("mp") * quarter, quarter, 1)
    index = lax.axis_index("mp")
    rows_n, width = term.shape
    parts = term.reshape(rows_n, 4, width // 4)
    total = jnp.take(parts, index, axis=1).astype(jnp.float32)
    for bit in (1, 2, 3):
        total = total + swap(jnp.take(parts, index ^ bit, axis=1), mp_pairs(bit)).astype(jnp.float32)
    return total


def mp_gather_cols(part):
    if lax.axis_size("mp") != 4:
        return lax.all_gather(part, "mp", axis=2, tiled=True)
    index = lax.axis_index("mp")
    moved = [part] + [swap(part, mp_pairs(bit)) for bit in (1, 2, 3)]
    placed = []
    for q in range(4):
        rel = index ^ q
        piece = jnp.where(rel == 0, moved[0], moved[1])
        piece = jnp.where(rel == 2, moved[2], piece)
        placed.append(jnp.where(rel == 3, moved[3], piece))
    return jnp.concatenate(placed, axis=2)


def mp_gather_steps(part):
    if lax.axis_size("mp") != 4:
        return lax.all_gather(part, "mp", axis=2, tiled=True)
    index = lax.axis_index("mp")
    core = index % 2
    chip = index // 2
    got = swap(part, mp_pairs(1))
    pair = jnp.where(
        core == 0, jnp.concatenate([part, got], axis=2), jnp.concatenate([got, part], axis=2)
    )
    other = swap(pair, mp_pairs(2))
    return jnp.where(
        chip == 0, jnp.concatenate([pair, other], axis=2), jnp.concatenate([other, pair], axis=2)
    )


def pairs_gather(payload, owners_n):
    if owners_n <= SHIFTS_MAX:
        return jnp.stack(
            [payload] + [pairs_shift(payload, step, owners_n) for step in range(1, owners_n)]
        )
    own = lax.axis_index("pairs")
    every = lax.all_gather(payload, "pairs", axis=0)
    return jnp.roll(every[::-1], own + 1, axis=0)


def pick_rows(onehot, values):
    shape = values.shape
    flat = values.reshape(shape[0], -1)
    picked = jnp.dot(onehot.astype(values.dtype), flat, preferred_element_type=jnp.float32)
    return picked.astype(values.dtype).reshape((onehot.shape[0],) + shape[1:])


def per_device(
    tokens,
    pair_list,
    confidence,
    gain_self,
    gain_query,
    gain_context,
    gain_mlp,
    self_qkv,
    self_out,
    cross_query,
    cross_kv,
    cross_out,
    mlp_up,
    mlp_down,
):
    quarter = tokens.shape[1]
    img_dev = tokens.shape[0] // TOKS
    pair_dev = pair_list.shape[0]
    views_n = 2 * pair_dev
    owners_n = lax.axis_size("pairs")
    own = lax.axis_index("pairs")

    payload = jnp.concatenate(
        [
            tokens.astype(jnp.float32).reshape(-1),
            pair_list.astype(jnp.float32).reshape(-1),
            confidence.reshape(-1),
        ]
    )
    table = pairs_gather(payload, owners_n)
    cut_tok = img_dev * TOKS * quarter
    cut_ids = cut_tok + views_n
    all_tok = table[:, :cut_tok].astype(jnp.bfloat16).reshape(owners_n * img_dev, TOKS * quarter)
    all_ids = table[:, cut_tok:cut_ids].astype(jnp.int32)
    all_conf = table[:, cut_ids:].reshape(owners_n * views_n, TOKS)
    partner_ids = all_ids.reshape(owners_n, pair_dev, 2)[:, :, ::-1].reshape(-1)
    all_ids = all_ids.reshape(-1)

    mine = (all_ids // img_dev == own).astype(jnp.int32)
    rank = jnp.cumsum(mine) - 1
    choose = (mine[None, :] == 1) & (rank[None, :] == jnp.arange(views_n)[:, None])
    image = jnp.sum(jnp.where(choose, all_ids[None, :], 0), axis=1)
    other = jnp.sum(jnp.where(choose, partner_ids[None, :], 0), axis=1)
    conf = jnp.dot(choose.astype(jnp.float32), all_conf, precision=lax.Precision.HIGHEST)
    local = image % img_dev
    at = ((own - other // img_dev) % owners_n) * img_dev + other % img_dev
    far = (at[:, None] == jnp.arange(owners_n * img_dev)[None, :]).astype(jnp.bfloat16)
    context_q = pick_rows(far, all_tok).reshape(views_n, TOKS, quarter)

    own_tok = mp_gather_cols(tokens.reshape(img_dev, TOKS, quarter))
    width = own_tok.shape[2]
    img_rows = img_dev * TOKS
    begin = own_tok.astype(jnp.float32).reshape(img_rows, width)
    normed = layer_norm(begin, gain_self)
    qkv = jnp.einsum("rd,kdc->krc", normed, self_qkv, preferred_element_type=jnp.float32).astype(
        jnp.bfloat16
    )
    term = jnp.dot(
        attend(qkv[0], qkv[1], qkv[2], img_dev), self_out, preferred_element_type=jnp.float32
    )
    resid_img = begin + mp_allreduce(term.astype(jnp.bfloat16))
    normed = layer_norm(resid_img, gain_query)
    query_img = jnp.dot(normed, cross_query, preferred_element_type=jnp.float32).astype(
        jnp.bfloat16
    )

    rows_n = views_n * TOKS
    context = layer_norm(mp_gather_steps(context_q).astype(jnp.float32), gain_context).reshape(
        rows_n, width
    )
    keyval = jnp.einsum(
        "rd,kdc->krc", context, cross_kv, preferred_element_type=jnp.float32
    ).astype(jnp.bfloat16)
    near = (local[:, None] == jnp.arange(img_dev)[None, :]).astype(jnp.bfloat16)
    query = pick_rows(near, query_img.reshape(img_dev, TOKS, -1)).reshape(rows_n, -1)
    resid = jnp.take(resid_img.reshape(img_dev, TOKS, width), local, axis=0).reshape(
        rows_n, width
    )
    term = jnp.dot(
        attend(query, keyval[0], keyval[1], views_n), cross_out, preferred_element_type=jnp.float32
    )
    resid = resid + mp_allreduce(term.astype(jnp.bfloat16))
    normed = layer_norm(resid, gain_mlp)
    hidden = jax.nn.gelu(
        jnp.dot(normed, mlp_up, preferred_element_type=jnp.float32), approximate=False
    )
    hidden = lax.optimization_barrier(hidden.astype(jnp.bfloat16))
    term = jnp.dot(hidden, mlp_down, preferred_element_type=jnp.float32)
    offset = lax.axis_index("mp") * quarter
    final = lax.dynamic_slice_in_dim(resid, offset, quarter, 1) + mp_reduce_cols(
        term.astype(jnp.bfloat16)
    )
    part = (final.reshape(views_n, TOKS, quarter) * conf[:, :, None]).astype(jnp.bfloat16)
    weight = conf.astype(jnp.bfloat16)
    owner_match = near.astype(jnp.float32).T
    numer = jnp.einsum(
        "iv,vtc->itc", owner_match, part.astype(jnp.float32), precision=lax.Precision.HIGHEST
    )
    denom = jnp.dot(owner_match, weight.astype(jnp.float32), precision=lax.Precision.HIGHEST)
    result = numer / jnp.maximum(denom, 1.0)[:, :, None]
    return result.astype(jnp.bfloat16).reshape(img_dev * TOKS, quarter)


def solution(mesh):
    return jax.shard_map(
        per_device,
        mesh=mesh,
        in_specs=(
            P(("groups", "pairs"), "mp"),
            P(("groups", "pairs"), None),
            P(("groups", "pairs"), None),
            P(),
            P(),
            P(),
            P(),
            P(None, None, "mp"),
            P("mp", None),
            P(None, "mp"),
            P(None, None, "mp"),
            P("mp", None),
            P(None, "mp"),
            P("mp", None),
        ),
        out_specs=P(("groups", "pairs"), "mp"),
        check_vma=False,
    )
```

```python
import jax
import jax.numpy as jnp
from jax import lax
from jax.sharding import PartitionSpec as P

HEAD = 64
TOKS = 32


EPSILON = 1e-06


def layer_norm(values, gain):
    center = values - jnp.mean(values, axis=-1, keepdims=True)
    spread = jnp.mean(center * center, axis=-1, keepdims=True)
    return (center * lax.rsqrt(spread + EPSILON) * gain).astype(jnp.bfloat16)


def attend(query, keys, values, views_n):
    rows_n, width = query.shape
    heads_n = width // HEAD
    qh = query.reshape(views_n, TOKS, heads_n, HEAD)
    kh = keys.reshape(views_n, TOKS, heads_n, HEAD)
    vh = values.reshape(views_n, TOKS, heads_n, HEAD)
    scores = jnp.einsum("vqhc,vkhc->vhqk", qh, kh, preferred_element_type=jnp.float32) * HEAD ** (
        -0.5
    )
    probs = jax.nn.softmax(scores, axis=-1).astype(jnp.bfloat16)
    mixed = jnp.einsum("vhqk,vkhc->vqhc", probs, vh, preferred_element_type=jnp.float32)
    return mixed.astype(jnp.bfloat16).reshape(rows_n, width)


SHIFTS_MAX = 8


def pairs_shift(values, step, owners_n):
    return lax.ppermute(values, "pairs", [(i, (i + step) % owners_n) for i in range(owners_n)])


def swap(values, pairs):
    return lax.ppermute(values, "mp", pairs)


def mp_pairs(bit):
    n = 4
    return [(i, i ^ bit) for i in range(n)]


def mp_allreduce(term):
    if lax.axis_size("mp") != 4:
        return lax.psum(term.astype(jnp.float32), "mp")
    core = lax.axis_index("mp") % 2
    rows_n = term.shape[0]
    halves = term.reshape(2, rows_n // 2, term.shape[1])
    keep = jnp.where(core == 0, halves[0], halves[1])
    send = jnp.where(core == 0, halves[1], halves[0])
    got = swap(send, mp_pairs(1))
    chip_sum = (keep.astype(jnp.float32) + got.astype(jnp.float32)).astype(jnp.bfloat16)
    other = swap(chip_sum, mp_pairs(2))
    total = chip_sum.astype(jnp.float32) + other.astype(jnp.float32)
    rest = swap(total, mp_pairs(1))
    first = jnp.where(core == 0, total, rest)
    second = jnp.where(core == 0, rest, total)
    return jnp.concatenate([first, second], axis=0)


def mp_reduce_cols(term):
    if lax.axis_size("mp") != 4:
        full = lax.psum(term.astype(jnp.float32), "mp")
        quarter = term.shape[1] // lax.axis_size("mp")
        return lax.dynamic_slice_in_dim(full, lax.axis_index("mp") * quarter, quarter, 1)
    index = lax.axis_index("mp")
    rows_n, width = term.shape
    parts = term.reshape(rows_n, 4, width // 4)
    total = jnp.take(parts, index, axis=1).astype(jnp.float32)
    for bit in (1, 2, 3):
        total = total + swap(jnp.take(parts, index ^ bit, axis=1), mp_pairs(bit)).astype(jnp.float32)
    return total


def mp_gather_cols(part):
    if lax.axis_size("mp") != 4:
        return lax.all_gather(part, "mp", axis=2, tiled=True)
    index = lax.axis_index("mp")
    moved = [part] + [swap(part, mp_pairs(bit)) for bit in (1, 2, 3)]
    placed = []
    for q in range(4):
        rel = index ^ q
        piece = jnp.where(rel == 0, moved[0], moved[1])
        piece = jnp.where(rel == 2, moved[2], piece)
        placed.append(jnp.where(rel == 3, moved[3], piece))
    return jnp.concatenate(placed, axis=2)


def mp_gather_steps(part):
    if lax.axis_size("mp") != 4:
        return lax.all_gather(part, "mp", axis=2, tiled=True)
    index = lax.axis_index("mp")
    core = index % 2
    chip = index // 2
    got = swap(part, mp_pairs(1))
    pair = jnp.where(
        core == 0, jnp.concatenate([part, got], axis=2), jnp.concatenate([got, part], axis=2)
    )
    other = swap(pair, mp_pairs(2))
    return jnp.where(
        chip == 0, jnp.concatenate([pair, other], axis=2), jnp.concatenate([other, pair], axis=2)
    )


def pairs_gather(payload, owners_n):
    if owners_n <= SHIFTS_MAX:
        return jnp.stack(
            [payload] + [pairs_shift(payload, step, owners_n) for step in range(1, owners_n)]
        )
    own = lax.axis_index("pairs")
    every = lax.all_gather(payload, "pairs", axis=0)
    return jnp.roll(every[::-1], own + 1, axis=0)


def pick_rows(onehot, values):
    shape = values.shape
    flat = values.reshape(shape[0], -1)
    picked = jnp.dot(onehot.astype(values.dtype), flat, preferred_element_type=jnp.float32)
    return picked.astype(values.dtype).reshape((onehot.shape[0],) + shape[1:])


def per_device(
    tokens,
    pair_list,
    confidence,
    gain_self,
    gain_query,
    gain_context,
    gain_mlp,
    self_qkv,
    self_out,
    cross_query,
    cross_kv,
    cross_out,
    mlp_up,
    mlp_down,
):
    quarter = tokens.shape[1]
    img_dev = tokens.shape[0] // TOKS
    pair_dev = pair_list.shape[0]
    views_n = 2 * pair_dev
    owners_n = lax.axis_size("pairs")
    own = lax.axis_index("pairs")

    payload = jnp.concatenate(
        [
            tokens.astype(jnp.float32).reshape(-1),
            pair_list.astype(jnp.float32).reshape(-1),
            confidence.reshape(-1),
        ]
    )
    table = pairs_gather(payload, owners_n)
    cut_tok = img_dev * TOKS * quarter
    cut_ids = cut_tok + views_n
    all_tok = table[:, :cut_tok].astype(jnp.bfloat16).reshape(owners_n * img_dev, TOKS * quarter)
    all_ids = table[:, cut_tok:cut_ids].astype(jnp.int32)
    all_conf = table[:, cut_ids:].reshape(owners_n * views_n, TOKS)
    partner_ids = all_ids.reshape(owners_n, pair_dev, 2)[:, :, ::-1].reshape(-1)
    all_ids = all_ids.reshape(-1)

    mine = (all_ids // img_dev == own).astype(jnp.int32)
    rank = jnp.cumsum(mine) - 1
    choose = (mine[None, :] == 1) & (rank[None, :] == jnp.arange(views_n)[:, None])
    image = jnp.sum(jnp.where(choose, all_ids[None, :], 0), axis=1)
    other = jnp.sum(jnp.where(choose, partner_ids[None, :], 0), axis=1)
    conf = jnp.dot(choose.astype(jnp.float32), all_conf, precision=lax.Precision.HIGHEST)
    local = image % img_dev
    at = ((own - other // img_dev) % owners_n) * img_dev + other % img_dev
    far = (at[:, None] == jnp.arange(owners_n * img_dev)[None, :]).astype(jnp.bfloat16)
    context_q = pick_rows(far, all_tok).reshape(views_n, TOKS, quarter)

    own_tok = mp_gather_cols(tokens.reshape(img_dev, TOKS, quarter))
    width = own_tok.shape[2]
    img_rows = img_dev * TOKS
    begin = own_tok.astype(jnp.float32).reshape(img_rows, width)
    normed = lax.optimization_barrier(layer_norm(begin, gain_self))
    qkv = jnp.einsum("rd,kdc->krc", normed, self_qkv, preferred_element_type=jnp.float32).astype(
        jnp.bfloat16
    )
    term = jnp.dot(
        attend(qkv[0], qkv[1], qkv[2], img_dev), self_out, preferred_element_type=jnp.float32
    )
    resid_img = begin + mp_allreduce(term.astype(jnp.bfloat16))
    normed = lax.optimization_barrier(layer_norm(resid_img, gain_query))
    query_img = jnp.dot(normed, cross_query, preferred_element_type=jnp.float32).astype(
        jnp.bfloat16
    )

    rows_n = views_n * TOKS
    context = layer_norm(mp_gather_steps(context_q).astype(jnp.float32), gain_context).reshape(
        rows_n, width
    )
    keyval = jnp.einsum(
        "rd,kdc->krc", context, cross_kv, preferred_element_type=jnp.float32
    ).astype(jnp.bfloat16)
    near = (local[:, None] == jnp.arange(img_dev)[None, :]).astype(jnp.bfloat16)
    query = pick_rows(near, query_img.reshape(img_dev, TOKS, -1)).reshape(rows_n, -1)
    resid = jnp.take(resid_img.reshape(img_dev, TOKS, width), local, axis=0).reshape(
        rows_n, width
    )
    term = jnp.dot(
        attend(query, keyval[0], keyval[1], views_n), cross_out, preferred_element_type=jnp.float32
    )
    resid = resid + mp_allreduce(term.astype(jnp.bfloat16))
    normed = lax.optimization_barrier(layer_norm(resid, gain_mlp))
    hidden = jax.nn.gelu(
        jnp.dot(normed, mlp_up, preferred_element_type=jnp.float32), approximate=False
    )
    hidden = lax.optimization_barrier(hidden.astype(jnp.bfloat16))
    term = jnp.dot(hidden, mlp_down, preferred_element_type=jnp.float32)
    offset = lax.axis_index("mp") * quarter
    final = lax.dynamic_slice_in_dim(resid, offset, quarter, 1) + mp_reduce_cols(
        term.astype(jnp.bfloat16)
    )
    part = (final.reshape(views_n, TOKS, quarter) * conf[:, :, None]).astype(jnp.bfloat16)
    weight = conf.astype(jnp.bfloat16)
    owner_match = near.astype(jnp.float32).T
    partf = part.astype(jnp.float32)
    weightf = weight.astype(jnp.float32)
    rows = []
    for i in range(img_dev):
        numer = jnp.sum(owner_match[i][:, None, None] * partf, axis=0)
        denom = jnp.sum(owner_match[i][:, None] * weightf, axis=0)
        rows.append(numer / jnp.maximum(denom, 1.0)[:, None])
    return jnp.concatenate(rows, axis=0).astype(jnp.bfloat16)


def solution(mesh):
    return jax.shard_map(
        per_device,
        mesh=mesh,
        in_specs=(
            P(("groups", "pairs"), "mp"),
            P(("groups", "pairs"), None),
            P(("groups", "pairs"), None),
            P(),
            P(),
            P(),
            P(),
            P(None, None, "mp"),
            P("mp", None),
            P(None, "mp"),
            P(None, None, "mp"),
            P("mp", None),
            P(None, "mp"),
            P("mp", None),
        ),
        out_specs=P(("groups", "pairs"), "mp"),
        check_vma=False,
    )
```

```python
import jax
import jax.numpy as jnp
from jax import lax
from jax.sharding import PartitionSpec as P

HEAD = 64
TOKS = 32


EPSILON = 1e-06


def layer_norm(values, gain):
    center = values - jnp.mean(values, axis=-1, keepdims=True)
    spread = jnp.mean(center * center, axis=-1, keepdims=True)
    return (center * lax.rsqrt(spread + EPSILON) * gain).astype(jnp.bfloat16)


def attend(query, keys, values, views_n):
    rows_n, width = query.shape
    heads_n = width // HEAD
    qh = query.reshape(views_n, TOKS, heads_n, HEAD)
    kh = keys.reshape(views_n, TOKS, heads_n, HEAD)
    vh = values.reshape(views_n, TOKS, heads_n, HEAD)
    scores = jnp.einsum("vqhc,vkhc->vhqk", qh, kh, preferred_element_type=jnp.float32) * HEAD ** (
        -0.5
    )
    probs = jax.nn.softmax(scores, axis=-1).astype(jnp.bfloat16)
    mixed = jnp.einsum("vhqk,vkhc->vqhc", probs, vh, preferred_element_type=jnp.float32)
    return mixed.astype(jnp.bfloat16).reshape(rows_n, width)


SHIFTS_MAX = 8


def pairs_shift(values, step, owners_n):
    return lax.ppermute(values, "pairs", [(i, (i + step) % owners_n) for i in range(owners_n)])


def swap(values, pairs):
    return lax.ppermute(values, "mp", pairs)


def mp_pairs(bit):
    n = 4
    return [(i, i ^ bit) for i in range(n)]


def mp_allreduce(term):
    if lax.axis_size("mp") != 4:
        return lax.psum(term.astype(jnp.float32), "mp")
    core = lax.axis_index("mp") % 2
    rows_n = term.shape[0]
    halves = term.reshape(2, rows_n // 2, term.shape[1])
    keep = jnp.where(core == 0, halves[0], halves[1])
    send = jnp.where(core == 0, halves[1], halves[0])
    got = swap(send, mp_pairs(1))
    chip_sum = (keep.astype(jnp.float32) + got.astype(jnp.float32)).astype(jnp.bfloat16)
    other = swap(chip_sum, mp_pairs(2))
    total = chip_sum.astype(jnp.float32) + other.astype(jnp.float32)
    rest = swap(total, mp_pairs(1))
    first = jnp.where(core == 0, total, rest)
    second = jnp.where(core == 0, rest, total)
    return jnp.concatenate([first, second], axis=0)


def mp_reduce_cols(term):
    if lax.axis_size("mp") != 4:
        full = lax.psum(term.astype(jnp.float32), "mp")
        quarter = term.shape[1] // lax.axis_size("mp")
        return lax.dynamic_slice_in_dim(full, lax.axis_index("mp") * quarter, quarter, 1)
    index = lax.axis_index("mp")
    rows_n, width = term.shape
    parts = term.reshape(rows_n, 4, width // 4)
    total = jnp.take(parts, index, axis=1).astype(jnp.float32)
    for bit in (1, 2, 3):
        total = total + swap(jnp.take(parts, index ^ bit, axis=1), mp_pairs(bit)).astype(jnp.float32)
    return total


def mp_gather_cols(part):
    if lax.axis_size("mp") != 4:
        return lax.all_gather(part, "mp", axis=2, tiled=True)
    index = lax.axis_index("mp")
    moved = [part] + [swap(part, mp_pairs(bit)) for bit in (1, 2, 3)]
    placed = []
    for q in range(4):
        rel = index ^ q
        piece = jnp.where(rel == 0, moved[0], moved[1])
        piece = jnp.where(rel == 2, moved[2], piece)
        placed.append(jnp.where(rel == 3, moved[3], piece))
    return jnp.concatenate(placed, axis=2)


def mp_gather_steps(part):
    if lax.axis_size("mp") != 4:
        return lax.all_gather(part, "mp", axis=2, tiled=True)
    index = lax.axis_index("mp")
    core = index % 2
    chip = index // 2
    got = swap(part, mp_pairs(1))
    pair = jnp.where(
        core == 0, jnp.concatenate([part, got], axis=2), jnp.concatenate([got, part], axis=2)
    )
    other = swap(pair, mp_pairs(2))
    return jnp.where(
        chip == 0, jnp.concatenate([pair, other], axis=2), jnp.concatenate([other, pair], axis=2)
    )


def pairs_gather(payload, owners_n):
    if owners_n <= SHIFTS_MAX:
        return jnp.stack(
            [payload] + [pairs_shift(payload, step, owners_n) for step in range(1, owners_n)]
        )
    own = lax.axis_index("pairs")
    every = lax.all_gather(payload, "pairs", axis=0)
    return jnp.roll(every[::-1], own + 1, axis=0)


def pick_rows(onehot, values):
    shape = values.shape
    flat = values.reshape(shape[0], -1)
    picked = jnp.dot(onehot.astype(values.dtype), flat, preferred_element_type=jnp.float32)
    return picked.astype(values.dtype).reshape((onehot.shape[0],) + shape[1:])


def per_device(
    tokens,
    pair_list,
    confidence,
    gain_self,
    gain_query,
    gain_context,
    gain_mlp,
    self_qkv,
    self_out,
    cross_query,
    cross_kv,
    cross_out,
    mlp_up,
    mlp_down,
):
    quarter = tokens.shape[1]
    img_dev = tokens.shape[0] // TOKS
    pair_dev = pair_list.shape[0]
    views_n = 2 * pair_dev
    owners_n = lax.axis_size("pairs")
    own = lax.axis_index("pairs")

    payload = jnp.concatenate(
        [
            tokens.astype(jnp.float32).reshape(-1),
            pair_list.astype(jnp.float32).reshape(-1),
            confidence.reshape(-1),
        ]
    )
    table = pairs_gather(payload, owners_n)
    cut_tok = img_dev * TOKS * quarter
    cut_ids = cut_tok + views_n
    all_tok = table[:, :cut_tok].astype(jnp.bfloat16).reshape(owners_n * img_dev, TOKS * quarter)
    all_ids = table[:, cut_tok:cut_ids].astype(jnp.int32)
    all_conf = table[:, cut_ids:].reshape(owners_n * views_n, TOKS)
    partner_ids = all_ids.reshape(owners_n, pair_dev, 2)[:, :, ::-1].reshape(-1)
    all_ids = all_ids.reshape(-1)

    mine = (all_ids // img_dev == own).astype(jnp.int32)
    rank = jnp.cumsum(mine) - 1
    choose = (mine[None, :] == 1) & (rank[None, :] == jnp.arange(views_n)[:, None])
    image = jnp.sum(jnp.where(choose, all_ids[None, :], 0), axis=1)
    other = jnp.sum(jnp.where(choose, partner_ids[None, :], 0), axis=1)
    conf = jnp.dot(choose.astype(jnp.float32), all_conf, precision=lax.Precision.HIGHEST)
    local = image % img_dev
    at = ((own - other // img_dev) % owners_n) * img_dev + other % img_dev
    far = (at[:, None] == jnp.arange(owners_n * img_dev)[None, :]).astype(jnp.bfloat16)
    context_q = pick_rows(far, all_tok).reshape(views_n, TOKS, quarter)

    own_tok = mp_gather_cols(tokens.reshape(img_dev, TOKS, quarter))
    width = own_tok.shape[2]
    img_rows = img_dev * TOKS
    begin = own_tok.astype(jnp.float32).reshape(img_rows, width)
    normed = lax.optimization_barrier(layer_norm(begin, gain_self))
    qkv = jnp.einsum("rd,kdc->krc", normed, self_qkv, preferred_element_type=jnp.float32).astype(
        jnp.bfloat16
    )
    term = jnp.dot(
        attend(qkv[0], qkv[1], qkv[2], img_dev), self_out, preferred_element_type=jnp.float32
    )
    resid_img = begin + mp_allreduce(term.astype(jnp.bfloat16))
    normed = lax.optimization_barrier(layer_norm(resid_img, gain_query))
    query_img = jnp.dot(normed, cross_query, preferred_element_type=jnp.float32).astype(
        jnp.bfloat16
    )

    rows_n = views_n * TOKS
    context = lax.optimization_barrier(
        layer_norm(mp_gather_steps(context_q).astype(jnp.float32), gain_context)
    ).reshape(rows_n, width)
    keyval = jnp.einsum(
        "rd,kdc->krc", context, cross_kv, preferred_element_type=jnp.float32
    ).astype(jnp.bfloat16)
    near = (local[:, None] == jnp.arange(img_dev)[None, :]).astype(jnp.bfloat16)
    query = pick_rows(near, query_img.reshape(img_dev, TOKS, -1)).reshape(rows_n, -1)
    resid = jnp.take(resid_img.reshape(img_dev, TOKS, width), local, axis=0).reshape(
        rows_n, width
    )
    term = jnp.dot(
        attend(query, keyval[0], keyval[1], views_n), cross_out, preferred_element_type=jnp.float32
    )
    resid = resid + mp_allreduce(term.astype(jnp.bfloat16))
    normed = lax.optimization_barrier(layer_norm(resid, gain_mlp))
    hidden = jax.nn.gelu(
        jnp.dot(normed, mlp_up, preferred_element_type=jnp.float32), approximate=False
    )
    hidden = lax.optimization_barrier(hidden.astype(jnp.bfloat16))
    term = jnp.dot(hidden, mlp_down, preferred_element_type=jnp.float32)
    offset = lax.axis_index("mp") * quarter
    final = lax.dynamic_slice_in_dim(resid, offset, quarter, 1) + mp_reduce_cols(
        term.astype(jnp.bfloat16)
    )
    part = (final.reshape(views_n, TOKS, quarter) * conf[:, :, None]).astype(jnp.bfloat16)
    weight = conf.astype(jnp.bfloat16)
    owner_match = near.astype(jnp.float32).T
    partf = part.astype(jnp.float32)
    weightf = weight.astype(jnp.float32)
    rows = []
    for i in range(img_dev):
        numer = jnp.sum(owner_match[i][:, None, None] * partf, axis=0)
        denom = jnp.sum(owner_match[i][:, None] * weightf, axis=0)
        rows.append(numer / jnp.maximum(denom, 1.0)[:, None])
    return jnp.concatenate(rows, axis=0).astype(jnp.bfloat16)


def solution(mesh):
    return jax.shard_map(
        per_device,
        mesh=mesh,
        in_specs=(
            P(("groups", "pairs"), "mp"),
            P(("groups", "pairs"), None),
            P(("groups", "pairs"), None),
            P(),
            P(),
            P(),
            P(),
            P(None, None, "mp"),
            P("mp", None),
            P(None, "mp"),
            P(None, None, "mp"),
            P("mp", None),
            P(None, "mp"),
            P("mp", None),
        ),
        out_specs=P(("groups", "pairs"), "mp"),
        check_vma=False,
    )
```

```python
import jax
import jax.numpy as jnp
from jax import lax
from jax.sharding import PartitionSpec as P

HEAD = 64
TOKS = 32


EPSILON = 1e-06


def layer_norm(values, gain):
    center = values - jnp.mean(values, axis=-1, keepdims=True)
    spread = jnp.mean(center * center, axis=-1, keepdims=True)
    return (center * lax.rsqrt(spread + EPSILON) * gain).astype(jnp.bfloat16)


def attend(query, keys, values, views_n):
    rows_n, width = query.shape
    heads_n = width // HEAD
    qh = query.reshape(views_n, TOKS, heads_n, HEAD)
    kh = keys.reshape(views_n, TOKS, heads_n, HEAD)
    vh = values.reshape(views_n, TOKS, heads_n, HEAD)
    scores = jnp.einsum("vqhc,vkhc->vhqk", qh, kh, preferred_element_type=jnp.float32) * HEAD ** (
        -0.5
    )
    probs = jax.nn.softmax(scores, axis=-1).astype(jnp.bfloat16)
    mixed = jnp.einsum("vhqk,vkhc->vqhc", probs, vh, preferred_element_type=jnp.float32)
    return mixed.astype(jnp.bfloat16).reshape(rows_n, width)


SHIFTS_MAX = 8


def pairs_shift(values, step, owners_n):
    return lax.ppermute(values, "pairs", [(i, (i + step) % owners_n) for i in range(owners_n)])


def swap(values, pairs):
    return lax.ppermute(values, "mp", pairs)


def mp_pairs(bit):
    n = 4
    return [(i, i ^ bit) for i in range(n)]


def mp_allreduce(term):
    if lax.axis_size("mp") != 4:
        return lax.psum(term.astype(jnp.float32), "mp")
    core = lax.axis_index("mp") % 2
    rows_n = term.shape[0]
    halves = term.reshape(2, rows_n // 2, term.shape[1])
    keep = jnp.where(core == 0, halves[0], halves[1])
    send = jnp.where(core == 0, halves[1], halves[0])
    got = swap(send, mp_pairs(1))
    chip_sum = (keep.astype(jnp.float32) + got.astype(jnp.float32)).astype(jnp.bfloat16)
    other = swap(chip_sum, mp_pairs(2))
    total = chip_sum.astype(jnp.float32) + other.astype(jnp.float32)
    rest = swap(total, mp_pairs(1))
    first = jnp.where(core == 0, total, rest)
    second = jnp.where(core == 0, rest, total)
    return jnp.concatenate([first, second], axis=0)


def mp_reduce_cols(term):
    if lax.axis_size("mp") != 4:
        full = lax.psum(term.astype(jnp.float32), "mp")
        quarter = term.shape[1] // lax.axis_size("mp")
        return lax.dynamic_slice_in_dim(full, lax.axis_index("mp") * quarter, quarter, 1)
    index = lax.axis_index("mp")
    rows_n, width = term.shape
    parts = term.reshape(rows_n, 4, width // 4)
    total = jnp.take(parts, index, axis=1).astype(jnp.float32)
    for bit in (1, 2, 3):
        total = total + swap(jnp.take(parts, index ^ bit, axis=1), mp_pairs(bit)).astype(jnp.float32)
    return total


def mp_gather_cols(part):
    if lax.axis_size("mp") != 4:
        return lax.all_gather(part, "mp", axis=2, tiled=True)
    index = lax.axis_index("mp")
    moved = [part] + [swap(part, mp_pairs(bit)) for bit in (1, 2, 3)]
    placed = []
    for q in range(4):
        rel = index ^ q
        piece = jnp.where(rel == 0, moved[0], moved[1])
        piece = jnp.where(rel == 2, moved[2], piece)
        placed.append(jnp.where(rel == 3, moved[3], piece))
    return jnp.concatenate(placed, axis=2)


def mp_gather_steps(part):
    if lax.axis_size("mp") != 4:
        return lax.all_gather(part, "mp", axis=2, tiled=True)
    index = lax.axis_index("mp")
    core = index % 2
    chip = index // 2
    got = swap(part, mp_pairs(1))
    pair = jnp.where(
        core == 0, jnp.concatenate([part, got], axis=2), jnp.concatenate([got, part], axis=2)
    )
    other = swap(pair, mp_pairs(2))
    return jnp.where(
        chip == 0, jnp.concatenate([pair, other], axis=2), jnp.concatenate([other, pair], axis=2)
    )


def allreduce_with_context(term, context_q):
    if lax.axis_size("mp") != 4:
        return mp_allreduce(term), mp_gather_steps(context_q)
    index = lax.axis_index("mp")
    core = index % 2
    chip = index // 2
    rows_n = term.shape[0]
    halves = term.reshape(2, rows_n // 2, term.shape[1])
    keep = jnp.where(core == 0, halves[0], halves[1])
    send = jnp.where(core == 0, halves[1], halves[0])
    got = swap(send, mp_pairs(1))
    chip_sum = (keep.astype(jnp.float32) + got.astype(jnp.float32)).astype(jnp.bfloat16)
    near = swap(context_q, mp_pairs(1))
    pair = jnp.where(
        core == 0,
        jnp.concatenate([context_q, near], axis=2),
        jnp.concatenate([near, context_q], axis=2),
    )
    cut = chip_sum.size
    both = swap(jnp.concatenate([chip_sum.reshape(-1), pair.reshape(-1)]), mp_pairs(2))
    other = both[:cut].reshape(chip_sum.shape)
    far = both[cut:].reshape(pair.shape)
    total = chip_sum.astype(jnp.float32) + other.astype(jnp.float32)
    rest = swap(total, mp_pairs(1))
    first = jnp.where(core == 0, total, rest)
    second = jnp.where(core == 0, rest, total)
    context = jnp.where(
        chip == 0, jnp.concatenate([pair, far], axis=2), jnp.concatenate([far, pair], axis=2)
    )
    return jnp.concatenate([first, second], axis=0), context


def pairs_gather(payload, owners_n):
    if owners_n <= SHIFTS_MAX:
        return jnp.stack(
            [payload] + [pairs_shift(payload, step, owners_n) for step in range(1, owners_n)]
        )
    own = lax.axis_index("pairs")
    every = lax.all_gather(payload, "pairs", axis=0)
    return jnp.roll(every[::-1], own + 1, axis=0)


def pick_rows(onehot, values):
    shape = values.shape
    flat = values.reshape(shape[0], -1)
    picked = jnp.dot(onehot.astype(values.dtype), flat, preferred_element_type=jnp.float32)
    return picked.astype(values.dtype).reshape((onehot.shape[0],) + shape[1:])


def per_device(
    tokens,
    pair_list,
    confidence,
    gain_self,
    gain_query,
    gain_context,
    gain_mlp,
    self_qkv,
    self_out,
    cross_query,
    cross_kv,
    cross_out,
    mlp_up,
    mlp_down,
):
    quarter = tokens.shape[1]
    img_dev = tokens.shape[0] // TOKS
    pair_dev = pair_list.shape[0]
    views_n = 2 * pair_dev
    owners_n = lax.axis_size("pairs")
    own = lax.axis_index("pairs")

    payload = jnp.concatenate(
        [
            tokens.astype(jnp.float32).reshape(-1),
            pair_list.astype(jnp.float32).reshape(-1),
            confidence.reshape(-1),
        ]
    )
    table = pairs_gather(payload, owners_n)
    cut_tok = img_dev * TOKS * quarter
    cut_ids = cut_tok + views_n
    all_tok = table[:, :cut_tok].astype(jnp.bfloat16).reshape(owners_n * img_dev, TOKS * quarter)
    all_ids = table[:, cut_tok:cut_ids].astype(jnp.int32)
    all_conf = table[:, cut_ids:].reshape(owners_n * views_n, TOKS)
    partner_ids = all_ids.reshape(owners_n, pair_dev, 2)[:, :, ::-1].reshape(-1)
    all_ids = all_ids.reshape(-1)

    mine = (all_ids // img_dev == own).astype(jnp.int32)
    rank = jnp.cumsum(mine) - 1
    choose = (mine[None, :] == 1) & (rank[None, :] == jnp.arange(views_n)[:, None])
    image = jnp.sum(jnp.where(choose, all_ids[None, :], 0), axis=1)
    other = jnp.sum(jnp.where(choose, partner_ids[None, :], 0), axis=1)
    conf = jnp.dot(choose.astype(jnp.float32), all_conf, precision=lax.Precision.HIGHEST)
    local = image % img_dev
    at = ((own - other // img_dev) % owners_n) * img_dev + other % img_dev
    far = (at[:, None] == jnp.arange(owners_n * img_dev)[None, :]).astype(jnp.bfloat16)
    context_q = pick_rows(far, all_tok).reshape(views_n, TOKS, quarter)

    own_tok = mp_gather_cols(tokens.reshape(img_dev, TOKS, quarter))
    width = own_tok.shape[2]
    img_rows = img_dev * TOKS
    begin = own_tok.astype(jnp.float32).reshape(img_rows, width)
    normed = lax.optimization_barrier(layer_norm(begin, gain_self))
    qkv = jnp.einsum("rd,kdc->krc", normed, self_qkv, preferred_element_type=jnp.float32).astype(
        jnp.bfloat16
    )
    term = jnp.dot(
        attend(qkv[0], qkv[1], qkv[2], img_dev), self_out, preferred_element_type=jnp.float32
    )
    summed, context_full = allreduce_with_context(term.astype(jnp.bfloat16), context_q)
    resid_img = begin + summed
    normed = lax.optimization_barrier(layer_norm(resid_img, gain_query))
    query_img = jnp.dot(normed, cross_query, preferred_element_type=jnp.float32).astype(
        jnp.bfloat16
    )

    rows_n = views_n * TOKS
    context = lax.optimization_barrier(
        layer_norm(context_full.astype(jnp.float32), gain_context)
    ).reshape(rows_n, width)
    keyval = jnp.einsum(
        "rd,kdc->krc", context, cross_kv, preferred_element_type=jnp.float32
    ).astype(jnp.bfloat16)
    near = (local[:, None] == jnp.arange(img_dev)[None, :]).astype(jnp.bfloat16)
    query = pick_rows(near, query_img.reshape(img_dev, TOKS, -1)).reshape(rows_n, -1)
    resid = jnp.take(resid_img.reshape(img_dev, TOKS, width), local, axis=0).reshape(
        rows_n, width
    )
    term = jnp.dot(
        attend(query, keyval[0], keyval[1], views_n), cross_out, preferred_element_type=jnp.float32
    )
    resid = resid + mp_allreduce(term.astype(jnp.bfloat16))
    normed = lax.optimization_barrier(layer_norm(resid, gain_mlp))
    hidden = jax.nn.gelu(
        jnp.dot(normed, mlp_up, preferred_element_type=jnp.float32), approximate=False
    )
    hidden = lax.optimization_barrier(hidden.astype(jnp.bfloat16))
    term = jnp.dot(hidden, mlp_down, preferred_element_type=jnp.float32)
    offset = lax.axis_index("mp") * quarter
    final = lax.dynamic_slice_in_dim(resid, offset, quarter, 1) + mp_reduce_cols(
        term.astype(jnp.bfloat16)
    )
    part = (final.reshape(views_n, TOKS, quarter) * conf[:, :, None]).astype(jnp.bfloat16)
    weight = conf.astype(jnp.bfloat16)
    owner_match = near.astype(jnp.float32).T
    partf = part.astype(jnp.float32)
    weightf = weight.astype(jnp.float32)
    rows = []
    for i in range(img_dev):
        numer = jnp.sum(owner_match[i][:, None, None] * partf, axis=0)
        denom = jnp.sum(owner_match[i][:, None] * weightf, axis=0)
        rows.append(numer / jnp.maximum(denom, 1.0)[:, None])
    return jnp.concatenate(rows, axis=0).astype(jnp.bfloat16)


def solution(mesh):
    return jax.shard_map(
        per_device,
        mesh=mesh,
        in_specs=(
            P(("groups", "pairs"), "mp"),
            P(("groups", "pairs"), None),
            P(("groups", "pairs"), None),
            P(),
            P(),
            P(),
            P(),
            P(None, None, "mp"),
            P("mp", None),
            P(None, "mp"),
            P(None, None, "mp"),
            P("mp", None),
            P(None, "mp"),
            P("mp", None),
        ),
        out_specs=P(("groups", "pairs"), "mp"),
        check_vma=False,
    )
```

```python
import jax
import jax.numpy as jnp
from jax import lax
from jax.sharding import PartitionSpec as P

HEAD = 64
TOKS = 32


EPSILON = 1e-06


def layer_norm(values, gain):
    center = values - jnp.mean(values, axis=-1, keepdims=True)
    spread = jnp.mean(center * center, axis=-1, keepdims=True)
    return (center * lax.rsqrt(spread + EPSILON) * gain).astype(jnp.bfloat16)


def attend(query, keys, values, views_n):
    rows_n, width = query.shape
    heads_n = width // HEAD
    qh = query.reshape(views_n, TOKS, heads_n, HEAD)
    kh = keys.reshape(views_n, TOKS, heads_n, HEAD)
    vh = values.reshape(views_n, TOKS, heads_n, HEAD)
    scores = jnp.einsum("vqhc,vkhc->vhqk", qh, kh, preferred_element_type=jnp.float32) * HEAD ** (
        -0.5
    )
    probs = jax.nn.softmax(scores, axis=-1).astype(jnp.bfloat16)
    mixed = jnp.einsum("vhqk,vkhc->vqhc", probs, vh, preferred_element_type=jnp.float32)
    return mixed.astype(jnp.bfloat16).reshape(rows_n, width)


SHIFTS_MAX = 8


def pairs_shift(values, step, owners_n):
    return lax.ppermute(values, "pairs", [(i, (i + step) % owners_n) for i in range(owners_n)])


def swap(values, pairs):
    return lax.ppermute(values, "mp", pairs)


def mp_pairs(bit):
    n = 4
    return [(i, i ^ bit) for i in range(n)]


def mp_allreduce(term):
    if lax.axis_size("mp") != 4:
        return lax.psum(term.astype(jnp.float32), "mp")
    core = lax.axis_index("mp") % 2
    rows_n = term.shape[0]
    halves = term.reshape(2, rows_n // 2, term.shape[1])
    keep = jnp.where(core == 0, halves[0], halves[1])
    send = jnp.where(core == 0, halves[1], halves[0])
    got = swap(send, mp_pairs(1))
    chip_sum = (keep.astype(jnp.float32) + got.astype(jnp.float32)).astype(jnp.bfloat16)
    other = swap(chip_sum, mp_pairs(2))
    total = chip_sum.astype(jnp.float32) + other.astype(jnp.float32)
    rest = swap(total, mp_pairs(1))
    first = jnp.where(core == 0, total, rest)
    second = jnp.where(core == 0, rest, total)
    return jnp.concatenate([first, second], axis=0)


def mp_reduce_cols(term):
    if lax.axis_size("mp") != 4:
        full = lax.psum(term.astype(jnp.float32), "mp")
        quarter = term.shape[1] // lax.axis_size("mp")
        return lax.dynamic_slice_in_dim(full, lax.axis_index("mp") * quarter, quarter, 1)
    index = lax.axis_index("mp")
    rows_n, width = term.shape
    parts = term.reshape(rows_n, 4, width // 4)
    total = jnp.take(parts, index, axis=1).astype(jnp.float32)
    for bit in (1, 2, 3):
        total = total + swap(jnp.take(parts, index ^ bit, axis=1), mp_pairs(bit)).astype(jnp.float32)
    return total


def mp_gather_cols(part):
    if lax.axis_size("mp") != 4:
        return lax.all_gather(part, "mp", axis=2, tiled=True)
    index = lax.axis_index("mp")
    moved = [part] + [swap(part, mp_pairs(bit)) for bit in (1, 2, 3)]
    placed = []
    for q in range(4):
        rel = index ^ q
        piece = jnp.where(rel == 0, moved[0], moved[1])
        piece = jnp.where(rel == 2, moved[2], piece)
        placed.append(jnp.where(rel == 3, moved[3], piece))
    return jnp.concatenate(placed, axis=2)


def mp_gather_steps(part):
    if lax.axis_size("mp") != 4:
        return lax.all_gather(part, "mp", axis=2, tiled=True)
    index = lax.axis_index("mp")
    core = index % 2
    chip = index // 2
    got = swap(part, mp_pairs(1))
    pair = jnp.where(
        core == 0, jnp.concatenate([part, got], axis=2), jnp.concatenate([got, part], axis=2)
    )
    other = swap(pair, mp_pairs(2))
    return jnp.where(
        chip == 0, jnp.concatenate([pair, other], axis=2), jnp.concatenate([other, pair], axis=2)
    )


def pairs_gather(payload, owners_n):
    if owners_n <= SHIFTS_MAX:
        return jnp.stack(
            [payload] + [pairs_shift(payload, step, owners_n) for step in range(1, owners_n)]
        )
    own = lax.axis_index("pairs")
    every = lax.all_gather(payload, "pairs", axis=0)
    return jnp.roll(every[::-1], own + 1, axis=0)


def pick_rows(onehot, values):
    shape = values.shape
    flat = values.reshape(shape[0], -1)
    picked = jnp.dot(onehot.astype(values.dtype), flat, preferred_element_type=jnp.float32)
    return picked.astype(values.dtype).reshape((onehot.shape[0],) + shape[1:])


def per_device(
    tokens,
    pair_list,
    confidence,
    gain_self,
    gain_query,
    gain_context,
    gain_mlp,
    self_qkv,
    self_out,
    cross_query,
    cross_kv,
    cross_out,
    mlp_up,
    mlp_down,
):
    quarter = tokens.shape[1]
    img_dev = tokens.shape[0] // TOKS
    pair_dev = pair_list.shape[0]
    views_n = 2 * pair_dev
    owners_n = lax.axis_size("pairs")
    own = lax.axis_index("pairs")

    payload = jnp.concatenate(
        [
            tokens.astype(jnp.float32).reshape(-1),
            pair_list.astype(jnp.float32).reshape(-1),
            confidence.reshape(-1),
        ]
    )
    table = pairs_gather(payload, owners_n)
    cut_tok = img_dev * TOKS * quarter
    cut_ids = cut_tok + views_n
    all_tok = table[:, :cut_tok].astype(jnp.bfloat16).reshape(owners_n * img_dev, TOKS * quarter)
    all_ids = table[:, cut_tok:cut_ids].astype(jnp.int32)
    all_conf = table[:, cut_ids:].reshape(owners_n * views_n, TOKS)
    partner_ids = all_ids.reshape(owners_n, pair_dev, 2)[:, :, ::-1].reshape(-1)
    all_ids = all_ids.reshape(-1)

    mine = (all_ids // img_dev == own).astype(jnp.int32)
    rank = jnp.cumsum(mine) - 1
    choose = (mine[None, :] == 1) & (rank[None, :] == jnp.arange(views_n)[:, None])
    image = jnp.sum(jnp.where(choose, all_ids[None, :], 0), axis=1)
    other = jnp.sum(jnp.where(choose, partner_ids[None, :], 0), axis=1)
    conf = jnp.dot(choose.astype(jnp.float32), all_conf, precision=lax.Precision.HIGHEST)
    local = image % img_dev
    at = ((own - other // img_dev) % owners_n) * img_dev + other % img_dev
    far = (at[:, None] == jnp.arange(owners_n * img_dev)[None, :]).astype(jnp.bfloat16)
    context_q = pick_rows(far, all_tok).reshape(views_n, TOKS, quarter)

    own_tok = mp_gather_cols(tokens.reshape(img_dev, TOKS, quarter))
    width = own_tok.shape[2]
    img_rows = img_dev * TOKS
    begin = own_tok.astype(jnp.float32).reshape(img_rows, width)
    normed = lax.optimization_barrier(layer_norm(begin, gain_self))
    qkv = jnp.einsum("rd,kdc->krc", normed, self_qkv, preferred_element_type=jnp.float32).astype(
        jnp.bfloat16
    )
    term = jnp.dot(
        attend(qkv[0], qkv[1], qkv[2], img_dev), self_out, preferred_element_type=jnp.float32
    )
    resid_img = begin + mp_allreduce(term.astype(jnp.bfloat16))
    normed = lax.optimization_barrier(layer_norm(resid_img, gain_query))
    query_img = jnp.dot(normed, cross_query, preferred_element_type=jnp.float32).astype(
        jnp.bfloat16
    )

    rows_n = views_n * TOKS
    context = lax.optimization_barrier(
        layer_norm(mp_gather_steps(context_q).astype(jnp.float32), gain_context)
    ).reshape(rows_n, width)
    keyval = jnp.einsum(
        "rd,kdc->krc", context, cross_kv, preferred_element_type=jnp.float32
    ).astype(jnp.bfloat16)
    near = (local[:, None] == jnp.arange(img_dev)[None, :]).astype(jnp.bfloat16)
    query = pick_rows(near, query_img.reshape(img_dev, TOKS, -1)).reshape(rows_n, -1)
    resid = jnp.take(resid_img.reshape(img_dev, TOKS, width), local, axis=0).reshape(
        rows_n, width
    )
    term = jnp.dot(
        attend(query, keyval[0], keyval[1], views_n), cross_out, preferred_element_type=jnp.float32
    )
    resid = resid + mp_allreduce(term.astype(jnp.bfloat16))
    normed = lax.optimization_barrier(layer_norm(resid, gain_mlp))
    hidden = jax.nn.gelu(
        lax.optimization_barrier(jnp.dot(normed, mlp_up, preferred_element_type=jnp.float32)),
        approximate=False,
    )
    hidden = lax.optimization_barrier(hidden.astype(jnp.bfloat16))
    term = jnp.dot(hidden, mlp_down, preferred_element_type=jnp.float32)
    offset = lax.axis_index("mp") * quarter
    final = lax.dynamic_slice_in_dim(resid, offset, quarter, 1) + mp_reduce_cols(
        term.astype(jnp.bfloat16)
    )
    part = (final.reshape(views_n, TOKS, quarter) * conf[:, :, None]).astype(jnp.bfloat16)
    weight = conf.astype(jnp.bfloat16)
    owner_match = near.astype(jnp.float32).T
    partf = part.astype(jnp.float32)
    weightf = weight.astype(jnp.float32)
    rows = []
    for i in range(img_dev):
        numer = jnp.sum(owner_match[i][:, None, None] * partf, axis=0)
        denom = jnp.sum(owner_match[i][:, None] * weightf, axis=0)
        rows.append(numer / jnp.maximum(denom, 1.0)[:, None])
    return jnp.concatenate(rows, axis=0).astype(jnp.bfloat16)


def solution(mesh):
    return jax.shard_map(
        per_device,
        mesh=mesh,
        in_specs=(
            P(("groups", "pairs"), "mp"),
            P(("groups", "pairs"), None),
            P(("groups", "pairs"), None),
            P(),
            P(),
            P(),
            P(),
            P(None, None, "mp"),
            P("mp", None),
            P(None, "mp"),
            P(None, None, "mp"),
            P("mp", None),
            P(None, "mp"),
            P("mp", None),
        ),
        out_specs=P(("groups", "pairs"), "mp"),
        check_vma=False,
    )
```

```python
import jax
import jax.numpy as jnp
from jax import lax
from jax.sharding import PartitionSpec as P

HEAD = 64
TOKS = 32


EPSILON = 1e-06


def layer_norm(values, gain):
    center = values - jnp.mean(values, axis=-1, keepdims=True)
    spread = jnp.mean(center * center, axis=-1, keepdims=True)
    return (center * lax.rsqrt(spread + EPSILON) * gain).astype(jnp.bfloat16)


def attend(query, keys, values, views_n):
    rows_n, width = query.shape
    heads_n = width // HEAD
    qh = query.reshape(views_n, TOKS, heads_n, HEAD)
    kh = keys.reshape(views_n, TOKS, heads_n, HEAD)
    vh = values.reshape(views_n, TOKS, heads_n, HEAD)
    scores = jnp.einsum("vqhc,vkhc->vhqk", qh, kh, preferred_element_type=jnp.float32) * HEAD ** (
        -0.5
    )
    probs = jax.nn.softmax(scores, axis=-1).astype(jnp.bfloat16)
    mixed = jnp.einsum("vhqk,vkhc->vqhc", probs, vh, preferred_element_type=jnp.float32)
    return mixed.astype(jnp.bfloat16).reshape(rows_n, width)


SHIFTS_MAX = 8


def pairs_shift(values, step, owners_n):
    return lax.ppermute(values, "pairs", [(i, (i + step) % owners_n) for i in range(owners_n)])


def swap(values, pairs):
    return lax.ppermute(values, "mp", pairs)


def mp_pairs(bit):
    n = 4
    return [(i, i ^ bit) for i in range(n)]


def mp_allreduce(term):
    if lax.axis_size("mp") != 4:
        return lax.psum(term.astype(jnp.float32), "mp")
    core = lax.axis_index("mp") % 2
    rows_n = term.shape[0]
    halves = term.reshape(2, rows_n // 2, term.shape[1])
    keep = jnp.where(core == 0, halves[0], halves[1])
    send = jnp.where(core == 0, halves[1], halves[0])
    got = swap(send, mp_pairs(1))
    chip_sum = (keep.astype(jnp.float32) + got.astype(jnp.float32)).astype(jnp.bfloat16)
    other = swap(chip_sum, mp_pairs(2))
    total = chip_sum.astype(jnp.float32) + other.astype(jnp.float32)
    rest = swap(total, mp_pairs(1))
    first = jnp.where(core == 0, total, rest)
    second = jnp.where(core == 0, rest, total)
    return jnp.concatenate([first, second], axis=0)


def mp_reduce_cols(term):
    if lax.axis_size("mp") != 4:
        full = lax.psum(term.astype(jnp.float32), "mp")
        quarter = term.shape[1] // lax.axis_size("mp")
        return lax.dynamic_slice_in_dim(full, lax.axis_index("mp") * quarter, quarter, 1)
    index = lax.axis_index("mp")
    rows_n, width = term.shape
    parts = term.reshape(rows_n, 4, width // 4)
    total = jnp.take(parts, index, axis=1).astype(jnp.float32)
    for bit in (1, 2, 3):
        total = total + swap(jnp.take(parts, index ^ bit, axis=1), mp_pairs(bit)).astype(jnp.float32)
    return total


def mp_gather_cols(part):
    if lax.axis_size("mp") != 4:
        return lax.all_gather(part, "mp", axis=2, tiled=True)
    index = lax.axis_index("mp")
    moved = [part] + [swap(part, mp_pairs(bit)) for bit in (1, 2, 3)]
    placed = []
    for q in range(4):
        rel = index ^ q
        piece = jnp.where(rel == 0, moved[0], moved[1])
        piece = jnp.where(rel == 2, moved[2], piece)
        placed.append(jnp.where(rel == 3, moved[3], piece))
    return jnp.concatenate(placed, axis=2)


def mp_gather_steps(part):
    if lax.axis_size("mp") != 4:
        return lax.all_gather(part, "mp", axis=2, tiled=True)
    index = lax.axis_index("mp")
    core = index % 2
    chip = index // 2
    got = swap(part, mp_pairs(1))
    pair = jnp.where(
        core == 0, jnp.concatenate([part, got], axis=2), jnp.concatenate([got, part], axis=2)
    )
    other = swap(pair, mp_pairs(2))
    return jnp.where(
        chip == 0, jnp.concatenate([pair, other], axis=2), jnp.concatenate([other, pair], axis=2)
    )


def pairs_gather(payload, owners_n):
    if owners_n <= SHIFTS_MAX:
        return jnp.stack(
            [payload] + [pairs_shift(payload, step, owners_n) for step in range(1, owners_n)]
        )
    own = lax.axis_index("pairs")
    every = lax.all_gather(payload, "pairs", axis=0)
    return jnp.roll(every[::-1], own + 1, axis=0)


def pick_rows(onehot, values):
    shape = values.shape
    flat = values.reshape(shape[0], -1)
    picked = jnp.dot(onehot.astype(values.dtype), flat, preferred_element_type=jnp.float32)
    return picked.astype(values.dtype).reshape((onehot.shape[0],) + shape[1:])


def per_device(
    tokens,
    pair_list,
    confidence,
    gain_self,
    gain_query,
    gain_context,
    gain_mlp,
    self_qkv,
    self_out,
    cross_query,
    cross_kv,
    cross_out,
    mlp_up,
    mlp_down,
):
    quarter = tokens.shape[1]
    img_dev = tokens.shape[0] // TOKS
    pair_dev = pair_list.shape[0]
    views_n = 2 * pair_dev
    owners_n = lax.axis_size("pairs")
    own = lax.axis_index("pairs")

    high = lax.optimization_barrier(confidence.astype(jnp.bfloat16))
    rest = confidence - high.astype(jnp.float32)
    mid = lax.optimization_barrier(rest.astype(jnp.bfloat16))
    low = (rest - mid.astype(jnp.float32)).astype(jnp.bfloat16)
    conf_w = confidence.shape[1]
    tok_rows = img_dev * TOKS
    extra_n = -(-(3 * pair_dev + 1) // 8) * 8
    extra = jnp.concatenate(
        [
            jnp.pad(jnp.concatenate([high, mid, low]), ((0, 0), (0, quarter - conf_w))),
            jnp.pad(pair_list.reshape(1, views_n).astype(jnp.bfloat16), ((0, 0), (0, quarter - views_n))),
            jnp.zeros((extra_n - 3 * pair_dev - 1, quarter), jnp.bfloat16),
        ]
    )
    table = pairs_gather(jnp.concatenate([tokens, extra]), owners_n)
    all_tok = table[:, :tok_rows].reshape(owners_n * img_dev, TOKS * quarter)
    pieces = table[:, tok_rows : tok_rows + 3 * pair_dev, :conf_w].astype(jnp.float32)
    pieces = pieces.reshape(owners_n, 3, pair_dev, conf_w)
    all_conf = (pieces[:, 0] + pieces[:, 1] + pieces[:, 2]).reshape(owners_n * views_n, TOKS)
    all_ids = table[:, tok_rows + 3 * pair_dev, :views_n].astype(jnp.int32)
    partner_ids = all_ids.reshape(owners_n, pair_dev, 2)[:, :, ::-1].reshape(-1)
    all_ids = all_ids.reshape(-1)

    mine = (all_ids // img_dev == own).astype(jnp.int32)
    rank = jnp.cumsum(mine) - 1
    choose = (mine[None, :] == 1) & (rank[None, :] == jnp.arange(views_n)[:, None])
    image = jnp.sum(jnp.where(choose, all_ids[None, :], 0), axis=1)
    other = jnp.sum(jnp.where(choose, partner_ids[None, :], 0), axis=1)
    conf = jnp.dot(choose.astype(jnp.float32), all_conf, precision=lax.Precision.HIGHEST)
    local = image % img_dev
    at = ((own - other // img_dev) % owners_n) * img_dev + other % img_dev
    far = (at[:, None] == jnp.arange(owners_n * img_dev)[None, :]).astype(jnp.bfloat16)
    context_q = pick_rows(far, all_tok).reshape(views_n, TOKS, quarter)

    own_tok = mp_gather_cols(tokens.reshape(img_dev, TOKS, quarter))
    width = own_tok.shape[2]
    img_rows = img_dev * TOKS
    begin = own_tok.astype(jnp.float32).reshape(img_rows, width)
    normed = lax.optimization_barrier(layer_norm(begin, gain_self))
    qkv = jnp.einsum("rd,kdc->krc", normed, self_qkv, preferred_element_type=jnp.float32).astype(
        jnp.bfloat16
    )
    term = jnp.dot(
        attend(qkv[0], qkv[1], qkv[2], img_dev), self_out, preferred_element_type=jnp.float32
    )
    resid_img = begin + mp_allreduce(term.astype(jnp.bfloat16))
    normed = lax.optimization_barrier(layer_norm(resid_img, gain_query))
    query_img = jnp.dot(normed, cross_query, preferred_element_type=jnp.float32).astype(
        jnp.bfloat16
    )

    rows_n = views_n * TOKS
    context = lax.optimization_barrier(
        layer_norm(mp_gather_steps(context_q).astype(jnp.float32), gain_context)
    ).reshape(rows_n, width)
    keyval = jnp.einsum(
        "rd,kdc->krc", context, cross_kv, preferred_element_type=jnp.float32
    ).astype(jnp.bfloat16)
    near = (local[:, None] == jnp.arange(img_dev)[None, :]).astype(jnp.bfloat16)
    query = pick_rows(near, query_img.reshape(img_dev, TOKS, -1)).reshape(rows_n, -1)
    resid = jnp.take(resid_img.reshape(img_dev, TOKS, width), local, axis=0).reshape(
        rows_n, width
    )
    term = jnp.dot(
        attend(query, keyval[0], keyval[1], views_n), cross_out, preferred_element_type=jnp.float32
    )
    resid = resid + mp_allreduce(term.astype(jnp.bfloat16))
    normed = lax.optimization_barrier(layer_norm(resid, gain_mlp))
    hidden = jax.nn.gelu(
        lax.optimization_barrier(jnp.dot(normed, mlp_up, preferred_element_type=jnp.float32)),
        approximate=False,
    )
    hidden = lax.optimization_barrier(hidden.astype(jnp.bfloat16))
    term = jnp.dot(hidden, mlp_down, preferred_element_type=jnp.float32)
    offset = lax.axis_index("mp") * quarter
    final = lax.dynamic_slice_in_dim(resid, offset, quarter, 1) + mp_reduce_cols(
        term.astype(jnp.bfloat16)
    )
    part = (final.reshape(views_n, TOKS, quarter) * conf[:, :, None]).astype(jnp.bfloat16)
    weight = conf.astype(jnp.bfloat16)
    owner_match = near.astype(jnp.float32).T
    partf = part.astype(jnp.float32)
    weightf = weight.astype(jnp.float32)
    rows = []
    for i in range(img_dev):
        numer = jnp.sum(owner_match[i][:, None, None] * partf, axis=0)
        denom = jnp.sum(owner_match[i][:, None] * weightf, axis=0)
        rows.append(numer / jnp.maximum(denom, 1.0)[:, None])
    return jnp.concatenate(rows, axis=0).astype(jnp.bfloat16)


def solution(mesh):
    return jax.shard_map(
        per_device,
        mesh=mesh,
        in_specs=(
            P(("groups", "pairs"), "mp"),
            P(("groups", "pairs"), None),
            P(("groups", "pairs"), None),
            P(),
            P(),
            P(),
            P(),
            P(None, None, "mp"),
            P("mp", None),
            P(None, "mp"),
            P(None, None, "mp"),
            P("mp", None),
            P(None, "mp"),
            P("mp", None),
        ),
        out_specs=P(("groups", "pairs"), "mp"),
        check_vma=False,
    )
```

```python
import jax
import jax.numpy as jnp
from jax import lax
from jax.sharding import PartitionSpec as P

HEAD = 64
TOKS = 32


EPSILON = 1e-06


def layer_norm(values, gain):
    center = values - jnp.mean(values, axis=-1, keepdims=True)
    spread = jnp.mean(center * center, axis=-1, keepdims=True)
    return (center * lax.rsqrt(spread + EPSILON) * gain).astype(jnp.bfloat16)


def attend(query, keys, values, views_n):
    rows_n, width = query.shape
    heads_n = width // HEAD
    qh = query.reshape(views_n, TOKS, heads_n, HEAD)
    kh = keys.reshape(views_n, TOKS, heads_n, HEAD)
    vh = values.reshape(views_n, TOKS, heads_n, HEAD)
    scores = jnp.einsum("vqhc,vkhc->vhqk", qh, kh, preferred_element_type=jnp.float32) * HEAD ** (
        -0.5
    )
    probs = jax.nn.softmax(scores, axis=-1).astype(jnp.bfloat16)
    mixed = jnp.einsum("vhqk,vkhc->vqhc", probs, vh, preferred_element_type=jnp.float32)
    return mixed.astype(jnp.bfloat16).reshape(rows_n, width)


SHIFTS_MAX = 8


def pairs_shift(values, step, owners_n):
    return lax.ppermute(values, "pairs", [(i, (i + step) % owners_n) for i in range(owners_n)])


def swap(values, pairs):
    return lax.ppermute(values, "mp", pairs)


def mp_pairs(bit):
    n = 4
    return [(i, i ^ bit) for i in range(n)]


def mp_allreduce(term):
    if lax.axis_size("mp") != 4:
        return lax.psum(term.astype(jnp.float32), "mp")
    core = lax.axis_index("mp") % 2
    rows_n = term.shape[0]
    halves = term.reshape(2, rows_n // 2, term.shape[1])
    keep = jnp.where(core == 0, halves[0], halves[1])
    send = jnp.where(core == 0, halves[1], halves[0])
    got = swap(send, mp_pairs(1))
    chip_sum = (keep.astype(jnp.float32) + got.astype(jnp.float32)).astype(jnp.bfloat16)
    other = swap(chip_sum, mp_pairs(2))
    total = chip_sum.astype(jnp.float32) + other.astype(jnp.float32)
    rest = swap(total, mp_pairs(1))
    first = jnp.where(core == 0, total, rest)
    second = jnp.where(core == 0, rest, total)
    return jnp.concatenate([first, second], axis=0)


def mp_reduce_cols(term):
    if lax.axis_size("mp") != 4:
        full = lax.psum(term.astype(jnp.float32), "mp")
        quarter = term.shape[1] // lax.axis_size("mp")
        return lax.dynamic_slice_in_dim(full, lax.axis_index("mp") * quarter, quarter, 1)
    index = lax.axis_index("mp")
    rows_n, width = term.shape
    parts = term.reshape(rows_n, 4, width // 4)
    total = jnp.take(parts, index, axis=1).astype(jnp.float32)
    for bit in (1, 2, 3):
        total = total + swap(jnp.take(parts, index ^ bit, axis=1), mp_pairs(bit)).astype(jnp.float32)
    return total


def mp_gather_cols(part):
    if lax.axis_size("mp") != 4:
        return lax.all_gather(part, "mp", axis=2, tiled=True)
    index = lax.axis_index("mp")
    moved = [part] + [swap(part, mp_pairs(bit)) for bit in (1, 2, 3)]
    placed = []
    for q in range(4):
        rel = index ^ q
        piece = jnp.where(rel == 0, moved[0], moved[1])
        piece = jnp.where(rel == 2, moved[2], piece)
        placed.append(jnp.where(rel == 3, moved[3], piece))
    return jnp.concatenate(placed, axis=2)


def mp_gather_steps(part):
    if lax.axis_size("mp") != 4:
        return lax.all_gather(part, "mp", axis=2, tiled=True)
    index = lax.axis_index("mp")
    core = index % 2
    chip = index // 2
    got = swap(part, mp_pairs(1))
    pair = jnp.where(
        core == 0, jnp.concatenate([part, got], axis=2), jnp.concatenate([got, part], axis=2)
    )
    other = swap(pair, mp_pairs(2))
    return jnp.where(
        chip == 0, jnp.concatenate([pair, other], axis=2), jnp.concatenate([other, pair], axis=2)
    )


def pairs_gather(payload, owners_n):
    if owners_n <= SHIFTS_MAX:
        moved = {step: pairs_shift(payload, step, owners_n) for step in range(owners_n - 1, 0, -1)}
        return jnp.stack([payload] + [moved[step] for step in range(1, owners_n)])
    own = lax.axis_index("pairs")
    every = lax.all_gather(payload, "pairs", axis=0)
    return jnp.roll(every[::-1], own + 1, axis=0)


def pick_rows(onehot, values):
    shape = values.shape
    flat = values.reshape(shape[0], -1)
    picked = jnp.dot(onehot.astype(values.dtype), flat, preferred_element_type=jnp.float32)
    return picked.astype(values.dtype).reshape((onehot.shape[0],) + shape[1:])


def per_device(
    tokens,
    pair_list,
    confidence,
    gain_self,
    gain_query,
    gain_context,
    gain_mlp,
    self_qkv,
    self_out,
    cross_query,
    cross_kv,
    cross_out,
    mlp_up,
    mlp_down,
):
    quarter = tokens.shape[1]
    img_dev = tokens.shape[0] // TOKS
    pair_dev = pair_list.shape[0]
    views_n = 2 * pair_dev
    owners_n = lax.axis_size("pairs")
    own = lax.axis_index("pairs")

    payload = jnp.concatenate(
        [
            tokens.astype(jnp.float32).reshape(-1),
            pair_list.astype(jnp.float32).reshape(-1),
            confidence.reshape(-1),
        ]
    )
    table = pairs_gather(payload, owners_n)
    cut_tok = img_dev * TOKS * quarter
    cut_ids = cut_tok + views_n
    all_tok = table[:, :cut_tok].astype(jnp.bfloat16).reshape(owners_n * img_dev, TOKS * quarter)
    all_ids = table[:, cut_tok:cut_ids].astype(jnp.int32)
    all_conf = table[:, cut_ids:].reshape(owners_n * views_n, TOKS)
    partner_ids = all_ids.reshape(owners_n, pair_dev, 2)[:, :, ::-1].reshape(-1)
    all_ids = all_ids.reshape(-1)

    mine = (all_ids // img_dev == own).astype(jnp.int32)
    rank = jnp.cumsum(mine) - 1
    choose = (mine[None, :] == 1) & (rank[None, :] == jnp.arange(views_n)[:, None])
    image = jnp.sum(jnp.where(choose, all_ids[None, :], 0), axis=1)
    other = jnp.sum(jnp.where(choose, partner_ids[None, :], 0), axis=1)
    conf = jnp.dot(choose.astype(jnp.float32), all_conf, precision=lax.Precision.HIGHEST)
    local = image % img_dev
    at = ((own - other // img_dev) % owners_n) * img_dev + other % img_dev
    far = (at[:, None] == jnp.arange(owners_n * img_dev)[None, :]).astype(jnp.bfloat16)
    context_q = pick_rows(far, all_tok).reshape(views_n, TOKS, quarter)

    own_tok = mp_gather_cols(tokens.reshape(img_dev, TOKS, quarter))
    width = own_tok.shape[2]
    img_rows = img_dev * TOKS
    begin = own_tok.astype(jnp.float32).reshape(img_rows, width)
    normed = lax.optimization_barrier(layer_norm(begin, gain_self))
    qkv = jnp.einsum("rd,kdc->krc", normed, self_qkv, preferred_element_type=jnp.float32).astype(
        jnp.bfloat16
    )
    term = jnp.dot(
        attend(qkv[0], qkv[1], qkv[2], img_dev), self_out, preferred_element_type=jnp.float32
    )
    resid_img = begin + mp_allreduce(term.astype(jnp.bfloat16))
    normed = lax.optimization_barrier(layer_norm(resid_img, gain_query))
    query_img = jnp.dot(normed, cross_query, preferred_element_type=jnp.float32).astype(
        jnp.bfloat16
    )

    rows_n = views_n * TOKS
    context = lax.optimization_barrier(
        layer_norm(mp_gather_steps(context_q).astype(jnp.float32), gain_context)
    ).reshape(rows_n, width)
    keyval = jnp.einsum(
        "rd,kdc->krc", context, cross_kv, preferred_element_type=jnp.float32
    ).astype(jnp.bfloat16)
    near = (local[:, None] == jnp.arange(img_dev)[None, :]).astype(jnp.bfloat16)
    query = pick_rows(near, query_img.reshape(img_dev, TOKS, -1)).reshape(rows_n, -1)
    resid = jnp.take(resid_img.reshape(img_dev, TOKS, width), local, axis=0).reshape(
        rows_n, width
    )
    term = jnp.dot(
        attend(query, keyval[0], keyval[1], views_n), cross_out, preferred_element_type=jnp.float32
    )
    resid = resid + mp_allreduce(term.astype(jnp.bfloat16))
    normed = lax.optimization_barrier(layer_norm(resid, gain_mlp))
    hidden = jax.nn.gelu(
        lax.optimization_barrier(jnp.dot(normed, mlp_up, preferred_element_type=jnp.float32)),
        approximate=False,
    )
    hidden = lax.optimization_barrier(hidden.astype(jnp.bfloat16))
    term = jnp.dot(hidden, mlp_down, preferred_element_type=jnp.float32)
    offset = lax.axis_index("mp") * quarter
    final = lax.dynamic_slice_in_dim(resid, offset, quarter, 1) + mp_reduce_cols(
        term.astype(jnp.bfloat16)
    )
    part = (final.reshape(views_n, TOKS, quarter) * conf[:, :, None]).astype(jnp.bfloat16)
    weight = conf.astype(jnp.bfloat16)
    owner_match = near.astype(jnp.float32).T
    partf = part.astype(jnp.float32)
    weightf = weight.astype(jnp.float32)
    rows = []
    for i in range(img_dev):
        numer = jnp.sum(owner_match[i][:, None, None] * partf, axis=0)
        denom = jnp.sum(owner_match[i][:, None] * weightf, axis=0)
        rows.append(numer / jnp.maximum(denom, 1.0)[:, None])
    return jnp.concatenate(rows, axis=0).astype(jnp.bfloat16)


def solution(mesh):
    return jax.shard_map(
        per_device,
        mesh=mesh,
        in_specs=(
            P(("groups", "pairs"), "mp"),
            P(("groups", "pairs"), None),
            P(("groups", "pairs"), None),
            P(),
            P(),
            P(),
            P(),
            P(None, None, "mp"),
            P("mp", None),
            P(None, "mp"),
            P(None, None, "mp"),
            P("mp", None),
            P(None, "mp"),
            P("mp", None),
        ),
        out_specs=P(("groups", "pairs"), "mp"),
        check_vma=False,
    )
```

```python
import jax
import jax.numpy as jnp
from jax import lax
from jax.sharding import PartitionSpec as P

HEAD = 64
TOKS = 32


EPSILON = 1e-06


def layer_norm(values, gain):
    center = values - jnp.mean(values, axis=-1, keepdims=True)
    spread = jnp.mean(center * center, axis=-1, keepdims=True)
    return (center * lax.rsqrt(spread + EPSILON) * gain).astype(jnp.bfloat16)


def attend(query, keys, values, views_n):
    rows_n, width = query.shape
    heads_n = width // HEAD
    qh = query.reshape(views_n, TOKS, heads_n, HEAD)
    kh = keys.reshape(views_n, TOKS, heads_n, HEAD)
    vh = values.reshape(views_n, TOKS, heads_n, HEAD)
    scores = jnp.einsum("vqhc,vkhc->vhqk", qh, kh, preferred_element_type=jnp.float32) * HEAD ** (
        -0.5
    )
    probs = jax.nn.softmax(scores, axis=-1).astype(jnp.bfloat16)
    mixed = jnp.einsum("vhqk,vkhc->vqhc", probs, vh, preferred_element_type=jnp.float32)
    return mixed.astype(jnp.bfloat16).reshape(rows_n, width)


SHIFTS_MAX = 8


def pairs_shift(values, step, owners_n):
    return lax.ppermute(values, "pairs", [(i, (i + step) % owners_n) for i in range(owners_n)])


def swap(values, pairs):
    return lax.ppermute(values, "mp", pairs)


def mp_pairs(bit):
    n = 4
    return [(i, i ^ bit) for i in range(n)]


def mp_allreduce(term):
    if lax.axis_size("mp") != 4:
        return lax.psum(term.astype(jnp.float32), "mp")
    core = lax.axis_index("mp") % 2
    rows_n = term.shape[0]
    halves = term.reshape(2, rows_n // 2, term.shape[1])
    keep = jnp.where(core == 0, halves[0], halves[1])
    send = jnp.where(core == 0, halves[1], halves[0])
    got = swap(send, mp_pairs(1))
    chip_sum = (keep.astype(jnp.float32) + got.astype(jnp.float32)).astype(jnp.bfloat16)
    other = swap(chip_sum, mp_pairs(2))
    total = chip_sum.astype(jnp.float32) + other.astype(jnp.float32)
    rest = swap(total, mp_pairs(1))
    first = jnp.where(core == 0, total, rest)
    second = jnp.where(core == 0, rest, total)
    return jnp.concatenate([first, second], axis=0)


def mp_reduce_cols(term):
    if lax.axis_size("mp") != 4:
        full = lax.psum(term.astype(jnp.float32), "mp")
        quarter = term.shape[1] // lax.axis_size("mp")
        return lax.dynamic_slice_in_dim(full, lax.axis_index("mp") * quarter, quarter, 1)
    index = lax.axis_index("mp")
    rows_n, width = term.shape
    parts = term.reshape(rows_n, 4, width // 4)
    total = jnp.take(parts, index, axis=1).astype(jnp.float32)
    for bit in (1, 2, 3):
        total = total + swap(jnp.take(parts, index ^ bit, axis=1), mp_pairs(bit)).astype(jnp.float32)
    return total


def mp_gather_cols(part):
    if lax.axis_size("mp") != 4:
        return lax.all_gather(part, "mp", axis=2, tiled=True)
    index = lax.axis_index("mp")
    moved = [part] + [swap(part, mp_pairs(bit)) for bit in (1, 2, 3)]
    placed = []
    for q in range(4):
        rel = index ^ q
        piece = jnp.where(rel == 0, moved[0], moved[1])
        piece = jnp.where(rel == 2, moved[2], piece)
        placed.append(jnp.where(rel == 3, moved[3], piece))
    return jnp.concatenate(placed, axis=2)


def mp_gather_steps(part):
    if lax.axis_size("mp") != 4:
        return lax.all_gather(part, "mp", axis=2, tiled=True)
    index = lax.axis_index("mp")
    core = index % 2
    chip = index // 2
    got = swap(part, mp_pairs(1))
    pair = jnp.where(
        core == 0, jnp.concatenate([part, got], axis=2), jnp.concatenate([got, part], axis=2)
    )
    other = swap(pair, mp_pairs(2))
    return jnp.where(
        chip == 0, jnp.concatenate([pair, other], axis=2), jnp.concatenate([other, pair], axis=2)
    )


def pairs_gather(payload, owners_n):
    if owners_n <= SHIFTS_MAX:
        return jnp.stack(
            [payload] + [pairs_shift(payload, step, owners_n) for step in range(1, owners_n)]
        )
    own = lax.axis_index("pairs")
    every = lax.all_gather(payload, "pairs", axis=0)
    return jnp.roll(every[::-1], own + 1, axis=0)


def pick_rows(onehot, values):
    shape = values.shape
    flat = values.reshape(shape[0], -1)
    picked = jnp.dot(onehot.astype(values.dtype), flat, preferred_element_type=jnp.float32)
    return picked.astype(values.dtype).reshape((onehot.shape[0],) + shape[1:])


def per_device(
    tokens,
    pair_list,
    confidence,
    gain_self,
    gain_query,
    gain_context,
    gain_mlp,
    self_qkv,
    self_out,
    cross_query,
    cross_kv,
    cross_out,
    mlp_up,
    mlp_down,
):
    quarter = tokens.shape[1]
    img_dev = tokens.shape[0] // TOKS
    pair_dev = pair_list.shape[0]
    views_n = 2 * pair_dev
    owners_n = lax.axis_size("pairs")
    own = lax.axis_index("pairs")

    payload = jnp.concatenate(
        [
            tokens.astype(jnp.float32).reshape(-1),
            pair_list.astype(jnp.float32).reshape(-1),
            confidence.reshape(-1),
        ]
    )
    table = pairs_gather(payload, owners_n)
    cut_tok = img_dev * TOKS * quarter
    cut_ids = cut_tok + views_n
    all_tok = table[:, :cut_tok].astype(jnp.bfloat16).reshape(owners_n * img_dev, TOKS * quarter)
    all_ids = table[:, cut_tok:cut_ids].astype(jnp.int32)
    all_conf = table[:, cut_ids:].reshape(owners_n * views_n, TOKS)
    partner_ids = all_ids.reshape(owners_n, pair_dev, 2)[:, :, ::-1].reshape(-1)
    all_ids = all_ids.reshape(-1)

    mine = (all_ids // img_dev == own).astype(jnp.int32)
    rank = jnp.cumsum(mine) - 1
    choose = (mine[None, :] == 1) & (rank[None, :] == jnp.arange(views_n)[:, None])
    image = jnp.sum(jnp.where(choose, all_ids[None, :], 0), axis=1)
    other = jnp.sum(jnp.where(choose, partner_ids[None, :], 0), axis=1)
    conf = jnp.dot(choose.astype(jnp.float32), all_conf, precision=lax.Precision.HIGHEST)
    local = image % img_dev
    at = ((own - other // img_dev) % owners_n) * img_dev + other % img_dev
    far = (at[:, None] == jnp.arange(owners_n * img_dev)[None, :]).astype(jnp.bfloat16)
    context_q = pick_rows(far, all_tok).reshape(views_n, TOKS, quarter)

    own_tok = mp_gather_cols(tokens.reshape(img_dev, TOKS, quarter))
    width = own_tok.shape[2]
    img_rows = img_dev * TOKS
    begin = own_tok.astype(jnp.float32).reshape(img_rows, width)
    normed = lax.optimization_barrier(layer_norm(begin, gain_self))
    qkv = jnp.einsum("rd,kdc->krc", normed, self_qkv, preferred_element_type=jnp.float32).astype(
        jnp.bfloat16
    )
    term = jnp.dot(
        attend(qkv[0], qkv[1], qkv[2], img_dev), self_out, preferred_element_type=jnp.float32
    )
    resid_img = begin + mp_allreduce(term.astype(jnp.bfloat16))
    normed = lax.optimization_barrier(layer_norm(resid_img, gain_query))
    query_img = jnp.dot(normed, cross_query, preferred_element_type=jnp.float32).astype(
        jnp.bfloat16
    )

    rows_n = views_n * TOKS
    context = lax.optimization_barrier(
        layer_norm(mp_gather_steps(context_q).astype(jnp.float32), gain_context)
    ).reshape(rows_n, width)
    keyval = jnp.einsum(
        "rd,kdc->krc", context, cross_kv, preferred_element_type=jnp.float32
    ).astype(jnp.bfloat16)
    near = (local[:, None] == jnp.arange(img_dev)[None, :]).astype(jnp.bfloat16)
    query = pick_rows(near, query_img.reshape(img_dev, TOKS, -1)).reshape(rows_n, -1)
    per_image = resid_img.reshape(img_dev, 1, TOKS, width)
    resid = jnp.broadcast_to(per_image[0], (views_n, TOKS, width))
    for i in range(1, img_dev):
        resid = jnp.where((local == i)[:, None, None], per_image[i], resid)
    resid = resid.reshape(rows_n, width)
    term = jnp.dot(
        attend(query, keyval[0], keyval[1], views_n), cross_out, preferred_element_type=jnp.float32
    )
    resid = resid + mp_allreduce(term.astype(jnp.bfloat16))
    normed = lax.optimization_barrier(layer_norm(resid, gain_mlp))
    hidden = jax.nn.gelu(
        lax.optimization_barrier(jnp.dot(normed, mlp_up, preferred_element_type=jnp.float32)),
        approximate=False,
    )
    hidden = lax.optimization_barrier(hidden.astype(jnp.bfloat16))
    term = jnp.dot(hidden, mlp_down, preferred_element_type=jnp.float32)
    offset = lax.axis_index("mp") * quarter
    final = lax.dynamic_slice_in_dim(resid, offset, quarter, 1) + mp_reduce_cols(
        term.astype(jnp.bfloat16)
    )
    part = (final.reshape(views_n, TOKS, quarter) * conf[:, :, None]).astype(jnp.bfloat16)
    weight = conf.astype(jnp.bfloat16)
    owner_match = near.astype(jnp.float32).T
    partf = part.astype(jnp.float32)
    weightf = weight.astype(jnp.float32)
    rows = []
    for i in range(img_dev):
        numer = jnp.sum(owner_match[i][:, None, None] * partf, axis=0)
        denom = jnp.sum(owner_match[i][:, None] * weightf, axis=0)
        rows.append(numer / jnp.maximum(denom, 1.0)[:, None])
    return jnp.concatenate(rows, axis=0).astype(jnp.bfloat16)


def solution(mesh):
    return jax.shard_map(
        per_device,
        mesh=mesh,
        in_specs=(
            P(("groups", "pairs"), "mp"),
            P(("groups", "pairs"), None),
            P(("groups", "pairs"), None),
            P(),
            P(),
            P(),
            P(),
            P(None, None, "mp"),
            P("mp", None),
            P(None, "mp"),
            P(None, None, "mp"),
            P("mp", None),
            P(None, "mp"),
            P("mp", None),
        ),
        out_specs=P(("groups", "pairs"), "mp"),
        check_vma=False,
    )
```
